32 devices in a mesh: seq: 8 (over y, x, core), clip: 4 (over z).
Axes of the slice: x: 2, y: 2, z: 4, core: 2. Of those that a mesh axis runs over, the one named last changes fastest.
Arguments:
- raw_tokens: bfloat16 [4, 4096, 1024], P('clip', 'seq'), may hold values from -6 to 6
- teacher: bfloat16 [4, 4096, 1024], P('clip', 'seq'), may hold values from -6 to 6
- keep_rows: int32 [4, 1536], P('clip', 'seq'), may hold values from -1 to 511, as said below
- w_qkv: bfloat16 [1024, 1536], replicated, may hold values from -4 to 4
- w_out: bfloat16 [512, 1024], replicated, may hold values from -0.25 to 0.25
- ln_gain: float32 [1024], replicated, may hold values from 0.1 to 1.9
Outputs:
- align_loss: float32 [], replicated
- grad_qkv: float32 [1572864], P(('seq', 'clip'))
- grad_out: float32 [524288], P(('seq', 'clip'))
- grad_gain: float32 [1024], replicated
The draws below stay inside these ranges and needn't reach their ends.
Inputs may be any that keep to these rules, and one draw needn't show every extreme that they name: `keep_rows`: in each clip, block s of 192 entries lists its kept local indices (0 to 511) in ascending order followed by -1; the blocks' counts of kept patches lie between 64 and 192 and sum to 1024, and some block of every clip keeps exactly 192.
All inputs are finite; a program needn't handle non-finite values.
Results may differ from the reference program's by a relative error of at most 0.023.
Values may be sent and summed in bfloat16 or wider, within the bound.
No kernel may reach another device: no remote copies, remote signals or barrier semaphores. Data moves between devices by JAX's collectives and lax.ppermute only.
A program may use at most 128 MiB of HBM per device.

```python
import math
import jax
import jax.numpy as jnp
from jax import lax

D = 1024
HEADS = 8
HEAD_DIM = 64
TOK_DEV = 128
INNER = 512
RAW_DEV = 512
KCAP = 192
LEN = 1024
RAW = 4096
CLIPS = 4


def draw_keep_rows(key, part):
    shards = LEN // TOK_DEV

    def one_clip(clip_key):
        perm_key, delta_key, pick_key, rows_key = jax.random.split(clip_key, 4)
        shuffle = jax.random.permutation(perm_key, shards)
        pair_count = shards // 2
        half_tok = TOK_DEV // 2
        deltas = jax.random.randint(delta_key, (pair_count,), 0, half_tok + 1)
        forced = jax.random.randint(pick_key, (), 0, pair_count)
        deltas = jnp.where(jnp.arange(pair_count) == forced, half_tok, deltas)
        values = jnp.stack([TOK_DEV + deltas, TOK_DEV - deltas], axis=1).reshape(-1).astype(jnp.int32)
        counts = jnp.zeros((shards,), jnp.int32).at[shuffle].set(values)
        row_keys = jax.random.split(rows_key, shards)

        def one_shard(row_key, count):
            picked = jax.random.permutation(row_key, RAW_DEV)[:KCAP]
            slot_idx = jnp.arange(KCAP)
            chosen = jnp.where(slot_idx < count, picked, RAW_DEV)
            chosen = jnp.sort(chosen)
            return jnp.where(chosen == RAW_DEV, -1, chosen)
        return jax.vmap(one_shard)(row_keys, counts).reshape(-1)
    clip_keys = jax.random.split(key, CLIPS)
    return jax.vmap(one_clip)(clip_keys).astype(jnp.int32)


def draw_w_qkv(key, part):
    query_key, pair_key = jax.random.split(key, 2)
    query_part = jax.random.normal(query_key, (D, INNER), jnp.float32) * (3.0 / math.sqrt(D))
    pair_part = jax.random.normal(pair_key, (D, 2 * INNER), jnp.float32) * (1.0 / math.sqrt(D))
    joined = jnp.concatenate([query_part, pair_part], axis=1)
    return jnp.clip(joined, -4.0, 4.0).astype(jnp.bfloat16)


def level_of(key, extent, cuts, smallest, largest):
    level, own = 1.0, jax.random.fold_in(key, 6)
    for axis_at, blocks in cuts:
        draws = jnp.exp(jax.random.uniform(jax.random.fold_in(own, axis_at), (blocks,), jnp.float32, smallest / len(cuts), largest / len(cuts)))
        level = level * jnp.repeat(draws, extent[axis_at] // blocks).reshape([-1 if axis == axis_at else 1 for axis in range(len(extent))])
    return level


def normal_values(stream_key, extent, deviation, most, cuts=(), kind=jnp.bfloat16):
    result = jax.random.normal(stream_key, extent, jnp.float32) * deviation
    if len(cuts) > 0:
        result = level_of(stream_key, extent, cuts, -0.22, 0.18) * result
    return jnp.clip(result, min=-most, max=most).astype(kind)


def setup_inputs(seed: int = 0) -> dict:
    seeds = jax.random.split(jax.random.key(seed), 7)
    raw_tokens = normal_values(seeds[0], (CLIPS, RAW, D), 1.0, 6.0, ((0, 4), (1, 8)))
    teacher = normal_values(seeds[1], (CLIPS, RAW, D), 1.0, 6.0, ((0, 4), (1, 8)))
    keep_rows = draw_keep_rows(jax.random.fold_in(seeds[6], 71), 0)
    w_qkv = draw_w_qkv(jax.random.fold_in(seeds[6], 71), 0)
    w_out = normal_values(seeds[4], (INNER, D), INNER ** -0.5, 0.25)
    ln_gain = jnp.clip(1.0 + 0.18 * jax.random.normal(seeds[5], (D,), jnp.float32), 0.1, 1.9)
    return {"raw_tokens": raw_tokens, "teacher": teacher, "keep_rows": keep_rows, "w_qkv": w_qkv, "w_out": w_out, "ln_gain": ln_gain}


def layer_norm(tokens, ln_gain):
    values = tokens.astype(jnp.float32)
    center = values - lax.optimization_barrier(jnp.mean(values, axis=-1, keepdims=True))
    spread = lax.optimization_barrier(jnp.mean(center * center, axis=-1, keepdims=True))
    normed = center * lax.rsqrt(spread + 1e-05)
    return (normed, (normed * ln_gain).astype(jnp.bfloat16))

def align_terms(student, target):
    target_f = target.astype(jnp.float32)
    inv_y = lax.rsqrt(lax.optimization_barrier(jnp.sum(student * student, axis=-1, keepdims=True)) + 1e-06)
    inv_t = lax.rsqrt(lax.optimization_barrier(jnp.sum(target_f * target_f, axis=-1, keepdims=True)) + 1e-06)
    differ = student * inv_y - target_f * inv_t
    token_loss = lax.optimization_barrier(jnp.sum(differ * differ, axis=-1))
    slopes = 2.0 * differ
    grad_y = inv_y * slopes - student * (inv_y * inv_y * inv_y) * lax.optimization_barrier(jnp.sum(slopes * student, axis=-1, keepdims=True))
    return (token_loss, grad_y)

def compact(rows_all, source):
    row_table = rows_all.reshape(-1, KCAP)
    shards = row_table.shape[0]
    is_kept = row_table >= 0
    counts = lax.optimization_barrier(jnp.sum(is_kept.astype(jnp.int32), axis=1)).astype(jnp.int32)
    starts = (jnp.cumsum(counts) - counts).astype(jnp.int32)
    slot_idx = jnp.arange(KCAP, dtype=jnp.int32)
    target_pos = jnp.where(is_kept, starts[:, None] + slot_idx[None, :], LEN).astype(jnp.int32)
    source_pos = (jnp.arange(shards, dtype=jnp.int32)[:, None] * RAW_DEV + jnp.maximum(row_table, 0)).astype(jnp.int32)
    picked = source[source_pos.reshape(-1)]
    canvas = jnp.zeros((LEN, source.shape[1]), source.dtype)
    return canvas.at[target_pos.reshape(-1)].set(picked, mode='drop')

def reference(raw_tokens, teacher, keep_rows, w_qkv, w_out, ln_gain):

    def one_clip(packed):
        raw_clip, teach_clip, rows_clip = packed
        tokens = compact(rows_clip, raw_clip)
        target = compact(rows_clip, teach_clip)
        normed, hidden = layer_norm(tokens, ln_gain)
        projected = jnp.dot(hidden, w_qkv, preferred_element_type=jnp.float32)
        queries = projected[:, :INNER].astype(jnp.bfloat16).reshape(LEN, HEADS, HEAD_DIM).transpose(1, 0, 2)
        pair_part = projected[:, INNER:].astype(jnp.bfloat16).reshape(LEN, HEADS, 2, HEAD_DIM)
        key_rows = pair_part[:, :, 0].transpose(1, 0, 2)
        values = pair_part[:, :, 1].transpose(1, 0, 2)

        def forward_head(head_item):
            q_head, k_head, v_head = head_item
            scores = jnp.dot(q_head, k_head.T, preferred_element_type=jnp.float32) * 0.125
            row_max = lax.optimization_barrier(jnp.max(scores, axis=1, keepdims=True))
            weights = jnp.exp(scores - row_max)
            row_sum = lax.optimization_barrier(jnp.sum(weights, axis=1, keepdims=True))
            blended = jnp.dot(weights.astype(jnp.bfloat16), v_head, preferred_element_type=jnp.float32) / row_sum
            return (blended, (row_max + jnp.log(row_sum))[:, 0])
        blended, log_total = lax.map(forward_head, (queries, key_rows, values))
        attended = blended.transpose(1, 0, 2).reshape(LEN, INNER).astype(jnp.bfloat16)
        student = tokens.astype(jnp.float32) + jnp.dot(attended, w_out, preferred_element_type=jnp.float32)
        token_loss, grad_y = align_terms(student, target)
        grad_b = grad_y.astype(jnp.bfloat16)
        grad_wout = jnp.dot(attended.T, grad_b, preferred_element_type=jnp.float32)
        grad_heads = jnp.dot(grad_b, w_out.T, preferred_element_type=jnp.float32).astype(jnp.bfloat16)
        grad_heads = grad_heads.reshape(LEN, HEADS, HEAD_DIM).transpose(1, 0, 2)
        att_heads = attended.reshape(LEN, HEADS, HEAD_DIM).transpose(1, 0, 2)
        row_dot = lax.optimization_barrier(jnp.sum(grad_heads.astype(jnp.float32) * att_heads.astype(jnp.float32), axis=2))

        def backward_head(head_item):
            q_head, k_head, v_head, do_head, lse_head, dot_head = head_item
            scores = jnp.dot(q_head, k_head.T, preferred_element_type=jnp.float32) * 0.125
            prob_full = jnp.exp(scores - lse_head[:, None])
            d_value = jnp.dot(prob_full.astype(jnp.bfloat16).T, do_head, preferred_element_type=jnp.float32)
            d_prob = jnp.dot(do_head, v_head.T, preferred_element_type=jnp.float32)
            d_score = (prob_full * (d_prob - dot_head[:, None])).astype(jnp.bfloat16)
            d_query = 0.125 * jnp.dot(d_score, k_head, preferred_element_type=jnp.float32)
            d_key = 0.125 * jnp.dot(d_score.T, q_head, preferred_element_type=jnp.float32)
            return (d_query, d_key, d_value)
        d_query, d_key, d_value = lax.map(backward_head, (queries, key_rows, values, grad_heads, log_total, row_dot))
        d_pairs = jnp.stack([d_key.transpose(1, 0, 2), d_value.transpose(1, 0, 2)], axis=2).reshape(LEN, 2 * INNER)
        d_proj = jnp.concatenate([d_query.transpose(1, 0, 2).reshape(LEN, INNER), d_pairs], axis=1).astype(jnp.bfloat16)
        grad_wqkv = jnp.dot(hidden.T, d_proj, preferred_element_type=jnp.float32)
        d_hidden = jnp.dot(d_proj, w_qkv.T, preferred_element_type=jnp.float32)
        grad_ln = lax.optimization_barrier(jnp.sum(d_hidden * normed, axis=0))
        return (jnp.sum(token_loss), grad_wqkv, grad_wout, grad_ln)
    loss_sums, grads_qkv, grads_out, grads_gain = lax.map(one_clip, (raw_tokens, teacher, keep_rows))
    align_loss = jnp.sum(loss_sums) / (CLIPS * LEN)
    return (align_loss, lax.optimization_barrier(jnp.sum(grads_qkv, axis=0)).reshape(-1), lax.optimization_barrier(jnp.sum(grads_out, axis=0)).reshape(-1), lax.optimization_barrier(jnp.sum(grads_gain, axis=0)))
```

```python
import jax
import jax.numpy as jnp
from jax import lax
from jax.sharding import PartitionSpec as P

HEAD_DIM = 64
TOK_DEV = 128


def shifted(value, axis, steps):
    count = lax.axis_size(axis)
    pairs = [(source, (source + steps) % count) for source in range(count)]
    return lax.ppermute(value, axis, pairs)


def layer_norm(tokens, ln_gain):
    values = tokens.astype(jnp.float32)
    center = values - jnp.mean(values, axis=-1, keepdims=True)
    spread = jnp.mean(center * center, axis=-1, keepdims=True)
    normed = center * lax.rsqrt(spread + 1e-05)
    return (normed, (normed * ln_gain).astype(jnp.bfloat16))


def align_terms(student, target):
    target_f = target.astype(jnp.float32)
    inv_y = lax.rsqrt(jnp.sum(student * student, axis=-1, keepdims=True) + 1e-06)
    inv_t = lax.rsqrt(jnp.sum(target_f * target_f, axis=-1, keepdims=True) + 1e-06)
    differ = student * inv_y - target_f * inv_t
    token_loss = jnp.sum(differ * differ, axis=-1)
    slopes = 2.0 * differ
    grad_y = inv_y * slopes - student * (inv_y * inv_y * inv_y) * jnp.sum(
        slopes * student, axis=-1, keepdims=True
    )
    return (token_loss, grad_y)


def key_mask(key_count, rows, heads):
    slot_idx = jnp.arange(rows, dtype=jnp.int32)
    halves = slot_idx[None, :] < key_count[:, None]
    return jnp.repeat(halves, heads // 2, axis=0)


def head_scores(queries, pair_rows, key_count):
    rows = pair_rows.shape[0]
    heads = queries.shape[1]
    split_kv = pair_rows.reshape(rows, heads, 2, HEAD_DIM)
    scores = (
        jnp.einsum("qhd,khd->hqk", queries, split_kv[:, :, 0], preferred_element_type=jnp.float32)
        * 0.125
    )
    mask_rows = key_mask(key_count, rows, heads)
    return (jnp.where(mask_rows[:, None, :], scores, -1e30), split_kv)


def absorb(state, queries, pair_rows, key_count):
    row_max, row_sum, blended = state
    scores, split_kv = head_scores(queries, pair_rows, key_count)
    new_max = jnp.maximum(row_max, jnp.max(scores, axis=2))
    rescale = jnp.exp(row_max - new_max)
    weights = jnp.exp(scores - new_max[:, :, None])
    row_sum = row_sum * rescale + jnp.sum(weights, axis=2)
    blended = blended * rescale[:, :, None] + jnp.einsum(
        "hqk,khd->hqd",
        weights.astype(jnp.bfloat16),
        split_kv[:, :, 1],
        preferred_element_type=jnp.float32,
    )
    return (new_max, row_sum, blended)


def contribution(queries, grad_heads, log_total, row_dot, pair_rows, key_count):
    scores, split_kv = head_scores(queries, pair_rows, key_count)
    prob_full = jnp.exp(scores - log_total[:, :, None])
    d_value = jnp.einsum(
        "hqk,qhd->khd",
        prob_full.astype(jnp.bfloat16),
        grad_heads,
        preferred_element_type=jnp.float32,
    )
    d_prob = jnp.einsum(
        "qhd,khd->hqk", grad_heads, split_kv[:, :, 1], preferred_element_type=jnp.float32
    )
    d_score = (prob_full * (d_prob - row_dot[:, :, None])).astype(jnp.bfloat16)
    d_query = 0.125 * jnp.einsum(
        "hqk,khd->qhd", d_score, split_kv[:, :, 0], preferred_element_type=jnp.float32
    )
    d_key = 0.125 * jnp.einsum("hqk,qhd->khd", d_score, queries, preferred_element_type=jnp.float32)
    rows = pair_rows.shape[0]
    return (d_query, jnp.stack([d_key, d_value], axis=2).reshape(rows, -1))


def move_keys(pair_rows):
    moved = shifted(pair_rows, "seq", 1)
    return moved


def move_grads(accum):
    moved = shifted(accum.astype(jnp.bfloat16), "seq", 1).astype(accum.dtype)
    return moved


def per_device(raw_tokens, teacher, keep_rows, w_qkv, w_out, ln_gain):
    shards = lax.axis_size("seq")
    my_index = lax.axis_index("seq")
    row_ids = keep_rows[0]
    list_slots = row_ids.shape[0]
    is_kept = row_ids >= 0
    kept_count = jnp.sum(is_kept.astype(jnp.int32))
    safe_ids = jnp.maximum(row_ids, 0)
    kept_tokens = jnp.where(is_kept[:, None], raw_tokens[0][safe_ids], jnp.zeros((), jnp.bfloat16))
    kept_target = jnp.where(is_kept[:, None], teacher[0][safe_ids], jnp.zeros((), jnp.bfloat16))
    count_table = lax.all_gather(kept_count.reshape(1), "seq", axis=0, tiled=True)
    shard_ids = jnp.arange(shards, dtype=jnp.int32)
    per_peer = -(-list_slots // shards)
    starts = jnp.cumsum(count_table) - count_table
    before = jnp.sum(jnp.where(shard_ids < my_index, count_table, 0))
    slot_ids = jnp.arange(per_peer, dtype=jnp.int32)
    pick = (shard_ids[:, None] - before) % shards + slot_ids[None, :] * shards
    pick_ok = pick < kept_count
    pick_safe = jnp.minimum(pick, list_slots - 1)
    send_tokens = jnp.where(
        pick_ok[:, :, None], kept_tokens[pick_safe], jnp.zeros((), jnp.bfloat16)
    )
    send_target = jnp.where(
        pick_ok[:, :, None], kept_target[pick_safe], jnp.zeros((), jnp.bfloat16)
    )
    got_tokens, got_target = (
        lax.all_to_all(send_tokens, "seq", split_axis=0, concat_axis=0, tiled=True),
        lax.all_to_all(send_target, "seq", split_axis=0, concat_axis=0, tiled=True),
    )
    from_pick = (my_index - starts[:, None]) % shards + slot_ids[None, :] * shards
    from_ok = from_pick < count_table[:, None]
    place = jnp.where(from_ok, (starts[:, None] + from_pick) // shards, TOK_DEV).reshape(-1)
    width = got_tokens.shape[2]
    tokens = (
        jnp.zeros((TOK_DEV, width), jnp.bfloat16)
        .at[place]
        .set(got_tokens.reshape(-1, width), mode="drop")
    )
    target = (
        jnp.zeros((TOK_DEV, width), jnp.bfloat16)
        .at[place]
        .set(got_target.reshape(-1, width), mode="drop")
    )
    live_count = jnp.full((), TOK_DEV, jnp.int32)
    anchor_table = jnp.full((shards,), TOK_DEV, jnp.int32)

    def counts_at(step):
        front_count = jnp.sum(jnp.where(shard_ids == (my_index - step) % shards, anchor_table, 0))
        return jnp.stack([front_count, front_count])

    rows = tokens.shape[0]
    inner = w_out.shape[0]
    heads = inner // HEAD_DIM
    normed, hidden = layer_norm(tokens, ln_gain)
    projected = jnp.dot(hidden, w_qkv, preferred_element_type=jnp.float32)
    queries = projected[:, :inner].astype(jnp.bfloat16).reshape(rows, heads, HEAD_DIM)
    pair_rows = projected[:, inner:].astype(jnp.bfloat16)
    start_state = (
        jnp.full((heads, rows), -1e30, jnp.float32),
        jnp.zeros((heads, rows), jnp.float32),
        jnp.zeros((heads, rows, HEAD_DIM), jnp.float32),
    )
    steps_ids = jnp.arange(1, shards, dtype=jnp.int32)
    own_count = counts_at(jnp.zeros((), jnp.int32))
    state = absorb(start_state, queries, pair_rows, own_count)

    def forward_step(carry, step):
        travel_rows, inner_state = carry
        travel_rows = move_keys(travel_rows)
        inner_state = absorb(inner_state, queries, travel_rows, counts_at(step))
        return ((travel_rows, inner_state), travel_rows)

    (unused_rows, state), stored_rows = lax.scan(forward_step, (pair_rows, state), steps_ids)
    row_max, row_sum, blended = state
    log_total = row_max + jnp.log(row_sum)
    attended = (
        (blended / row_sum[:, :, None]).transpose(1, 0, 2).reshape(rows, inner).astype(jnp.bfloat16)
    )
    student = tokens.astype(jnp.float32) + jnp.dot(
        attended, w_out, preferred_element_type=jnp.float32
    )
    token_loss, grad_y = align_terms(student, target)
    is_live = jnp.arange(rows, dtype=jnp.int32) < live_count
    token_loss = jnp.where(is_live, token_loss, 0.0)
    grad_b = jnp.where(is_live[:, None], grad_y, 0.0).astype(jnp.bfloat16)
    grad_wout = jnp.dot(attended.T, grad_b, preferred_element_type=jnp.float32)
    grad_heads = (
        jnp.dot(grad_b, w_out.T, preferred_element_type=jnp.float32)
        .astype(jnp.bfloat16)
        .reshape(rows, heads, HEAD_DIM)
    )
    row_dot = jnp.sum(
        grad_heads.astype(jnp.float32)
        * attended.reshape(rows, heads, HEAD_DIM).astype(jnp.float32),
        axis=2,
    ).T
    d_query, accum = contribution(queries, grad_heads, log_total, row_dot, pair_rows, own_count)

    def backward_step(carry, stored):
        query_sum, travel_grads = carry
        block_rows, step = stored
        travel_grads = move_grads(travel_grads)
        part_query, part_pairs = contribution(
            queries, grad_heads, log_total, row_dot, block_rows, counts_at(step)
        )
        return ((query_sum + part_query, travel_grads + part_pairs), None)

    (d_query, accum), unused_out = lax.scan(
        backward_step, (d_query, accum), (stored_rows, steps_ids)
    )
    accum = move_grads(accum)
    d_proj = jnp.concatenate([d_query.reshape(rows, inner), accum], axis=1).astype(jnp.bfloat16)
    grad_wqkv = jnp.dot(hidden.T, d_proj, preferred_element_type=jnp.float32)
    d_hidden = jnp.dot(d_proj, w_qkv.T, preferred_element_type=jnp.float32)
    grad_ln = jnp.sum(d_hidden * normed, axis=0)
    loss_part = jnp.sum(token_loss)
    loss_total, grad_gain = lax.psum((loss_part, grad_ln), ("seq", "clip"))
    grad_qkv, grad_out = (
        lax.psum_scatter(grad_wqkv, ("seq", "clip"), scatter_dimension=0, tiled=True).astype(jnp.float32).reshape(-1),
        lax.psum_scatter(grad_wout, ("seq", "clip"), scatter_dimension=0, tiled=True).astype(jnp.float32).reshape(-1),
    )
    count_all = shards * lax.axis_size("clip") * TOK_DEV
    return (loss_total / count_all, grad_qkv, grad_out, grad_gain)


def solution(mesh):
    placed = (P("clip", "seq", None), P("clip", "seq", None), P("clip", "seq"), P(), P(), P())
    return jax.shard_map(
        per_device,
        mesh=mesh,
        in_specs=placed,
        out_specs=(P(), P(("seq", "clip")), P(("seq", "clip")), P()),
        check_vma=False,
    )
```

```python
import jax
import jax.numpy as jnp
from jax import lax
from jax.sharding import PartitionSpec as P

HEAD_DIM = 64
TOK_DEV = 128


def shifted(value, axis, steps):
    count = lax.axis_size(axis)
    pairs = [(source, (source + steps) % count) for source in range(count)]
    return lax.ppermute(value, axis, pairs)


def layer_norm(tokens, ln_gain):
    values = tokens.astype(jnp.float32)
    center = values - jnp.mean(values, axis=-1, keepdims=True)
    spread = jnp.mean(center * center, axis=-1, keepdims=True)
    normed = center * lax.rsqrt(spread + 1e-05)
    return (normed, (normed * ln_gain).astype(jnp.bfloat16))


def align_terms(student, target):
    target_f = target.astype(jnp.float32)
    inv_y = lax.rsqrt(jnp.sum(student * student, axis=-1, keepdims=True) + 1e-06)
    inv_t = lax.rsqrt(jnp.sum(target_f * target_f, axis=-1, keepdims=True) + 1e-06)
    differ = student * inv_y - target_f * inv_t
    token_loss = jnp.sum(differ * differ, axis=-1)
    slopes = 2.0 * differ
    grad_y = inv_y * slopes - student * (inv_y * inv_y * inv_y) * jnp.sum(
        slopes * student, axis=-1, keepdims=True
    )
    return (token_loss, grad_y)


def key_mask(key_count, rows, heads):
    slot_idx = jnp.arange(rows, dtype=jnp.int32)
    halves = slot_idx[None, :] < key_count[:, None]
    return jnp.repeat(halves, heads // 2, axis=0)


def head_scores(queries, pair_rows, key_count):
    rows = pair_rows.shape[0]
    heads = queries.shape[1]
    split_kv = pair_rows.reshape(rows, heads, 2, HEAD_DIM)
    scores = (
        jnp.einsum("qhd,khd->hqk", queries, split_kv[:, :, 0], preferred_element_type=jnp.float32)
        * 0.125
    )
    mask_rows = key_mask(key_count, rows, heads)
    return (jnp.where(mask_rows[:, None, :], scores, -1e30), split_kv)


def absorb(state, queries, pair_rows, key_count):
    row_max, row_sum, blended = state
    scores, split_kv = head_scores(queries, pair_rows, key_count)
    new_max = jnp.maximum(row_max, jnp.max(scores, axis=2))
    rescale = jnp.exp(row_max - new_max)
    weights = jnp.exp(scores - new_max[:, :, None])
    row_sum = row_sum * rescale + jnp.sum(weights, axis=2)
    blended = blended * rescale[:, :, None] + jnp.einsum(
        "hqk,khd->hqd",
        weights.astype(jnp.bfloat16),
        split_kv[:, :, 1],
        preferred_element_type=jnp.float32,
    )
    return (new_max, row_sum, blended)


def contribution(queries, grad_heads, log_total, row_dot, pair_rows, key_count):
    scores, split_kv = head_scores(queries, pair_rows, key_count)
    prob_full = jnp.exp(scores - log_total[:, :, None])
    d_value = jnp.einsum(
        "hqk,qhd->khd",
        prob_full.astype(jnp.bfloat16),
        grad_heads,
        preferred_element_type=jnp.float32,
    )
    d_prob = jnp.einsum(
        "qhd,khd->hqk", grad_heads, split_kv[:, :, 1], preferred_element_type=jnp.float32
    )
    d_score = (prob_full * (d_prob - row_dot[:, :, None])).astype(jnp.bfloat16)
    d_query = 0.125 * jnp.einsum(
        "hqk,khd->qhd", d_score, split_kv[:, :, 0], preferred_element_type=jnp.float32
    )
    d_key = 0.125 * jnp.einsum("hqk,qhd->khd", d_score, queries, preferred_element_type=jnp.float32)
    rows = pair_rows.shape[0]
    return (d_query, jnp.stack([d_key, d_value], axis=2).reshape(rows, -1))


def move_keys(pair_rows):
    moved = shifted(pair_rows, "seq", 1)
    return moved


def move_grads(accum):
    moved = shifted(accum.astype(jnp.bfloat16), "seq", 1).astype(accum.dtype)
    return moved


def per_device(raw_tokens, teacher, keep_rows, w_qkv, w_out, ln_gain):
    shards = lax.axis_size("seq")
    my_index = lax.axis_index("seq")
    row_ids = keep_rows[0]
    list_slots = row_ids.shape[0]
    is_kept = row_ids >= 0
    kept_count = jnp.sum(is_kept.astype(jnp.int32))
    safe_ids = jnp.maximum(row_ids, 0)
    kept_tokens = jnp.where(is_kept[:, None], raw_tokens[0][safe_ids], jnp.zeros((), jnp.bfloat16))
    kept_target = jnp.where(is_kept[:, None], teacher[0][safe_ids], jnp.zeros((), jnp.bfloat16))
    count_table = lax.all_gather(kept_count.reshape(1), "seq", axis=0, tiled=True)
    shard_ids = jnp.arange(shards, dtype=jnp.int32)
    per_peer = -(-list_slots // shards)
    starts = jnp.cumsum(count_table) - count_table
    before = jnp.sum(jnp.where(shard_ids < my_index, count_table, 0))
    slot_ids = jnp.arange(per_peer, dtype=jnp.int32)
    pick = (shard_ids[:, None] - before) % shards + slot_ids[None, :] * shards
    pick_ok = pick < kept_count
    pick_safe = jnp.minimum(pick, list_slots - 1)
    send_tokens = jnp.where(
        pick_ok[:, :, None], kept_tokens[pick_safe], jnp.zeros((), jnp.bfloat16)
    )
    send_target = jnp.where(
        pick_ok[:, :, None], kept_target[pick_safe], jnp.zeros((), jnp.bfloat16)
    )
    got_tokens, got_target = (
        lax.all_to_all(send_tokens, "seq", split_axis=0, concat_axis=0, tiled=True),
        lax.all_to_all(send_target, "seq", split_axis=0, concat_axis=0, tiled=True),
    )
    from_pick = (my_index - starts[:, None]) % shards + slot_ids[None, :] * shards
    from_ok = from_pick < count_table[:, None]
    place = jnp.where(from_ok, (starts[:, None] + from_pick) // shards, TOK_DEV).reshape(-1)
    width = got_tokens.shape[2]
    tokens = (
        jnp.zeros((TOK_DEV, width), jnp.bfloat16)
        .at[place]
        .set(got_tokens.reshape(-1, width), mode="drop")
    )
    target = (
        jnp.zeros((TOK_DEV, width), jnp.bfloat16)
        .at[place]
        .set(got_target.reshape(-1, width), mode="drop")
    )
    live_count = jnp.full((), TOK_DEV, jnp.int32)
    anchor_table = jnp.full((shards,), TOK_DEV, jnp.int32)

    def counts_at(step):
        front_count = jnp.sum(jnp.where(shard_ids == (my_index - step) % shards, anchor_table, 0))
        return jnp.stack([front_count, front_count])

    rows = tokens.shape[0]
    inner = w_out.shape[0]
    heads = inner // HEAD_DIM
    normed, hidden = layer_norm(tokens, ln_gain)
    projected = jnp.dot(hidden, w_qkv, preferred_element_type=jnp.float32)
    queries = projected[:, :inner].astype(jnp.bfloat16).reshape(rows, heads, HEAD_DIM)
    pair_rows = projected[:, inner:].astype(jnp.bfloat16)
    start_state = (
        jnp.full((heads, rows), -1e30, jnp.float32),
        jnp.zeros((heads, rows), jnp.float32),
        jnp.zeros((heads, rows, HEAD_DIM), jnp.float32),
    )
    steps_ids = jnp.arange(1, shards, dtype=jnp.int32)
    own_count = counts_at(jnp.zeros((), jnp.int32))
    state = absorb(start_state, queries, pair_rows, own_count)

    def forward_step(carry, step):
        travel_rows, inner_state = carry
        travel_rows = move_keys(travel_rows)
        inner_state = absorb(inner_state, queries, travel_rows, counts_at(step))
        return ((travel_rows, inner_state), travel_rows)

    (unused_rows, state), stored_rows = lax.scan(forward_step, (pair_rows, state), steps_ids)
    row_max, row_sum, blended = state
    log_total = row_max + jnp.log(row_sum)
    attended = (
        (blended / row_sum[:, :, None]).transpose(1, 0, 2).reshape(rows, inner).astype(jnp.bfloat16)
    )
    student = tokens.astype(jnp.float32) + jnp.dot(
        attended, w_out, preferred_element_type=jnp.float32
    )
    token_loss, grad_y = align_terms(student, target)
    is_live = jnp.arange(rows, dtype=jnp.int32) < live_count
    token_loss = jnp.where(is_live, token_loss, 0.0)
    grad_b = jnp.where(is_live[:, None], grad_y, 0.0).astype(jnp.bfloat16)
    grad_wout = jnp.dot(attended.T, grad_b, preferred_element_type=jnp.float32)
    grad_heads = (
        jnp.dot(grad_b, w_out.T, preferred_element_type=jnp.float32)
        .astype(jnp.bfloat16)
        .reshape(rows, heads, HEAD_DIM)
    )
    row_dot = jnp.sum(
        grad_heads.astype(jnp.float32)
        * attended.reshape(rows, heads, HEAD_DIM).astype(jnp.float32),
        axis=2,
    ).T
    d_query, accum = contribution(queries, grad_heads, log_total, row_dot, pair_rows, own_count)

    def backward_step(carry, stored):
        query_sum, travel_grads = carry
        block_rows, step = stored
        travel_grads = move_grads(travel_grads)
        part_query, part_pairs = contribution(
            queries, grad_heads, log_total, row_dot, block_rows, counts_at(step)
        )
        return ((query_sum + part_query, travel_grads + part_pairs), None)

    (d_query, accum), unused_out = lax.scan(
        backward_step, (d_query, accum), (stored_rows, steps_ids)
    )
    accum = move_grads(accum)
    d_proj = jnp.concatenate([d_query.reshape(rows, inner), accum], axis=1).astype(jnp.bfloat16)
    grad_wqkv = jnp.dot(hidden.T, d_proj, preferred_element_type=jnp.float32)
    d_hidden = jnp.dot(d_proj, w_qkv.T, preferred_element_type=jnp.float32)
    grad_ln = jnp.sum(d_hidden * normed, axis=0)
    loss_part = jnp.sum(token_loss)
    loss_total, grad_gain = lax.psum((loss_part, grad_ln), ("seq", "clip"))
    grad_qkv, grad_out = (
        lax.psum_scatter(grad_wqkv.astype(jnp.bfloat16), ("seq", "clip"), scatter_dimension=0, tiled=True).astype(jnp.float32).reshape(-1),
        lax.psum_scatter(grad_wout.astype(jnp.bfloat16), ("seq", "clip"), scatter_dimension=0, tiled=True).astype(jnp.float32).reshape(-1),
    )
    count_all = shards * lax.axis_size("clip") * TOK_DEV
    return (loss_total / count_all, grad_qkv, grad_out, grad_gain)


def solution(mesh):
    placed = (P("clip", "seq", None), P("clip", "seq", None), P("clip", "seq"), P(), P(), P())
    return jax.shard_map(
        per_device,
        mesh=mesh,
        in_specs=placed,
        out_specs=(P(), P(("seq", "clip")), P(("seq", "clip")), P()),
        check_vma=False,
    )
```

```python
import jax
import jax.numpy as jnp
from jax import lax
from jax.sharding import PartitionSpec as P

HEAD_DIM = 64
TOK_DEV = 128


def shifted(value, axis, steps):
    count = lax.axis_size(axis)
    pairs = [(source, (source + steps) % count) for source in range(count)]
    return lax.ppermute(value, axis, pairs)


def layer_norm(tokens, ln_gain):
    values = tokens.astype(jnp.float32)
    center = values - jnp.mean(values, axis=-1, keepdims=True)
    spread = jnp.mean(center * center, axis=-1, keepdims=True)
    normed = center * lax.rsqrt(spread + 1e-05)
    return (normed, (normed * ln_gain).astype(jnp.bfloat16))


def align_terms(student, target):
    target_f = target.astype(jnp.float32)
    inv_y = lax.rsqrt(jnp.sum(student * student, axis=-1, keepdims=True) + 1e-06)
    inv_t = lax.rsqrt(jnp.sum(target_f * target_f, axis=-1, keepdims=True) + 1e-06)
    differ = student * inv_y - target_f * inv_t
    token_loss = jnp.sum(differ * differ, axis=-1)
    slopes = 2.0 * differ
    grad_y = inv_y * slopes - student * (inv_y * inv_y * inv_y) * jnp.sum(
        slopes * student, axis=-1, keepdims=True
    )
    return (token_loss, grad_y)


def key_mask(key_count, rows, heads):
    slot_idx = jnp.arange(rows, dtype=jnp.int32)
    halves = slot_idx[None, :] < key_count[:, None]
    return jnp.repeat(halves, heads // 2, axis=0)


def head_scores(queries, pair_rows, key_count):
    rows = pair_rows.shape[0]
    heads = queries.shape[1]
    split_kv = pair_rows.reshape(rows, heads, 2, HEAD_DIM)
    scores = (
        jnp.einsum("qhd,khd->hqk", queries, split_kv[:, :, 0], preferred_element_type=jnp.float32)
        * 0.125
    )
    mask_rows = key_mask(key_count, rows, heads)
    return (jnp.where(mask_rows[:, None, :], scores, -1e30), split_kv)


def absorb(state, queries, pair_rows, key_count):
    row_max, row_sum, blended = state
    scores, split_kv = head_scores(queries, pair_rows, key_count)
    new_max = jnp.maximum(row_max, jnp.max(scores, axis=2))
    rescale = jnp.exp(row_max - new_max)
    weights = jnp.exp(scores - new_max[:, :, None])
    row_sum = row_sum * rescale + jnp.sum(weights, axis=2)
    blended = blended * rescale[:, :, None] + jnp.einsum(
        "hqk,khd->hqd",
        weights.astype(jnp.bfloat16),
        split_kv[:, :, 1],
        preferred_element_type=jnp.float32,
    )
    return (new_max, row_sum, blended)


def contribution(queries, grad_heads, log_total, row_dot, pair_rows, key_count):
    scores, split_kv = head_scores(queries, pair_rows, key_count)
    prob_full = jnp.exp(scores - log_total[:, :, None])
    d_value = jnp.einsum(
        "hqk,qhd->khd",
        prob_full.astype(jnp.bfloat16),
        grad_heads,
        preferred_element_type=jnp.float32,
    )
    d_prob = jnp.einsum(
        "qhd,khd->hqk", grad_heads, split_kv[:, :, 1], preferred_element_type=jnp.float32
    )
    d_score = (prob_full * (d_prob - row_dot[:, :, None])).astype(jnp.bfloat16)
    d_query = 0.125 * jnp.einsum(
        "hqk,khd->qhd", d_score, split_kv[:, :, 0], preferred_element_type=jnp.float32
    )
    d_key = 0.125 * jnp.einsum("hqk,qhd->khd", d_score, queries, preferred_element_type=jnp.float32)
    rows = pair_rows.shape[0]
    return (d_query, jnp.stack([d_key, d_value], axis=2).reshape(rows, -1))


def move_keys(pair_rows):
    moved = shifted(pair_rows, "seq", 1)
    return moved


def move_grads(accum):
    moved = shifted(accum.astype(jnp.bfloat16), "seq", 1).astype(accum.dtype)
    return moved


def halving_scatter(parts):
    seq_n = lax.axis_size("seq")
    clip_n = lax.axis_size("clip")
    seq_bits = seq_n.bit_length() - 1
    clip_bits = clip_n.bit_length() - 1
    assert (1 << seq_bits) == seq_n and (1 << clip_bits) == clip_n
    blocks = seq_n * clip_n
    sizes = [p.size // blocks for p in parts]
    flat = jnp.concatenate([p.reshape(blocks, -1) for p in parts], axis=1)
    data = flat.reshape([2] * (seq_bits + clip_bits) + [flat.shape[1]])
    seq_me = lax.axis_index("seq")
    clip_me = lax.axis_index("clip")
    order = [("seq", bit) for bit in range(seq_bits)] + [("clip", bit) for bit in range(clip_bits)]
    dims = {}
    for bit in range(seq_bits):
        dims[("seq", bit)] = seq_bits - 1 - bit
    for bit in range(clip_bits):
        dims[("clip", bit)] = seq_bits + clip_bits - 1 - bit
    removed = []
    for axis, bit in order:
        dim = dims[(axis, bit)] - sum(1 for r in removed if r < dims[(axis, bit)])
        me = seq_me if axis == "seq" else clip_me
        mine = (me >> bit) & 1
        keep = lax.dynamic_index_in_dim(data, mine, axis=dim, keepdims=False)
        give = lax.dynamic_index_in_dim(data, 1 - mine, axis=dim, keepdims=False)
        count = seq_n if axis == "seq" else clip_n
        pairs = [(src, src ^ (1 << bit)) for src in range(count)]
        got = lax.ppermute(give.astype(jnp.bfloat16), axis, pairs)
        data = keep + got.astype(jnp.float32)
        removed.append(dims[(axis, bit)])
    out = []
    start = 0
    for size in sizes:
        out.append(data[start:start + size])
        start += size
    return out


def per_device(raw_tokens, teacher, keep_rows, w_qkv, w_out, ln_gain):
    shards = lax.axis_size("seq")
    my_index = lax.axis_index("seq")
    row_ids = keep_rows[0]
    list_slots = row_ids.shape[0]
    is_kept = row_ids >= 0
    kept_count = jnp.sum(is_kept.astype(jnp.int32))
    safe_ids = jnp.maximum(row_ids, 0)
    kept_tokens = jnp.where(is_kept[:, None], raw_tokens[0][safe_ids], jnp.zeros((), jnp.bfloat16))
    kept_target = jnp.where(is_kept[:, None], teacher[0][safe_ids], jnp.zeros((), jnp.bfloat16))
    count_table = lax.all_gather(kept_count.reshape(1), "seq", axis=0, tiled=True)
    shard_ids = jnp.arange(shards, dtype=jnp.int32)
    per_peer = -(-list_slots // shards)
    starts = jnp.cumsum(count_table) - count_table
    before = jnp.sum(jnp.where(shard_ids < my_index, count_table, 0))
    slot_ids = jnp.arange(per_peer, dtype=jnp.int32)
    pick = (shard_ids[:, None] - before) % shards + slot_ids[None, :] * shards
    pick_ok = pick < kept_count
    pick_safe = jnp.minimum(pick, list_slots - 1)
    send_tokens = jnp.where(
        pick_ok[:, :, None], kept_tokens[pick_safe], jnp.zeros((), jnp.bfloat16)
    )
    send_target = jnp.where(
        pick_ok[:, :, None], kept_target[pick_safe], jnp.zeros((), jnp.bfloat16)
    )
    got_tokens, got_target = (
        lax.all_to_all(send_tokens, "seq", split_axis=0, concat_axis=0, tiled=True),
        lax.all_to_all(send_target, "seq", split_axis=0, concat_axis=0, tiled=True),
    )
    from_pick = (my_index - starts[:, None]) % shards + slot_ids[None, :] * shards
    from_ok = from_pick < count_table[:, None]
    place = jnp.where(from_ok, (starts[:, None] + from_pick) // shards, TOK_DEV).reshape(-1)
    width = got_tokens.shape[2]
    tokens = (
        jnp.zeros((TOK_DEV, width), jnp.bfloat16)
        .at[place]
        .set(got_tokens.reshape(-1, width), mode="drop")
    )
    target = (
        jnp.zeros((TOK_DEV, width), jnp.bfloat16)
        .at[place]
        .set(got_target.reshape(-1, width), mode="drop")
    )
    live_count = jnp.full((), TOK_DEV, jnp.int32)
    anchor_table = jnp.full((shards,), TOK_DEV, jnp.int32)

    def counts_at(step):
        front_count = jnp.sum(jnp.where(shard_ids == (my_index - step) % shards, anchor_table, 0))
        return jnp.stack([front_count, front_count])

    rows = tokens.shape[0]
    inner = w_out.shape[0]
    heads = inner // HEAD_DIM
    normed, hidden = layer_norm(tokens, ln_gain)
    projected = jnp.dot(hidden, w_qkv, preferred_element_type=jnp.float32)
    queries = projected[:, :inner].astype(jnp.bfloat16).reshape(rows, heads, HEAD_DIM)
    pair_rows = projected[:, inner:].astype(jnp.bfloat16)
    start_state = (
        jnp.full((heads, rows), -1e30, jnp.float32),
        jnp.zeros((heads, rows), jnp.float32),
        jnp.zeros((heads, rows, HEAD_DIM), jnp.float32),
    )
    steps_ids = jnp.arange(1, shards, dtype=jnp.int32)
    own_count = counts_at(jnp.zeros((), jnp.int32))
    state = absorb(start_state, queries, pair_rows, own_count)

    def forward_step(carry, step):
        travel_rows, inner_state = carry
        travel_rows = move_keys(travel_rows)
        inner_state = absorb(inner_state, queries, travel_rows, counts_at(step))
        return ((travel_rows, inner_state), travel_rows)

    (unused_rows, state), stored_rows = lax.scan(forward_step, (pair_rows, state), steps_ids)
    row_max, row_sum, blended = state
    log_total = row_max + jnp.log(row_sum)
    attended = (
        (blended / row_sum[:, :, None]).transpose(1, 0, 2).reshape(rows, inner).astype(jnp.bfloat16)
    )
    student = tokens.astype(jnp.float32) + jnp.dot(
        attended, w_out, preferred_element_type=jnp.float32
    )
    token_loss, grad_y = align_terms(student, target)
    is_live = jnp.arange(rows, dtype=jnp.int32) < live_count
    token_loss = jnp.where(is_live, token_loss, 0.0)
    grad_b = jnp.where(is_live[:, None], grad_y, 0.0).astype(jnp.bfloat16)
    grad_wout = jnp.dot(attended.T, grad_b, preferred_element_type=jnp.float32)
    grad_heads = (
        jnp.dot(grad_b, w_out.T, preferred_element_type=jnp.float32)
        .astype(jnp.bfloat16)
        .reshape(rows, heads, HEAD_DIM)
    )
    row_dot = jnp.sum(
        grad_heads.astype(jnp.float32)
        * attended.reshape(rows, heads, HEAD_DIM).astype(jnp.float32),
        axis=2,
    ).T
    d_query, accum = contribution(queries, grad_heads, log_total, row_dot, pair_rows, own_count)

    def backward_step(carry, stored):
        query_sum, travel_grads = carry
        block_rows, step = stored
        travel_grads = move_grads(travel_grads)
        part_query, part_pairs = contribution(
            queries, grad_heads, log_total, row_dot, block_rows, counts_at(step)
        )
        return ((query_sum + part_query, travel_grads + part_pairs), None)

    (d_query, accum), unused_out = lax.scan(
        backward_step, (d_query, accum), (stored_rows, steps_ids)
    )
    accum = move_grads(accum)
    d_proj = jnp.concatenate([d_query.reshape(rows, inner), accum], axis=1).astype(jnp.bfloat16)
    grad_wqkv = jnp.dot(hidden.T, d_proj, preferred_element_type=jnp.float32)
    d_hidden = jnp.dot(d_proj, w_qkv.T, preferred_element_type=jnp.float32)
    grad_ln = jnp.sum(d_hidden * normed, axis=0)
    loss_part = jnp.sum(token_loss)
    loss_total, grad_gain = lax.psum((loss_part, grad_ln), ("seq", "clip"))
    grad_qkv, grad_out = halving_scatter([grad_wqkv, grad_wout])
    count_all = shards * lax.axis_size("clip") * TOK_DEV
    return (loss_total / count_all, grad_qkv, grad_out, grad_gain)


def solution(mesh):
    placed = (P("clip", "seq", None), P("clip", "seq", None), P("clip", "seq"), P(), P(), P())
    return jax.shard_map(
        per_device,
        mesh=mesh,
        in_specs=placed,
        out_specs=(P(), P(("seq", "clip")), P(("seq", "clip")), P()),
        check_vma=False,
    )
```

```python
import jax
import jax.numpy as jnp
from jax import lax
from jax.sharding import PartitionSpec as P

HEAD_DIM = 64
TOK_DEV = 128


def shifted(value, axis, steps):
    count = lax.axis_size(axis)
    pairs = [(source, (source + steps) % count) for source in range(count)]
    return lax.ppermute(value, axis, pairs)


def layer_norm(tokens, ln_gain):
    values = tokens.astype(jnp.float32)
    center = values - jnp.mean(values, axis=-1, keepdims=True)
    spread = jnp.mean(center * center, axis=-1, keepdims=True)
    normed = center * lax.rsqrt(spread + 1e-05)
    return (normed, (normed * ln_gain).astype(jnp.bfloat16))


def align_terms(student, target):
    target_f = target.astype(jnp.float32)
    inv_y = lax.rsqrt(jnp.sum(student * student, axis=-1, keepdims=True) + 1e-06)
    inv_t = lax.rsqrt(jnp.sum(target_f * target_f, axis=-1, keepdims=True) + 1e-06)
    differ = student * inv_y - target_f * inv_t
    token_loss = jnp.sum(differ * differ, axis=-1)
    slopes = 2.0 * differ
    grad_y = inv_y * slopes - student * (inv_y * inv_y * inv_y) * jnp.sum(
        slopes * student, axis=-1, keepdims=True
    )
    return (token_loss, grad_y)


def key_mask(key_count, rows, heads):
    slot_idx = jnp.arange(rows, dtype=jnp.int32)
    halves = slot_idx[None, :] < key_count[:, None]
    return jnp.repeat(halves, heads // 2, axis=0)


def head_scores(queries, pair_rows, key_count):
    rows = pair_rows.shape[0]
    heads = queries.shape[1]
    split_kv = pair_rows.reshape(rows, heads, 2, HEAD_DIM)
    scores = (
        jnp.einsum("qhd,khd->hqk", queries, split_kv[:, :, 0], preferred_element_type=jnp.float32)
        * 0.125
    )
    mask_rows = key_mask(key_count, rows, heads)
    return (jnp.where(mask_rows[:, None, :], scores, -1e30), split_kv)


def absorb(state, queries, pair_rows, key_count):
    row_max, row_sum, blended = state
    scores, split_kv = head_scores(queries, pair_rows, key_count)
    new_max = jnp.maximum(row_max, jnp.max(scores, axis=2))
    rescale = jnp.exp(row_max - new_max)
    weights = jnp.exp(scores - new_max[:, :, None])
    row_sum = row_sum * rescale + jnp.sum(weights, axis=2)
    blended = blended * rescale[:, :, None] + jnp.einsum(
        "hqk,khd->hqd",
        weights.astype(jnp.bfloat16),
        split_kv[:, :, 1],
        preferred_element_type=jnp.float32,
    )
    return (new_max, row_sum, blended)


def contribution(queries, grad_heads, log_total, row_dot, pair_rows, key_count):
    scores, split_kv = head_scores(queries, pair_rows, key_count)
    prob_full = jnp.exp(scores - log_total[:, :, None])
    d_value = jnp.einsum(
        "hqk,qhd->khd",
        prob_full.astype(jnp.bfloat16),
        grad_heads,
        preferred_element_type=jnp.float32,
    )
    d_prob = jnp.einsum(
        "qhd,khd->hqk", grad_heads, split_kv[:, :, 1], preferred_element_type=jnp.float32
    )
    d_score = (prob_full * (d_prob - row_dot[:, :, None])).astype(jnp.bfloat16)
    d_query = 0.125 * jnp.einsum(
        "hqk,khd->qhd", d_score, split_kv[:, :, 0], preferred_element_type=jnp.float32
    )
    d_key = 0.125 * jnp.einsum("hqk,qhd->khd", d_score, queries, preferred_element_type=jnp.float32)
    rows = pair_rows.shape[0]
    return (d_query, jnp.stack([d_key, d_value], axis=2).reshape(rows, -1))


def move_keys(pair_rows):
    moved = shifted(pair_rows, "seq", 1)
    return moved


def move_grads(accum):
    moved = shifted(accum.astype(jnp.bfloat16), "seq", 1).astype(accum.dtype)
    return moved


def exchange_bits():
    seq_bits = lax.axis_size("seq").bit_length() - 1
    clip_bits = lax.axis_size("clip").bit_length() - 1
    assert (1 << seq_bits) == lax.axis_size("seq")
    assert (1 << clip_bits) == lax.axis_size("clip")
    return seq_bits, clip_bits


def exchange_order(values):
    seq_bits, clip_bits = exchange_bits()
    total = seq_bits + clip_bits
    lead = values.shape[0]
    split = values.reshape([lead] + [2] * total + [-1])
    seq_dims = [1 + seq_bits - 1 - bit for bit in range(seq_bits)]
    clip_dims = [1 + seq_bits + clip_bits - 1 - bit for bit in range(clip_bits)]
    perm = [0] + seq_dims + clip_dims + [total + 1]
    return split.transpose(perm).reshape(values.shape)


def halving_scatter(grad_wqkv, grad_wout, small):
    seq_bits, clip_bits = exchange_bits()
    total = seq_bits + clip_bits
    first = grad_wqkv.reshape([2] * total + [-1, grad_wqkv.shape[1]])
    second = grad_wout.reshape([2] * total + [-1, grad_wout.shape[1]])
    order = [("seq", bit) for bit in range(seq_bits)] + [("clip", bit) for bit in range(clip_bits)]
    for axis, bit in order:
        mine = (lax.axis_index(axis) >> bit) & 1
        count = lax.axis_size(axis)
        pairs = [(src, src ^ (1 << bit)) for src in range(count)]
        keep_a = lax.dynamic_index_in_dim(first, mine, axis=0, keepdims=False)
        give_a = lax.dynamic_index_in_dim(first, 1 - mine, axis=0, keepdims=False)
        keep_b = lax.dynamic_index_in_dim(second, mine, axis=0, keepdims=False)
        give_b = lax.dynamic_index_in_dim(second, 1 - mine, axis=0, keepdims=False)
        got_a, got_b, got_s = lax.ppermute(
            (give_a.astype(jnp.bfloat16), give_b.astype(jnp.bfloat16), small), axis, pairs
        )
        first = keep_a + got_a.astype(jnp.float32)
        second = keep_b + got_b.astype(jnp.float32)
        small = small + got_s
    return (first, second, small)


def per_device(raw_tokens, teacher, keep_rows, w_qkv, w_out, ln_gain):
    shards = lax.axis_size("seq")
    my_index = lax.axis_index("seq")
    row_ids = keep_rows[0]
    list_slots = row_ids.shape[0]
    is_kept = row_ids >= 0
    kept_count = jnp.sum(is_kept.astype(jnp.int32))
    safe_ids = jnp.maximum(row_ids, 0)
    kept_tokens = jnp.where(is_kept[:, None], raw_tokens[0][safe_ids], jnp.zeros((), jnp.bfloat16))
    kept_target = jnp.where(is_kept[:, None], teacher[0][safe_ids], jnp.zeros((), jnp.bfloat16))
    count_table = lax.all_gather(kept_count.reshape(1), "seq", axis=0, tiled=True)
    shard_ids = jnp.arange(shards, dtype=jnp.int32)
    per_peer = -(-list_slots // shards)
    starts = jnp.cumsum(count_table) - count_table
    before = jnp.sum(jnp.where(shard_ids < my_index, count_table, 0))
    slot_ids = jnp.arange(per_peer, dtype=jnp.int32)
    pick = (shard_ids[:, None] - before) % shards + slot_ids[None, :] * shards
    pick_ok = pick < kept_count
    pick_safe = jnp.minimum(pick, list_slots - 1)
    send_tokens = jnp.where(
        pick_ok[:, :, None], kept_tokens[pick_safe], jnp.zeros((), jnp.bfloat16)
    )
    send_target = jnp.where(
        pick_ok[:, :, None], kept_target[pick_safe], jnp.zeros((), jnp.bfloat16)
    )
    got_tokens, got_target = (
        lax.all_to_all(send_tokens, "seq", split_axis=0, concat_axis=0, tiled=True),
        lax.all_to_all(send_target, "seq", split_axis=0, concat_axis=0, tiled=True),
    )
    from_pick = (my_index - starts[:, None]) % shards + slot_ids[None, :] * shards
    from_ok = from_pick < count_table[:, None]
    place = jnp.where(from_ok, (starts[:, None] + from_pick) // shards, TOK_DEV).reshape(-1)
    width = got_tokens.shape[2]
    tokens = (
        jnp.zeros((TOK_DEV, width), jnp.bfloat16)
        .at[place]
        .set(got_tokens.reshape(-1, width), mode="drop")
    )
    target = (
        jnp.zeros((TOK_DEV, width), jnp.bfloat16)
        .at[place]
        .set(got_target.reshape(-1, width), mode="drop")
    )
    rows = tokens.shape[0]
    inner = w_out.shape[0]
    heads = inner // HEAD_DIM
    normed, hidden = layer_norm(tokens, ln_gain)
    projected = jnp.dot(hidden, w_qkv, preferred_element_type=jnp.float32)
    queries = projected[:, :inner].astype(jnp.bfloat16).reshape(rows, heads, HEAD_DIM)
    pair_rows = projected[:, inner:].astype(jnp.bfloat16)
    gathered = jnp.stack([pair_rows] + [shifted(pair_rows, "seq", step) for step in range(1, shards)])
    split_kv = gathered.reshape(shards * rows, heads, 2, HEAD_DIM)
    all_keys = split_kv[:, :, 0]
    all_values = split_kv[:, :, 1]
    scores = (
        jnp.einsum("qhd,khd->hqk", queries, all_keys, preferred_element_type=jnp.float32) * 0.125
    )
    row_max = jnp.max(scores, axis=2)
    weights = jnp.exp(scores - row_max[:, :, None])
    row_sum = jnp.sum(weights, axis=2)
    blended = jnp.einsum(
        "hqk,khd->hqd", weights.astype(jnp.bfloat16), all_values, preferred_element_type=jnp.float32
    )
    log_total = row_max + jnp.log(row_sum)
    attended = (
        (blended / row_sum[:, :, None]).transpose(1, 0, 2).reshape(rows, inner).astype(jnp.bfloat16)
    )
    student = tokens.astype(jnp.float32) + jnp.dot(
        attended, w_out, preferred_element_type=jnp.float32
    )
    token_loss, grad_y = align_terms(student, target)
    grad_b = grad_y.astype(jnp.bfloat16)
    grad_wout = jnp.dot(exchange_order(attended).T, grad_b, preferred_element_type=jnp.float32)
    grad_heads = (
        jnp.dot(grad_b, w_out.T, preferred_element_type=jnp.float32)
        .astype(jnp.bfloat16)
        .reshape(rows, heads, HEAD_DIM)
    )
    row_dot = jnp.sum(
        grad_heads.astype(jnp.float32)
        * attended.reshape(rows, heads, HEAD_DIM).astype(jnp.float32),
        axis=2,
    ).T
    prob_full = jnp.exp(scores - log_total[:, :, None])
    d_value = jnp.einsum(
        "hqk,qhd->khd", prob_full.astype(jnp.bfloat16), grad_heads, preferred_element_type=jnp.float32
    )
    d_prob = jnp.einsum(
        "qhd,khd->hqk", grad_heads, all_values, preferred_element_type=jnp.float32
    )
    d_score = (prob_full * (d_prob - row_dot[:, :, None])).astype(jnp.bfloat16)
    d_query = 0.125 * jnp.einsum(
        "hqk,khd->qhd", d_score, all_keys, preferred_element_type=jnp.float32
    )
    d_key = 0.125 * jnp.einsum("hqk,qhd->khd", d_score, queries, preferred_element_type=jnp.float32)
    d_pairs = jnp.stack([d_key, d_value], axis=2).reshape(shards, rows, 2 * inner)
    accum = d_pairs[0]
    for step in range(1, shards):
        accum = accum + shifted(d_pairs[step].astype(jnp.bfloat16), "seq", -step).astype(jnp.float32)
    d_proj = jnp.concatenate([d_query.reshape(rows, inner), accum], axis=1).astype(jnp.bfloat16)
    grad_wqkv = jnp.dot(exchange_order(hidden).T, d_proj, preferred_element_type=jnp.float32)
    d_hidden = jnp.dot(d_proj, w_qkv.T, preferred_element_type=jnp.float32)
    grad_ln = jnp.sum(d_hidden * normed, axis=0)
    loss_part = jnp.sum(token_loss)
    small = jnp.concatenate([grad_ln, loss_part.reshape(1)])
    grad_qkv, grad_out, small = halving_scatter(grad_wqkv, grad_wout, small)
    count_all = shards * lax.axis_size("clip") * TOK_DEV
    return (small[-1] / count_all, grad_qkv.reshape(-1), grad_out.reshape(-1), small[:-1])


def solution(mesh):
    placed = (P("clip", "seq", None), P("clip", "seq", None), P("clip", "seq"), P(), P(), P())
    return jax.shard_map(
        per_device,
        mesh=mesh,
        in_specs=placed,
        out_specs=(P(), P(("seq", "clip")), P(("seq", "clip")), P()),
        check_vma=False,
    )
```

```python
import jax
import jax.numpy as jnp
from jax import lax
from jax.sharding import PartitionSpec as P

HEAD_DIM = 64
TOK_DEV = 128


def shifted(value, axis, steps):
    count = lax.axis_size(axis)
    pairs = [(source, (source + steps) % count) for source in range(count)]
    return lax.ppermute(value, axis, pairs)


def layer_norm(tokens, ln_gain):
    values = tokens.astype(jnp.float32)
    center = values - jnp.mean(values, axis=-1, keepdims=True)
    spread = jnp.mean(center * center, axis=-1, keepdims=True)
    normed = center * lax.rsqrt(spread + 1e-05)
    return (normed, (normed * ln_gain).astype(jnp.bfloat16))


def align_terms(student, target):
    target_f = target.astype(jnp.float32)
    inv_y = lax.rsqrt(jnp.sum(student * student, axis=-1, keepdims=True) + 1e-06)
    inv_t = lax.rsqrt(jnp.sum(target_f * target_f, axis=-1, keepdims=True) + 1e-06)
    differ = student * inv_y - target_f * inv_t
    token_loss = jnp.sum(differ * differ, axis=-1)
    slopes = 2.0 * differ
    grad_y = inv_y * slopes - student * (inv_y * inv_y * inv_y) * jnp.sum(
        slopes * student, axis=-1, keepdims=True
    )
    return (token_loss, grad_y)


def key_mask(key_count, rows, heads):
    slot_idx = jnp.arange(rows, dtype=jnp.int32)
    halves = slot_idx[None, :] < key_count[:, None]
    return jnp.repeat(halves, heads // 2, axis=0)


def head_scores(queries, pair_rows, key_count):
    rows = pair_rows.shape[0]
    heads = queries.shape[1]
    split_kv = pair_rows.reshape(rows, heads, 2, HEAD_DIM)
    scores = (
        jnp.einsum("qhd,khd->hqk", queries, split_kv[:, :, 0], preferred_element_type=jnp.float32)
        * 0.125
    )
    mask_rows = key_mask(key_count, rows, heads)
    return (jnp.where(mask_rows[:, None, :], scores, -1e30), split_kv)


def absorb(state, queries, pair_rows, key_count):
    row_max, row_sum, blended = state
    scores, split_kv = head_scores(queries, pair_rows, key_count)
    new_max = jnp.maximum(row_max, jnp.max(scores, axis=2))
    rescale = jnp.exp(row_max - new_max)
    weights = jnp.exp(scores - new_max[:, :, None])
    row_sum = row_sum * rescale + jnp.sum(weights, axis=2)
    blended = blended * rescale[:, :, None] + jnp.einsum(
        "hqk,khd->hqd",
        weights.astype(jnp.bfloat16),
        split_kv[:, :, 1],
        preferred_element_type=jnp.float32,
    )
    return (new_max, row_sum, blended)


def contribution(queries, grad_heads, log_total, row_dot, pair_rows, key_count):
    scores, split_kv = head_scores(queries, pair_rows, key_count)
    prob_full = jnp.exp(scores - log_total[:, :, None])
    d_value = jnp.einsum(
        "hqk,qhd->khd",
        prob_full.astype(jnp.bfloat16),
        grad_heads,
        preferred_element_type=jnp.float32,
    )
    d_prob = jnp.einsum(
        "qhd,khd->hqk", grad_heads, split_kv[:, :, 1], preferred_element_type=jnp.float32
    )
    d_score = (prob_full * (d_prob - row_dot[:, :, None])).astype(jnp.bfloat16)
    d_query = 0.125 * jnp.einsum(
        "hqk,khd->qhd", d_score, split_kv[:, :, 0], preferred_element_type=jnp.float32
    )
    d_key = 0.125 * jnp.einsum("hqk,qhd->khd", d_score, queries, preferred_element_type=jnp.float32)
    rows = pair_rows.shape[0]
    return (d_query, jnp.stack([d_key, d_value], axis=2).reshape(rows, -1))


def move_keys(pair_rows):
    moved = shifted(pair_rows, "seq", 1)
    return moved


def move_grads(accum):
    moved = shifted(accum.astype(jnp.bfloat16), "seq", 1).astype(accum.dtype)
    return moved


def exchange_bits():
    seq_bits = lax.axis_size("seq").bit_length() - 1
    clip_bits = lax.axis_size("clip").bit_length() - 1
    assert (1 << seq_bits) == lax.axis_size("seq")
    assert (1 << clip_bits) == lax.axis_size("clip")
    return seq_bits, clip_bits


def exchange_order(values):
    seq_bits, clip_bits = exchange_bits()
    total = seq_bits + clip_bits
    lead = values.shape[0]
    split = values.reshape([lead] + [2] * total + [-1])
    seq_dims = [1 + seq_bits - 1 - bit for bit in range(seq_bits)]
    clip_dims = [1 + seq_bits + clip_bits - 1 - bit for bit in range(clip_bits)]
    perm = [0] + seq_dims + clip_dims + [total + 1]
    return split.transpose(perm).reshape(values.shape)


def halving_scatter(grad_wqkv, grad_wout, small):
    seq_bits, clip_bits = exchange_bits()
    total = seq_bits + clip_bits
    first = grad_wqkv.reshape([2] * total + [-1, grad_wqkv.shape[1]])
    second = grad_wout.reshape([2] * total + [-1, grad_wout.shape[1]])
    order = [("seq", bit) for bit in range(seq_bits)] + [("clip", bit) for bit in range(clip_bits)]
    for axis, bit in order:
        mine = (lax.axis_index(axis) >> bit) & 1
        count = lax.axis_size(axis)
        pairs = [(src, src ^ (1 << bit)) for src in range(count)]
        keep_a = lax.dynamic_index_in_dim(first, mine, axis=0, keepdims=False)
        give_a = lax.dynamic_index_in_dim(first, 1 - mine, axis=0, keepdims=False)
        keep_b = lax.dynamic_index_in_dim(second, mine, axis=0, keepdims=False)
        give_b = lax.dynamic_index_in_dim(second, 1 - mine, axis=0, keepdims=False)
        got_a, got_b, got_s = lax.ppermute(
            (give_a.astype(jnp.bfloat16), give_b.astype(jnp.bfloat16), small), axis, pairs
        )
        first = keep_a + got_a.astype(jnp.float32)
        second = keep_b + got_b.astype(jnp.float32)
        small = small + got_s
    return (first, second, small)


def per_device(raw_tokens, teacher, keep_rows, w_qkv, w_out, ln_gain):
    shards = lax.axis_size("seq")
    my_index = lax.axis_index("seq")
    row_ids = keep_rows[0]
    list_slots = row_ids.shape[0]
    is_kept = row_ids >= 0
    kept_count = jnp.sum(is_kept.astype(jnp.int32))
    safe_ids = jnp.maximum(row_ids, 0)
    kept_tokens = jnp.where(is_kept[:, None], raw_tokens[0][safe_ids], jnp.zeros((), jnp.bfloat16))
    kept_target = jnp.where(is_kept[:, None], teacher[0][safe_ids], jnp.zeros((), jnp.bfloat16))
    count_table = lax.all_gather(kept_count.reshape(1), "seq", axis=0, tiled=True)
    shard_ids = jnp.arange(shards, dtype=jnp.int32)
    per_peer = -(-list_slots // shards)
    starts = jnp.cumsum(count_table) - count_table
    before = jnp.sum(jnp.where(shard_ids < my_index, count_table, 0))
    slot_ids = jnp.arange(per_peer, dtype=jnp.int32)
    pick = (shard_ids[:, None] - before) % shards + slot_ids[None, :] * shards
    pick_ok = pick < kept_count
    pick_safe = jnp.minimum(pick, list_slots - 1)
    send_tokens = jnp.where(
        pick_ok[:, :, None], kept_tokens[pick_safe], jnp.zeros((), jnp.bfloat16)
    )
    send_target = jnp.where(
        pick_ok[:, :, None], kept_target[pick_safe], jnp.zeros((), jnp.bfloat16)
    )
    got_tokens, got_target = (
        lax.all_to_all(send_tokens, "seq", split_axis=0, concat_axis=0, tiled=True),
        lax.all_to_all(send_target, "seq", split_axis=0, concat_axis=0, tiled=True),
    )
    from_pick = (my_index - starts[:, None]) % shards + slot_ids[None, :] * shards
    from_ok = from_pick < count_table[:, None]
    place = jnp.where(from_ok, (starts[:, None] + from_pick) // shards, TOK_DEV).reshape(-1)
    width = got_tokens.shape[2]
    tokens = (
        jnp.zeros((TOK_DEV, width), jnp.bfloat16)
        .at[place]
        .set(got_tokens.reshape(-1, width), mode="drop")
    )
    target = (
        jnp.zeros((TOK_DEV, width), jnp.bfloat16)
        .at[place]
        .set(got_target.reshape(-1, width), mode="drop")
    )
    rows = tokens.shape[0]
    inner = w_out.shape[0]
    heads = inner // HEAD_DIM
    normed, hidden = layer_norm(tokens, ln_gain)
    queries = (
        jnp.dot(hidden, w_qkv[:, :inner], preferred_element_type=jnp.float32)
        .astype(jnp.bfloat16)
        .reshape(rows, heads, HEAD_DIM)
        .transpose(1, 0, 2)
    )
    pair_cols = jnp.dot(w_qkv[:, inner:].T, hidden.T, preferred_element_type=jnp.float32).astype(
        jnp.bfloat16
    )
    gathered = jnp.stack([pair_cols] + [shifted(pair_cols, "seq", step) for step in range(1, shards)])
    split_kv = gathered.reshape(shards, heads, 2, HEAD_DIM, rows).transpose(1, 2, 3, 0, 4)
    split_kv = split_kv.reshape(heads, 2, HEAD_DIM, shards * rows)
    keys_t = split_kv[:, 0]
    values_t = split_kv[:, 1]
    scores = jnp.einsum("hqd,hdk->hqk", queries, keys_t, preferred_element_type=jnp.float32) * 0.125
    row_max = jnp.max(scores, axis=2)
    weights = jnp.exp(scores - row_max[:, :, None])
    row_sum = jnp.sum(weights, axis=2)
    blended = jnp.einsum(
        "hqk,hdk->hqd", weights.astype(jnp.bfloat16), values_t, preferred_element_type=jnp.float32
    )
    log_total = row_max + jnp.log(row_sum)
    attended = (
        (blended / row_sum[:, :, None]).transpose(1, 0, 2).reshape(rows, inner).astype(jnp.bfloat16)
    )
    student = tokens.astype(jnp.float32) + jnp.dot(
        attended, w_out, preferred_element_type=jnp.float32
    )
    token_loss, grad_y = align_terms(student, target)
    grad_b = grad_y.astype(jnp.bfloat16)
    grad_wout = jnp.dot(exchange_order(attended).T, grad_b, preferred_element_type=jnp.float32)
    grad_heads = (
        jnp.dot(grad_b, w_out.T, preferred_element_type=jnp.float32)
        .astype(jnp.bfloat16)
        .reshape(rows, heads, HEAD_DIM)
        .transpose(1, 0, 2)
    )
    row_dot = jnp.sum(
        grad_heads.astype(jnp.float32)
        * attended.reshape(rows, heads, HEAD_DIM).transpose(1, 0, 2).astype(jnp.float32),
        axis=2,
    )
    prob_full = jnp.exp(scores - log_total[:, :, None])
    d_value_t = jnp.einsum(
        "hqd,hqk->hdk", grad_heads, prob_full.astype(jnp.bfloat16), preferred_element_type=jnp.float32
    )
    d_prob = jnp.einsum("hqd,hdk->hqk", grad_heads, values_t, preferred_element_type=jnp.float32)
    d_score = (prob_full * (d_prob - row_dot[:, :, None])).astype(jnp.bfloat16)
    d_query = 0.125 * jnp.einsum("hqk,hdk->qhd", d_score, keys_t, preferred_element_type=jnp.float32)
    d_key_t = 0.125 * jnp.einsum("hqd,hqk->hdk", queries, d_score, preferred_element_type=jnp.float32)
    d_pairs = jnp.stack([d_key_t, d_value_t], axis=1).reshape(heads, 2, HEAD_DIM, shards, rows)
    d_pairs = d_pairs.transpose(3, 0, 1, 2, 4).reshape(shards, 2 * inner, rows)
    accum = d_pairs[0]
    for step in range(1, shards):
        accum = accum + shifted(d_pairs[step].astype(jnp.bfloat16), "seq", -step).astype(jnp.float32)
    d_proj = jnp.concatenate([d_query.reshape(rows, inner), accum.T], axis=1).astype(jnp.bfloat16)
    grad_wqkv = jnp.dot(exchange_order(hidden).T, d_proj, preferred_element_type=jnp.float32)
    d_hidden = jnp.dot(d_proj, w_qkv.T, preferred_element_type=jnp.float32)
    grad_ln = jnp.sum(d_hidden * normed, axis=0)
    loss_part = jnp.sum(token_loss)
    small = jnp.concatenate([grad_ln, loss_part.reshape(1)])
    grad_qkv, grad_out, small = halving_scatter(grad_wqkv, grad_wout, small)
    count_all = shards * lax.axis_size("clip") * TOK_DEV
    return (small[-1] / count_all, grad_qkv.reshape(-1), grad_out.reshape(-1), small[:-1])


def solution(mesh):
    placed = (P("clip", "seq", None), P("clip", "seq", None), P("clip", "seq"), P(), P(), P())
    return jax.shard_map(
        per_device,
        mesh=mesh,
        in_specs=placed,
        out_specs=(P(), P(("seq", "clip")), P(("seq", "clip")), P()),
        check_vma=False,
    )
```

```python
import jax
import jax.numpy as jnp
from jax import lax
from jax.sharding import PartitionSpec as P

HEAD_DIM = 64
TOK_DEV = 128


def shifted(value, axis, steps):
    count = lax.axis_size(axis)
    pairs = [(source, (source + steps) % count) for source in range(count)]
    return lax.ppermute(value, axis, pairs)


def layer_norm(tokens, ln_gain):
    values = tokens.astype(jnp.float32)
    center = values - jnp.mean(values, axis=-1, keepdims=True)
    spread = jnp.mean(center * center, axis=-1, keepdims=True)
    normed = center * lax.rsqrt(spread + 1e-05)
    return (normed, (normed * ln_gain).astype(jnp.bfloat16))


def align_terms(student, target):
    target_f = target.astype(jnp.float32)
    inv_y = lax.rsqrt(jnp.sum(student * student, axis=-1, keepdims=True) + 1e-06)
    inv_t = lax.rsqrt(jnp.sum(target_f * target_f, axis=-1, keepdims=True) + 1e-06)
    differ = student * inv_y - target_f * inv_t
    token_loss = jnp.sum(differ * differ, axis=-1)
    slopes = 2.0 * differ
    grad_y = inv_y * slopes - student * (inv_y * inv_y * inv_y) * jnp.sum(
        slopes * student, axis=-1, keepdims=True
    )
    return (token_loss, grad_y)


def key_mask(key_count, rows, heads):
    slot_idx = jnp.arange(rows, dtype=jnp.int32)
    halves = slot_idx[None, :] < key_count[:, None]
    return jnp.repeat(halves, heads // 2, axis=0)


def head_scores(queries, pair_rows, key_count):
    rows = pair_rows.shape[0]
    heads = queries.shape[1]
    split_kv = pair_rows.reshape(rows, heads, 2, HEAD_DIM)
    scores = (
        jnp.einsum("qhd,khd->hqk", queries, split_kv[:, :, 0], preferred_element_type=jnp.float32)
        * 0.125
    )
    mask_rows = key_mask(key_count, rows, heads)
    return (jnp.where(mask_rows[:, None, :], scores, -1e30), split_kv)


def absorb(state, queries, pair_rows, key_count):
    row_max, row_sum, blended = state
    scores, split_kv = head_scores(queries, pair_rows, key_count)
    new_max = jnp.maximum(row_max, jnp.max(scores, axis=2))
    rescale = jnp.exp(row_max - new_max)
    weights = jnp.exp(scores - new_max[:, :, None])
    row_sum = row_sum * rescale + jnp.sum(weights, axis=2)
    blended = blended * rescale[:, :, None] + jnp.einsum(
        "hqk,khd->hqd",
        weights.astype(jnp.bfloat16),
        split_kv[:, :, 1],
        preferred_element_type=jnp.float32,
    )
    return (new_max, row_sum, blended)


def contribution(queries, grad_heads, log_total, row_dot, pair_rows, key_count):
    scores, split_kv = head_scores(queries, pair_rows, key_count)
    prob_full = jnp.exp(scores - log_total[:, :, None])
    d_value = jnp.einsum(
        "hqk,qhd->khd",
        prob_full.astype(jnp.bfloat16),
        grad_heads,
        preferred_element_type=jnp.float32,
    )
    d_prob = jnp.einsum(
        "qhd,khd->hqk", grad_heads, split_kv[:, :, 1], preferred_element_type=jnp.float32
    )
    d_score = (prob_full * (d_prob - row_dot[:, :, None])).astype(jnp.bfloat16)
    d_query = 0.125 * jnp.einsum(
        "hqk,khd->qhd", d_score, split_kv[:, :, 0], preferred_element_type=jnp.float32
    )
    d_key = 0.125 * jnp.einsum("hqk,qhd->khd", d_score, queries, preferred_element_type=jnp.float32)
    rows = pair_rows.shape[0]
    return (d_query, jnp.stack([d_key, d_value], axis=2).reshape(rows, -1))


def move_keys(pair_rows):
    moved = shifted(pair_rows, "seq", 1)
    return moved


def move_grads(accum):
    moved = shifted(accum.astype(jnp.bfloat16), "seq", 1).astype(accum.dtype)
    return moved


def exchange_bits():
    seq_bits = lax.axis_size("seq").bit_length() - 1
    clip_bits = lax.axis_size("clip").bit_length() - 1
    assert (1 << seq_bits) == lax.axis_size("seq")
    assert (1 << clip_bits) == lax.axis_size("clip")
    return seq_bits, clip_bits


def exchange_order(values):
    seq_bits, clip_bits = exchange_bits()
    total = seq_bits + clip_bits
    lead = values.shape[0]
    split = values.reshape([lead] + [2] * total + [-1])
    seq_dims = [1 + seq_bits - 1 - bit for bit in range(seq_bits)]
    clip_dims = [1 + seq_bits + clip_bits - 1 - bit for bit in range(clip_bits)]
    perm = [0] + seq_dims + clip_dims + [total + 1]
    return split.transpose(perm).reshape(values.shape)


def halving_scatter(grad, small=None):
    seq_bits, clip_bits = exchange_bits()
    total = seq_bits + clip_bits
    data = grad.reshape([2] * total + [-1, grad.shape[1]])
    order_a = list(range(seq_bits))
    order_b = [0] + list(range(seq_bits - 1, 0, -1))
    core_bit = lax.axis_index("seq") & 1
    left_a = list(range(seq_bits))
    left_b = list(range(seq_bits))
    for step in range(seq_bits):
        bit_a, bit_b = order_a[step], order_b[step]
        dim_a, dim_b = left_a.index(bit_a), left_b.index(bit_b)
        me = lax.axis_index("seq")
        mine_a = (me >> bit_a) & 1
        mine_b = (me >> bit_b) & 1
        pairs = []
        for src in range(lax.axis_size("seq")):
            bit = bit_a if (src & 1) == 0 else bit_b
            pairs.append((src, src ^ (1 << bit)))
        keep = jnp.where(
            core_bit == 0,
            lax.dynamic_index_in_dim(data, mine_a, axis=dim_a, keepdims=False),
            lax.dynamic_index_in_dim(data, mine_b, axis=dim_b, keepdims=False),
        )
        give = jnp.where(
            core_bit == 0,
            lax.dynamic_index_in_dim(data, 1 - mine_a, axis=dim_a, keepdims=False),
            lax.dynamic_index_in_dim(data, 1 - mine_b, axis=dim_b, keepdims=False),
        )
        left_a.pop(dim_a)
        left_b.pop(dim_b)
        if small is None:
            got = lax.ppermute(give.astype(jnp.bfloat16), "seq", pairs)
        else:
            got, got_small = lax.ppermute((give.astype(jnp.bfloat16), small), "seq", pairs)
            small = small + got_small
        data = keep + got.astype(jnp.float32)
    for bit in range(clip_bits):
        mine = (lax.axis_index("clip") >> bit) & 1
        pairs = [(src, src ^ (1 << bit)) for src in range(lax.axis_size("clip"))]
        keep = lax.dynamic_index_in_dim(data, mine, axis=0, keepdims=False)
        give = lax.dynamic_index_in_dim(data, 1 - mine, axis=0, keepdims=False)
        if small is None:
            got = lax.ppermute(give.astype(jnp.bfloat16), "clip", pairs)
        else:
            got, got_small = lax.ppermute((give.astype(jnp.bfloat16), small), "clip", pairs)
            small = small + got_small
        data = keep + got.astype(jnp.float32)
    return data, small


def per_device(raw_tokens, teacher, keep_rows, w_qkv, w_out, ln_gain):
    shards = lax.axis_size("seq")
    my_index = lax.axis_index("seq")
    row_ids = keep_rows[0]
    list_slots = row_ids.shape[0]
    is_kept = row_ids >= 0
    kept_count = jnp.sum(is_kept.astype(jnp.int32))
    safe_ids = jnp.maximum(row_ids, 0)
    kept_tokens = jnp.where(is_kept[:, None], raw_tokens[0][safe_ids], jnp.zeros((), jnp.bfloat16))
    kept_target = jnp.where(is_kept[:, None], teacher[0][safe_ids], jnp.zeros((), jnp.bfloat16))
    count_table = lax.all_gather(kept_count.reshape(1), "seq", axis=0, tiled=True)
    shard_ids = jnp.arange(shards, dtype=jnp.int32)
    per_peer = -(-list_slots // shards)
    starts = jnp.cumsum(count_table) - count_table
    before = jnp.sum(jnp.where(shard_ids < my_index, count_table, 0))
    slot_ids = jnp.arange(per_peer, dtype=jnp.int32)
    pick = (shard_ids[:, None] - before) % shards + slot_ids[None, :] * shards
    pick_ok = pick < kept_count
    pick_safe = jnp.minimum(pick, list_slots - 1)
    send_tokens = jnp.where(
        pick_ok[:, :, None], kept_tokens[pick_safe], jnp.zeros((), jnp.bfloat16)
    )
    send_target = jnp.where(
        pick_ok[:, :, None], kept_target[pick_safe], jnp.zeros((), jnp.bfloat16)
    )
    got_tokens, got_target = (
        lax.all_to_all(send_tokens, "seq", split_axis=0, concat_axis=0, tiled=True),
        lax.all_to_all(send_target, "seq", split_axis=0, concat_axis=0, tiled=True),
    )
    from_pick = (my_index - starts[:, None]) % shards + slot_ids[None, :] * shards
    from_ok = from_pick < count_table[:, None]
    place = jnp.where(from_ok, (starts[:, None] + from_pick) // shards, TOK_DEV).reshape(-1)
    width = got_tokens.shape[2]
    tokens = (
        jnp.zeros((TOK_DEV, width), jnp.bfloat16)
        .at[place]
        .set(got_tokens.reshape(-1, width), mode="drop")
    )
    target = (
        jnp.zeros((TOK_DEV, width), jnp.bfloat16)
        .at[place]
        .set(got_target.reshape(-1, width), mode="drop")
    )
    rows = tokens.shape[0]
    inner = w_out.shape[0]
    heads = inner // HEAD_DIM
    normed, hidden = layer_norm(tokens, ln_gain)
    queries = (
        jnp.dot(hidden, w_qkv[:, :inner], preferred_element_type=jnp.float32)
        .astype(jnp.bfloat16)
        .reshape(rows, heads, HEAD_DIM)
        .transpose(1, 0, 2)
    )
    pair_cols = jnp.dot(w_qkv[:, inner:].T, hidden.T, preferred_element_type=jnp.float32).astype(
        jnp.bfloat16
    )
    gathered = jnp.stack([pair_cols] + [shifted(pair_cols, "seq", step) for step in range(1, shards)])
    split_kv = gathered.reshape(shards, heads, 2, HEAD_DIM, rows).transpose(1, 2, 3, 0, 4)
    split_kv = split_kv.reshape(heads, 2, HEAD_DIM, shards * rows)
    keys_t = split_kv[:, 0]
    values_t = split_kv[:, 1]
    scores = jnp.einsum("hqd,hdk->hqk", queries, keys_t, preferred_element_type=jnp.float32) * 0.125
    row_max = jnp.max(scores, axis=2)
    weights = jnp.exp(scores - row_max[:, :, None])
    row_sum = jnp.sum(weights, axis=2)
    blended = jnp.einsum(
        "hqk,hdk->hqd", weights.astype(jnp.bfloat16), values_t, preferred_element_type=jnp.float32
    )
    log_total = row_max + jnp.log(row_sum)
    attended = (
        (blended / row_sum[:, :, None]).transpose(1, 0, 2).reshape(rows, inner).astype(jnp.bfloat16)
    )
    student = tokens.astype(jnp.float32) + jnp.dot(
        attended, w_out, preferred_element_type=jnp.float32
    )
    token_loss, grad_y = align_terms(student, target)
    grad_b = grad_y.astype(jnp.bfloat16)
    grad_wout = jnp.dot(exchange_order(attended).T, grad_b, preferred_element_type=jnp.float32)
    grad_heads = (
        jnp.dot(grad_b, w_out.T, preferred_element_type=jnp.float32)
        .astype(jnp.bfloat16)
        .reshape(rows, heads, HEAD_DIM)
        .transpose(1, 0, 2)
    )
    row_dot = jnp.sum(
        grad_heads.astype(jnp.float32)
        * attended.reshape(rows, heads, HEAD_DIM).transpose(1, 0, 2).astype(jnp.float32),
        axis=2,
    )
    prob_full = jnp.exp(scores - log_total[:, :, None])
    d_value_t = jnp.einsum(
        "hqd,hqk->hdk", grad_heads, prob_full.astype(jnp.bfloat16), preferred_element_type=jnp.float32
    )
    d_prob = jnp.einsum("hqd,hdk->hqk", grad_heads, values_t, preferred_element_type=jnp.float32)
    d_score = (prob_full * (d_prob - row_dot[:, :, None])).astype(jnp.bfloat16)
    d_query = 0.125 * jnp.einsum("hqk,hdk->qhd", d_score, keys_t, preferred_element_type=jnp.float32)
    d_key_t = 0.125 * jnp.einsum("hqd,hqk->hdk", queries, d_score, preferred_element_type=jnp.float32)
    d_pairs = jnp.stack([d_key_t, d_value_t], axis=1).reshape(heads, 2, HEAD_DIM, shards, rows)
    d_pairs = d_pairs.transpose(3, 0, 1, 2, 4).reshape(shards, 2 * inner, rows)
    accum = d_pairs[0]
    for step in range(1, shards):
        accum = accum + shifted(d_pairs[step].astype(jnp.bfloat16), "seq", -step).astype(jnp.float32)
    d_proj = jnp.concatenate([d_query.reshape(rows, inner), accum.T], axis=1).astype(jnp.bfloat16)
    grad_wqkv = jnp.dot(exchange_order(hidden).T, d_proj, preferred_element_type=jnp.float32)
    d_hidden = jnp.dot(d_proj, w_qkv.T, preferred_element_type=jnp.float32)
    grad_ln = jnp.sum(d_hidden * normed, axis=0)
    loss_part = jnp.sum(token_loss)
    small = jnp.concatenate([grad_ln, loss_part.reshape(1)])
    grad_out, unused = halving_scatter(grad_wout)
    grad_qkv, small = halving_scatter(grad_wqkv, small)
    count_all = shards * lax.axis_size("clip") * TOK_DEV
    return (small[-1] / count_all, grad_qkv.reshape(-1), grad_out.reshape(-1), small[:-1])


def solution(mesh):
    placed = (P("clip", "seq", None), P("clip", "seq", None), P("clip", "seq"), P(), P(), P())
    return jax.shard_map(
        per_device,
        mesh=mesh,
        in_specs=placed,
        out_specs=(P(), P(("seq", "clip")), P(("seq", "clip")), P()),
        check_vma=False,
    )
```

```python
import jax
import jax.numpy as jnp
from jax import lax
from jax.sharding import PartitionSpec as P

HEAD_DIM = 64
TOK_DEV = 128


def shifted(value, axis, steps):
    count = lax.axis_size(axis)
    pairs = [(source, (source + steps) % count) for source in range(count)]
    return lax.ppermute(value, axis, pairs)


def layer_norm(tokens, ln_gain):
    values = tokens.astype(jnp.float32)
    center = values - jnp.mean(values, axis=-1, keepdims=True)
    spread = jnp.mean(center * center, axis=-1, keepdims=True)
    normed = center * lax.rsqrt(spread + 1e-05)
    return (normed, (normed * ln_gain).astype(jnp.bfloat16))


def align_terms(student, target):
    target_f = target.astype(jnp.float32)
    inv_y = lax.rsqrt(jnp.sum(student * student, axis=-1, keepdims=True) + 1e-06)
    inv_t = lax.rsqrt(jnp.sum(target_f * target_f, axis=-1, keepdims=True) + 1e-06)
    differ = student * inv_y - target_f * inv_t
    token_loss = jnp.sum(differ * differ, axis=-1)
    slopes = 2.0 * differ
    grad_y = inv_y * slopes - student * (inv_y * inv_y * inv_y) * jnp.sum(
        slopes * student, axis=-1, keepdims=True
    )
    return (token_loss, grad_y)


def key_mask(key_count, rows, heads):
    slot_idx = jnp.arange(rows, dtype=jnp.int32)
    halves = slot_idx[None, :] < key_count[:, None]
    return jnp.repeat(halves, heads // 2, axis=0)


def head_scores(queries, pair_rows, key_count):
    rows = pair_rows.shape[0]
    heads = queries.shape[1]
    split_kv = pair_rows.reshape(rows, heads, 2, HEAD_DIM)
    scores = (
        jnp.einsum("qhd,khd->hqk", queries, split_kv[:, :, 0], preferred_element_type=jnp.float32)
        * 0.125
    )
    mask_rows = key_mask(key_count, rows, heads)
    return (jnp.where(mask_rows[:, None, :], scores, -1e30), split_kv)


def absorb(state, queries, pair_rows, key_count):
    row_max, row_sum, blended = state
    scores, split_kv = head_scores(queries, pair_rows, key_count)
    new_max = jnp.maximum(row_max, jnp.max(scores, axis=2))
    rescale = jnp.exp(row_max - new_max)
    weights = jnp.exp(scores - new_max[:, :, None])
    row_sum = row_sum * rescale + jnp.sum(weights, axis=2)
    blended = blended * rescale[:, :, None] + jnp.einsum(
        "hqk,khd->hqd",
        weights.astype(jnp.bfloat16),
        split_kv[:, :, 1],
        preferred_element_type=jnp.float32,
    )
    return (new_max, row_sum, blended)


def contribution(queries, grad_heads, log_total, row_dot, pair_rows, key_count):
    scores, split_kv = head_scores(queries, pair_rows, key_count)
    prob_full = jnp.exp(scores - log_total[:, :, None])
    d_value = jnp.einsum(
        "hqk,qhd->khd",
        prob_full.astype(jnp.bfloat16),
        grad_heads,
        preferred_element_type=jnp.float32,
    )
    d_prob = jnp.einsum(
        "qhd,khd->hqk", grad_heads, split_kv[:, :, 1], preferred_element_type=jnp.float32
    )
    d_score = (prob_full * (d_prob - row_dot[:, :, None])).astype(jnp.bfloat16)
    d_query = 0.125 * jnp.einsum(
        "hqk,khd->qhd", d_score, split_kv[:, :, 0], preferred_element_type=jnp.float32
    )
    d_key = 0.125 * jnp.einsum("hqk,qhd->khd", d_score, queries, preferred_element_type=jnp.float32)
    rows = pair_rows.shape[0]
    return (d_query, jnp.stack([d_key, d_value], axis=2).reshape(rows, -1))


def move_keys(pair_rows):
    moved = shifted(pair_rows, "seq", 1)
    return moved


def move_grads(accum):
    moved = shifted(accum.astype(jnp.bfloat16), "seq", 1).astype(accum.dtype)
    return moved


def exchange_bits():
    seq_bits = lax.axis_size("seq").bit_length() - 1
    clip_bits = lax.axis_size("clip").bit_length() - 1
    assert (1 << seq_bits) == lax.axis_size("seq")
    assert (1 << clip_bits) == lax.axis_size("clip")
    return seq_bits, clip_bits


def exchange_order(values):
    seq_bits, clip_bits = exchange_bits()
    total = seq_bits + clip_bits
    lead = values.shape[0]
    split = values.reshape([lead] + [2] * total + [-1])
    seq_dims = [1 + seq_bits - 1 - bit for bit in range(seq_bits)]
    clip_dims = [1 + seq_bits + clip_bits - 1 - bit for bit in range(clip_bits)]
    perm = [0] + seq_dims + clip_dims + [total + 1]
    return split.transpose(perm).reshape(values.shape)


def halving_scatter(grad, small=None):
    seq_bits, clip_bits = exchange_bits()
    total = seq_bits + clip_bits
    data = grad.reshape([2] * total + [-1, grad.shape[1]])
    order_a = list(range(seq_bits))
    order_b = [0] + list(range(seq_bits - 1, 0, -1))
    core_bit = lax.axis_index("seq") & 1
    left_a = list(range(seq_bits))
    left_b = list(range(seq_bits))
    for step in range(seq_bits):
        bit_a, bit_b = order_a[step], order_b[step]
        dim_a, dim_b = left_a.index(bit_a), left_b.index(bit_b)
        me = lax.axis_index("seq")
        mine_a = (me >> bit_a) & 1
        mine_b = (me >> bit_b) & 1
        pairs = []
        for src in range(lax.axis_size("seq")):
            bit = bit_a if (src & 1) == 0 else bit_b
            pairs.append((src, src ^ (1 << bit)))
        keep = jnp.where(
            core_bit == 0,
            lax.dynamic_index_in_dim(data, mine_a, axis=dim_a, keepdims=False),
            lax.dynamic_index_in_dim(data, mine_b, axis=dim_b, keepdims=False),
        )
        give = jnp.where(
            core_bit == 0,
            lax.dynamic_index_in_dim(data, 1 - mine_a, axis=dim_a, keepdims=False),
            lax.dynamic_index_in_dim(data, 1 - mine_b, axis=dim_b, keepdims=False),
        )
        left_a.pop(dim_a)
        left_b.pop(dim_b)
        if small is None:
            got = lax.ppermute(give.astype(jnp.bfloat16), "seq", pairs)
        else:
            got, got_small = lax.ppermute((give.astype(jnp.bfloat16), small), "seq", pairs)
            small = small + got_small
        data = keep + got.astype(jnp.float32)
    for bit in range(clip_bits):
        mine = (lax.axis_index("clip") >> bit) & 1
        pairs = [(src, src ^ (1 << bit)) for src in range(lax.axis_size("clip"))]
        keep = lax.dynamic_index_in_dim(data, mine, axis=0, keepdims=False)
        give = lax.dynamic_index_in_dim(data, 1 - mine, axis=0, keepdims=False)
        if small is None:
            got = lax.ppermute(give.astype(jnp.bfloat16), "clip", pairs)
        else:
            got, got_small = lax.ppermute((give.astype(jnp.bfloat16), small), "clip", pairs)
            small = small + got_small
        data = keep + got.astype(jnp.float32)
    return data, small


def per_device(raw_tokens, teacher, keep_rows, w_qkv, w_out, ln_gain):
    shards = lax.axis_size("seq")
    my_index = lax.axis_index("seq")
    row_ids = keep_rows[0]
    list_slots = row_ids.shape[0]
    is_kept = row_ids >= 0
    kept_count = jnp.sum(is_kept.astype(jnp.int32))
    safe_ids = jnp.maximum(row_ids, 0)
    kept_tokens = jnp.where(is_kept[:, None], raw_tokens[0][safe_ids], jnp.zeros((), jnp.bfloat16))
    kept_target = jnp.where(is_kept[:, None], teacher[0][safe_ids], jnp.zeros((), jnp.bfloat16))
    count_table = lax.all_to_all(
        jnp.broadcast_to(kept_count.reshape(1, 1), (shards, 1)), "seq", 0, 0, tiled=True
    ).reshape(shards)
    shard_ids = jnp.arange(shards, dtype=jnp.int32)
    per_peer = -(-list_slots // shards)
    starts = jnp.cumsum(count_table) - count_table
    before = jnp.sum(jnp.where(shard_ids < my_index, count_table, 0))
    slot_ids = jnp.arange(per_peer, dtype=jnp.int32)
    pick = (shard_ids[:, None] - before) % shards + slot_ids[None, :] * shards
    pick_ok = pick < kept_count
    pick_safe = jnp.minimum(pick, list_slots - 1)
    send_tokens = jnp.where(
        pick_ok[:, :, None], kept_tokens[pick_safe], jnp.zeros((), jnp.bfloat16)
    )
    send_target = jnp.where(
        pick_ok[:, :, None], kept_target[pick_safe], jnp.zeros((), jnp.bfloat16)
    )
    got_tokens, got_target = (
        lax.all_to_all(send_tokens, "seq", split_axis=0, concat_axis=0, tiled=True),
        lax.all_to_all(send_target, "seq", split_axis=0, concat_axis=0, tiled=True),
    )
    from_pick = (my_index - starts[:, None]) % shards + slot_ids[None, :] * shards
    from_ok = from_pick < count_table[:, None]
    place = jnp.where(from_ok, (starts[:, None] + from_pick) // shards, TOK_DEV).reshape(-1)
    width = got_tokens.shape[2]
    tokens = (
        jnp.zeros((TOK_DEV, width), jnp.bfloat16)
        .at[place]
        .set(got_tokens.reshape(-1, width), mode="drop")
    )
    target = (
        jnp.zeros((TOK_DEV, width), jnp.bfloat16)
        .at[place]
        .set(got_target.reshape(-1, width), mode="drop")
    )
    rows = tokens.shape[0]
    inner = w_out.shape[0]
    heads = inner // HEAD_DIM
    normed, hidden = layer_norm(tokens, ln_gain)
    queries = (
        jnp.dot(hidden, w_qkv[:, :inner], preferred_element_type=jnp.float32)
        .astype(jnp.bfloat16)
        .reshape(rows, heads, HEAD_DIM)
        .transpose(1, 0, 2)
    )
    pair_cols = jnp.dot(w_qkv[:, inner:].T, hidden.T, preferred_element_type=jnp.float32).astype(
        jnp.bfloat16
    )
    gathered = lax.all_to_all(
        jnp.broadcast_to(pair_cols[None], (shards,) + pair_cols.shape), "seq", 0, 0, tiled=True
    )
    split_kv = gathered.reshape(shards, heads, 2, HEAD_DIM, rows).transpose(1, 2, 3, 0, 4)
    split_kv = split_kv.reshape(heads, 2, HEAD_DIM, shards * rows)
    keys_t = split_kv[:, 0]
    values_t = split_kv[:, 1]
    scores = jnp.einsum("hqd,hdk->hqk", queries, keys_t, preferred_element_type=jnp.float32) * 0.125
    row_max = jnp.max(scores, axis=2)
    weights = jnp.exp(scores - row_max[:, :, None])
    row_sum = jnp.sum(weights, axis=2)
    blended = jnp.einsum(
        "hqk,hdk->hqd", weights.astype(jnp.bfloat16), values_t, preferred_element_type=jnp.float32
    )
    log_total = row_max + jnp.log(row_sum)
    attended = (
        (blended / row_sum[:, :, None]).transpose(1, 0, 2).reshape(rows, inner).astype(jnp.bfloat16)
    )
    student = tokens.astype(jnp.float32) + jnp.dot(
        attended, w_out, preferred_element_type=jnp.float32
    )
    token_loss, grad_y = align_terms(student, target)
    grad_b = grad_y.astype(jnp.bfloat16)
    grad_wout = jnp.dot(exchange_order(attended).T, grad_b, preferred_element_type=jnp.float32)
    grad_heads = (
        jnp.dot(grad_b, w_out.T, preferred_element_type=jnp.float32)
        .astype(jnp.bfloat16)
        .reshape(rows, heads, HEAD_DIM)
        .transpose(1, 0, 2)
    )
    row_dot = jnp.sum(
        grad_heads.astype(jnp.float32)
        * attended.reshape(rows, heads, HEAD_DIM).transpose(1, 0, 2).astype(jnp.float32),
        axis=2,
    )
    prob_full = jnp.exp(scores - log_total[:, :, None])
    d_value_t = jnp.einsum(
        "hqd,hqk->hdk", grad_heads, prob_full.astype(jnp.bfloat16), preferred_element_type=jnp.float32
    )
    d_prob = jnp.einsum("hqd,hdk->hqk", grad_heads, values_t, preferred_element_type=jnp.float32)
    d_score = (prob_full * (d_prob - row_dot[:, :, None])).astype(jnp.bfloat16)
    d_query = 0.125 * jnp.einsum("hqk,hdk->qhd", d_score, keys_t, preferred_element_type=jnp.float32)
    d_key_t = 0.125 * jnp.einsum("hqd,hqk->hdk", queries, d_score, preferred_element_type=jnp.float32)
    d_pairs = jnp.stack([d_key_t, d_value_t], axis=1).reshape(heads, 2, HEAD_DIM, shards, rows)
    d_pairs = d_pairs.transpose(3, 0, 1, 2, 4).reshape(shards, 2 * inner, rows).astype(jnp.bfloat16)
    returned = lax.all_to_all(d_pairs, "seq", 0, 0, tiled=True)
    accum = jnp.sum(returned.astype(jnp.float32), axis=0)
    d_proj = jnp.concatenate([d_query.reshape(rows, inner), accum.T], axis=1).astype(jnp.bfloat16)
    grad_wqkv = jnp.dot(exchange_order(hidden).T, d_proj, preferred_element_type=jnp.float32)
    d_hidden = jnp.dot(d_proj, w_qkv.T, preferred_element_type=jnp.float32)
    grad_ln = jnp.sum(d_hidden * normed, axis=0)
    loss_part = jnp.sum(token_loss)
    small = jnp.concatenate([grad_ln, loss_part.reshape(1)])
    grad_out, unused = halving_scatter(grad_wout)
    grad_qkv, small = halving_scatter(grad_wqkv, small)
    count_all = shards * lax.axis_size("clip") * TOK_DEV
    return (small[-1] / count_all, grad_qkv.reshape(-1), grad_out.reshape(-1), small[:-1])


def solution(mesh):
    placed = (P("clip", "seq", None), P("clip", "seq", None), P("clip", "seq"), P(), P(), P())
    return jax.shard_map(
        per_device,
        mesh=mesh,
        in_specs=placed,
        out_specs=(P(), P(("seq", "clip")), P(("seq", "clip")), P()),
        check_vma=False,
    )
```

```python
import jax
import jax.numpy as jnp
from jax import lax
from jax.sharding import PartitionSpec as P

HEAD_DIM = 64
TOK_DEV = 128


def shifted(value, axis, steps):
    count = lax.axis_size(axis)
    pairs = [(source, (source + steps) % count) for source in range(count)]
    return lax.ppermute(value, axis, pairs)


def layer_norm(tokens, ln_gain):
    values = tokens.astype(jnp.float32)
    center = values - jnp.mean(values, axis=-1, keepdims=True)
    spread = jnp.mean(center * center, axis=-1, keepdims=True)
    normed = center * lax.rsqrt(spread + 1e-05)
    return (normed, (normed * ln_gain).astype(jnp.bfloat16))


def align_terms(student, target):
    target_f = target.astype(jnp.float32)
    inv_y = lax.rsqrt(jnp.sum(student * student, axis=-1, keepdims=True) + 1e-06)
    inv_t = lax.rsqrt(jnp.sum(target_f * target_f, axis=-1, keepdims=True) + 1e-06)
    differ = student * inv_y - target_f * inv_t
    token_loss = jnp.sum(differ * differ, axis=-1)
    slopes = 2.0 * differ
    grad_y = inv_y * slopes - student * (inv_y * inv_y * inv_y) * jnp.sum(
        slopes * student, axis=-1, keepdims=True
    )
    return (token_loss, grad_y)


def key_mask(key_count, rows, heads):
    slot_idx = jnp.arange(rows, dtype=jnp.int32)
    halves = slot_idx[None, :] < key_count[:, None]
    return jnp.repeat(halves, heads // 2, axis=0)


def head_scores(queries, pair_rows, key_count):
    rows = pair_rows.shape[0]
    heads = queries.shape[1]
    split_kv = pair_rows.reshape(rows, heads, 2, HEAD_DIM)
    scores = (
        jnp.einsum("qhd,khd->hqk", queries, split_kv[:, :, 0], preferred_element_type=jnp.float32)
        * 0.125
    )
    mask_rows = key_mask(key_count, rows, heads)
    return (jnp.where(mask_rows[:, None, :], scores, -1e30), split_kv)


def absorb(state, queries, pair_rows, key_count):
    row_max, row_sum, blended = state
    scores, split_kv = head_scores(queries, pair_rows, key_count)
    new_max = jnp.maximum(row_max, jnp.max(scores, axis=2))
    rescale = jnp.exp(row_max - new_max)
    weights = jnp.exp(scores - new_max[:, :, None])
    row_sum = row_sum * rescale + jnp.sum(weights, axis=2)
    blended = blended * rescale[:, :, None] + jnp.einsum(
        "hqk,khd->hqd",
        weights.astype(jnp.bfloat16),
        split_kv[:, :, 1],
        preferred_element_type=jnp.float32,
    )
    return (new_max, row_sum, blended)


def contribution(queries, grad_heads, log_total, row_dot, pair_rows, key_count):
    scores, split_kv = head_scores(queries, pair_rows, key_count)
    prob_full = jnp.exp(scores - log_total[:, :, None])
    d_value = jnp.einsum(
        "hqk,qhd->khd",
        prob_full.astype(jnp.bfloat16),
        grad_heads,
        preferred_element_type=jnp.float32,
    )
    d_prob = jnp.einsum(
        "qhd,khd->hqk", grad_heads, split_kv[:, :, 1], preferred_element_type=jnp.float32
    )
    d_score = (prob_full * (d_prob - row_dot[:, :, None])).astype(jnp.bfloat16)
    d_query = 0.125 * jnp.einsum(
        "hqk,khd->qhd", d_score, split_kv[:, :, 0], preferred_element_type=jnp.float32
    )
    d_key = 0.125 * jnp.einsum("hqk,qhd->khd", d_score, queries, preferred_element_type=jnp.float32)
    rows = pair_rows.shape[0]
    return (d_query, jnp.stack([d_key, d_value], axis=2).reshape(rows, -1))


def move_keys(pair_rows):
    moved = shifted(pair_rows, "seq", 1)
    return moved


def move_grads(accum):
    moved = shifted(accum.astype(jnp.bfloat16), "seq", 1).astype(accum.dtype)
    return moved


def exchange_bits():
    seq_bits = lax.axis_size("seq").bit_length() - 1
    clip_bits = lax.axis_size("clip").bit_length() - 1
    assert (1 << seq_bits) == lax.axis_size("seq")
    assert (1 << clip_bits) == lax.axis_size("clip")
    return seq_bits, clip_bits


def exchange_order(values):
    seq_bits, clip_bits = exchange_bits()
    total = seq_bits + clip_bits
    lead = values.shape[0]
    split = values.reshape([lead] + [2] * total + [-1])
    seq_dims = [1 + seq_bits - 1 - bit for bit in range(seq_bits)]
    clip_dims = [1 + seq_bits + clip_bits - 1 - bit for bit in range(clip_bits)]
    perm = [0] + seq_dims + clip_dims + [total + 1]
    return split.transpose(perm).reshape(values.shape)


def halving_scatter(grad, small=None):
    seq_bits, clip_bits = exchange_bits()
    total = seq_bits + clip_bits
    data = grad.reshape([2] * total + [-1, grad.shape[1]])
    order_a = list(range(seq_bits))
    order_b = [0] + list(range(seq_bits - 1, 0, -1))
    core_bit = lax.axis_index("seq") & 1
    left_a = list(range(seq_bits))
    left_b = list(range(seq_bits))
    for step in range(seq_bits):
        bit_a, bit_b = order_a[step], order_b[step]
        dim_a, dim_b = left_a.index(bit_a), left_b.index(bit_b)
        me = lax.axis_index("seq")
        mine_a = (me >> bit_a) & 1
        mine_b = (me >> bit_b) & 1
        pairs = []
        for src in range(lax.axis_size("seq")):
            bit = bit_a if (src & 1) == 0 else bit_b
            pairs.append((src, src ^ (1 << bit)))
        keep = jnp.where(
            core_bit == 0,
            lax.dynamic_index_in_dim(data, mine_a, axis=dim_a, keepdims=False),
            lax.dynamic_index_in_dim(data, mine_b, axis=dim_b, keepdims=False),
        )
        give = jnp.where(
            core_bit == 0,
            lax.dynamic_index_in_dim(data, 1 - mine_a, axis=dim_a, keepdims=False),
            lax.dynamic_index_in_dim(data, 1 - mine_b, axis=dim_b, keepdims=False),
        )
        left_a.pop(dim_a)
        left_b.pop(dim_b)
        if small is None:
            got = lax.ppermute(give.astype(jnp.bfloat16), "seq", pairs)
        else:
            got, got_small = lax.ppermute((give.astype(jnp.bfloat16), small), "seq", pairs)
            small = small + got_small
        data = keep + got.astype(jnp.float32)
    for bit in range(clip_bits):
        mine = (lax.axis_index("clip") >> bit) & 1
        pairs = [(src, src ^ (1 << bit)) for src in range(lax.axis_size("clip"))]
        keep = lax.dynamic_index_in_dim(data, mine, axis=0, keepdims=False)
        give = lax.dynamic_index_in_dim(data, 1 - mine, axis=0, keepdims=False)
        if small is None:
            got = lax.ppermute(give.astype(jnp.bfloat16), "clip", pairs)
        else:
            got, got_small = lax.ppermute((give.astype(jnp.bfloat16), small), "clip", pairs)
            small = small + got_small
        data = keep + got.astype(jnp.float32)
    return data, small


def xor_pairs(mask):
    count = lax.axis_size("seq")
    return [(src, src ^ mask) for src in range(count)]


def gather_blocks(block):
    half = lax.axis_size("seq") // 2
    same_core = [block] + [lax.ppermute(block, "seq", xor_pairs(2 * k)) for k in range(1, half)]
    group = jnp.stack(same_core)
    other = lax.ppermute(group, "seq", xor_pairs(1))
    return jnp.concatenate([group, other], axis=0)


def return_blocks(parts):
    half = lax.axis_size("seq") // 2
    got = lax.ppermute(parts[half:], "seq", xor_pairs(1))
    summed = parts[:half].astype(jnp.float32) + got.astype(jnp.float32)
    accum = summed[0]
    for k in range(1, half):
        sent = lax.ppermute(summed[k].astype(jnp.bfloat16), "seq", xor_pairs(2 * k))
        accum = accum + sent.astype(jnp.float32)
    return accum


def per_device(raw_tokens, teacher, keep_rows, w_qkv, w_out, ln_gain):
    shards = lax.axis_size("seq")
    my_index = lax.axis_index("seq")
    row_ids = keep_rows[0]
    list_slots = row_ids.shape[0]
    is_kept = row_ids >= 0
    kept_count = jnp.sum(is_kept.astype(jnp.int32))
    safe_ids = jnp.maximum(row_ids, 0)
    kept_tokens = jnp.where(is_kept[:, None], raw_tokens[0][safe_ids], jnp.zeros((), jnp.bfloat16))
    kept_target = jnp.where(is_kept[:, None], teacher[0][safe_ids], jnp.zeros((), jnp.bfloat16))
    count_table = lax.all_to_all(
        jnp.broadcast_to(kept_count.reshape(1, 1), (shards, 1)), "seq", 0, 0, tiled=True
    ).reshape(shards)
    shard_ids = jnp.arange(shards, dtype=jnp.int32)
    per_peer = -(-list_slots // shards)
    starts = jnp.cumsum(count_table) - count_table
    before = jnp.sum(jnp.where(shard_ids < my_index, count_table, 0))
    slot_ids = jnp.arange(per_peer, dtype=jnp.int32)
    pick = (shard_ids[:, None] - before) % shards + slot_ids[None, :] * shards
    pick_ok = pick < kept_count
    pick_safe = jnp.minimum(pick, list_slots - 1)
    send_tokens = jnp.where(
        pick_ok[:, :, None], kept_tokens[pick_safe], jnp.zeros((), jnp.bfloat16)
    )
    send_target = jnp.where(
        pick_ok[:, :, None], kept_target[pick_safe], jnp.zeros((), jnp.bfloat16)
    )
    got_tokens, got_target = (
        lax.all_to_all(send_tokens, "seq", split_axis=0, concat_axis=0, tiled=True),
        lax.all_to_all(send_target, "seq", split_axis=0, concat_axis=0, tiled=True),
    )
    from_pick = (my_index - starts[:, None]) % shards + slot_ids[None, :] * shards
    from_ok = from_pick < count_table[:, None]
    place = jnp.where(from_ok, (starts[:, None] + from_pick) // shards, TOK_DEV).reshape(-1)
    width = got_tokens.shape[2]
    tokens = (
        jnp.zeros((TOK_DEV, width), jnp.bfloat16)
        .at[place]
        .set(got_tokens.reshape(-1, width), mode="drop")
    )
    target = (
        jnp.zeros((TOK_DEV, width), jnp.bfloat16)
        .at[place]
        .set(got_target.reshape(-1, width), mode="drop")
    )
    rows = tokens.shape[0]
    inner = w_out.shape[0]
    heads = inner // HEAD_DIM
    normed, hidden = layer_norm(tokens, ln_gain)
    queries = (
        jnp.dot(hidden, w_qkv[:, :inner], preferred_element_type=jnp.float32)
        .astype(jnp.bfloat16)
        .reshape(rows, heads, HEAD_DIM)
        .transpose(1, 0, 2)
    )
    pair_cols = jnp.dot(w_qkv[:, inner:].T, hidden.T, preferred_element_type=jnp.float32).astype(
        jnp.bfloat16
    )
    gathered = gather_blocks(pair_cols)
    split_kv = gathered.reshape(shards, heads, 2, HEAD_DIM, rows).transpose(1, 2, 3, 0, 4)
    split_kv = split_kv.reshape(heads, 2, HEAD_DIM, shards * rows)
    keys_t = split_kv[:, 0]
    values_t = split_kv[:, 1]
    scores = jnp.einsum("hqd,hdk->hqk", queries, keys_t, preferred_element_type=jnp.float32) * 0.125
    row_max = jnp.max(scores, axis=2)
    weights = jnp.exp(scores - row_max[:, :, None])
    row_sum = jnp.sum(weights, axis=2)
    blended = jnp.einsum(
        "hqk,hdk->hqd", weights.astype(jnp.bfloat16), values_t, preferred_element_type=jnp.float32
    )
    log_total = row_max + jnp.log(row_sum)
    attended = (
        (blended / row_sum[:, :, None]).transpose(1, 0, 2).reshape(rows, inner).astype(jnp.bfloat16)
    )
    student = tokens.astype(jnp.float32) + jnp.dot(
        attended, w_out, preferred_element_type=jnp.float32
    )
    token_loss, grad_y = align_terms(student, target)
    grad_b = grad_y.astype(jnp.bfloat16)
    grad_wout = jnp.dot(exchange_order(attended).T, grad_b, preferred_element_type=jnp.float32)
    grad_heads = (
        jnp.dot(grad_b, w_out.T, preferred_element_type=jnp.float32)
        .astype(jnp.bfloat16)
        .reshape(rows, heads, HEAD_DIM)
        .transpose(1, 0, 2)
    )
    row_dot = jnp.sum(
        grad_heads.astype(jnp.float32)
        * attended.reshape(rows, heads, HEAD_DIM).transpose(1, 0, 2).astype(jnp.float32),
        axis=2,
    )
    prob_full = jnp.exp(scores - log_total[:, :, None])
    d_value_t = jnp.einsum(
        "hqd,hqk->hdk", grad_heads, prob_full.astype(jnp.bfloat16), preferred_element_type=jnp.float32
    )
    d_prob = jnp.einsum("hqd,hdk->hqk", grad_heads, values_t, preferred_element_type=jnp.float32)
    d_score = (prob_full * (d_prob - row_dot[:, :, None])).astype(jnp.bfloat16)
    d_query = 0.125 * jnp.einsum("hqk,hdk->qhd", d_score, keys_t, preferred_element_type=jnp.float32)
    d_key_t = 0.125 * jnp.einsum("hqd,hqk->hdk", queries, d_score, preferred_element_type=jnp.float32)
    d_pairs = jnp.stack([d_key_t, d_value_t], axis=1).reshape(heads, 2, HEAD_DIM, shards, rows)
    d_pairs = d_pairs.transpose(3, 0, 1, 2, 4).reshape(shards, 2 * inner, rows).astype(jnp.bfloat16)
    accum = return_blocks(d_pairs)
    d_proj = jnp.concatenate([d_query.reshape(rows, inner), accum.T], axis=1).astype(jnp.bfloat16)
    grad_wqkv = jnp.dot(exchange_order(hidden).T, d_proj, preferred_element_type=jnp.float32)
    d_hidden = jnp.dot(d_proj, w_qkv.T, preferred_element_type=jnp.float32)
    grad_ln = jnp.sum(d_hidden * normed, axis=0)
    loss_part = jnp.sum(token_loss)
    small = jnp.concatenate([grad_ln, loss_part.reshape(1)])
    grad_out, unused = halving_scatter(grad_wout)
    grad_qkv, small = halving_scatter(grad_wqkv, small)
    count_all = shards * lax.axis_size("clip") * TOK_DEV
    return (small[-1] / count_all, grad_qkv.reshape(-1), grad_out.reshape(-1), small[:-1])


def solution(mesh):
    placed = (P("clip", "seq", None), P("clip", "seq", None), P("clip", "seq"), P(), P(), P())
    return jax.shard_map(
        per_device,
        mesh=mesh,
        in_specs=placed,
        out_specs=(P(), P(("seq", "clip")), P(("seq", "clip")), P()),
        check_vma=False,
    )
```

```python
import jax
import jax.numpy as jnp
from jax import lax
from jax.sharding import PartitionSpec as P

HEAD_DIM = 64
TOK_DEV = 128


def shifted(value, axis, steps):
    count = lax.axis_size(axis)
    pairs = [(source, (source + steps) % count) for source in range(count)]
    return lax.ppermute(value, axis, pairs)


def layer_norm(tokens, ln_gain):
    values = tokens.astype(jnp.float32)
    center = values - jnp.mean(values, axis=-1, keepdims=True)
    spread = jnp.mean(center * center, axis=-1, keepdims=True)
    normed = center * lax.rsqrt(spread + 1e-05)
    return (normed, (normed * ln_gain).astype(jnp.bfloat16))


def align_terms(student, target):
    target_f = target.astype(jnp.float32)
    inv_y = lax.rsqrt(jnp.sum(student * student, axis=-1, keepdims=True) + 1e-06)
    inv_t = lax.rsqrt(jnp.sum(target_f * target_f, axis=-1, keepdims=True) + 1e-06)
    differ = student * inv_y - target_f * inv_t
    token_loss = jnp.sum(differ * differ, axis=-1)
    slopes = 2.0 * differ
    grad_y = inv_y * slopes - student * (inv_y * inv_y * inv_y) * jnp.sum(
        slopes * student, axis=-1, keepdims=True
    )
    return (token_loss, grad_y)


def key_mask(key_count, rows, heads):
    slot_idx = jnp.arange(rows, dtype=jnp.int32)
    halves = slot_idx[None, :] < key_count[:, None]
    return jnp.repeat(halves, heads // 2, axis=0)


def head_scores(queries, pair_rows, key_count):
    rows = pair_rows.shape[0]
    heads = queries.shape[1]
    split_kv = pair_rows.reshape(rows, heads, 2, HEAD_DIM)
    scores = (
        jnp.einsum("qhd,khd->hqk", queries, split_kv[:, :, 0], preferred_element_type=jnp.float32)
        * 0.125
    )
    mask_rows = key_mask(key_count, rows, heads)
    return (jnp.where(mask_rows[:, None, :], scores, -1e30), split_kv)


def absorb(state, queries, pair_rows, key_count):
    row_max, row_sum, blended = state
    scores, split_kv = head_scores(queries, pair_rows, key_count)
    new_max = jnp.maximum(row_max, jnp.max(scores, axis=2))
    rescale = jnp.exp(row_max - new_max)
    weights = jnp.exp(scores - new_max[:, :, None])
    row_sum = row_sum * rescale + jnp.sum(weights, axis=2)
    blended = blended * rescale[:, :, None] + jnp.einsum(
        "hqk,khd->hqd",
        weights.astype(jnp.bfloat16),
        split_kv[:, :, 1],
        preferred_element_type=jnp.float32,
    )
    return (new_max, row_sum, blended)


def contribution(queries, grad_heads, log_total, row_dot, pair_rows, key_count):
    scores, split_kv = head_scores(queries, pair_rows, key_count)
    prob_full = jnp.exp(scores - log_total[:, :, None])
    d_value = jnp.einsum(
        "hqk,qhd->khd",
        prob_full.astype(jnp.bfloat16),
        grad_heads,
        preferred_element_type=jnp.float32,
    )
    d_prob = jnp.einsum(
        "qhd,khd->hqk", grad_heads, split_kv[:, :, 1], preferred_element_type=jnp.float32
    )
    d_score = (prob_full * (d_prob - row_dot[:, :, None])).astype(jnp.bfloat16)
    d_query = 0.125 * jnp.einsum(
        "hqk,khd->qhd", d_score, split_kv[:, :, 0], preferred_element_type=jnp.float32
    )
    d_key = 0.125 * jnp.einsum("hqk,qhd->khd", d_score, queries, preferred_element_type=jnp.float32)
    rows = pair_rows.shape[0]
    return (d_query, jnp.stack([d_key, d_value], axis=2).reshape(rows, -1))


def move_keys(pair_rows):
    moved = shifted(pair_rows, "seq", 1)
    return moved


def move_grads(accum):
    moved = shifted(accum.astype(jnp.bfloat16), "seq", 1).astype(accum.dtype)
    return moved


def exchange_bits():
    seq_bits = lax.axis_size("seq").bit_length() - 1
    clip_bits = lax.axis_size("clip").bit_length() - 1
    assert (1 << seq_bits) == lax.axis_size("seq")
    assert (1 << clip_bits) == lax.axis_size("clip")
    return seq_bits, clip_bits


def exchange_order(values):
    seq_bits, clip_bits = exchange_bits()
    total = seq_bits + clip_bits
    lead = values.shape[0]
    split = values.reshape([lead] + [2] * total + [-1])
    seq_dims = [1 + seq_bits - 1 - bit for bit in range(seq_bits)]
    clip_dims = [1 + seq_bits + clip_bits - 1 - bit for bit in range(clip_bits)]
    perm = [0] + seq_dims + clip_dims + [total + 1]
    return split.transpose(perm).reshape(values.shape)


def halving_scatter(grad, small=None):
    seq_bits, clip_bits = exchange_bits()
    total = seq_bits + clip_bits
    data = grad.reshape([2] * total + [-1, grad.shape[1]])
    order_a = list(range(seq_bits))
    order_b = [0] + list(range(seq_bits - 1, 0, -1))
    core_bit = lax.axis_index("seq") & 1
    left_a = list(range(seq_bits))
    left_b = list(range(seq_bits))
    for step in range(seq_bits):
        bit_a, bit_b = order_a[step], order_b[step]
        dim_a, dim_b = left_a.index(bit_a), left_b.index(bit_b)
        me = lax.axis_index("seq")
        mine_a = (me >> bit_a) & 1
        mine_b = (me >> bit_b) & 1
        pairs = []
        for src in range(lax.axis_size("seq")):
            bit = bit_a if (src & 1) == 0 else bit_b
            pairs.append((src, src ^ (1 << bit)))
        keep = jnp.where(
            core_bit == 0,
            lax.dynamic_index_in_dim(data, mine_a, axis=dim_a, keepdims=False),
            lax.dynamic_index_in_dim(data, mine_b, axis=dim_b, keepdims=False),
        )
        give = jnp.where(
            core_bit == 0,
            lax.dynamic_index_in_dim(data, 1 - mine_a, axis=dim_a, keepdims=False),
            lax.dynamic_index_in_dim(data, 1 - mine_b, axis=dim_b, keepdims=False),
        )
        left_a.pop(dim_a)
        left_b.pop(dim_b)
        if small is None:
            got = lax.ppermute(give.astype(jnp.bfloat16), "seq", pairs)
        else:
            got, got_small = lax.ppermute((give.astype(jnp.bfloat16), small), "seq", pairs)
            small = small + got_small
        data = keep + got.astype(jnp.float32)
    for bit in range(clip_bits):
        mine = (lax.axis_index("clip") >> bit) & 1
        pairs = [(src, src ^ (1 << bit)) for src in range(lax.axis_size("clip"))]
        keep = lax.dynamic_index_in_dim(data, mine, axis=0, keepdims=False)
        give = lax.dynamic_index_in_dim(data, 1 - mine, axis=0, keepdims=False)
        if small is None:
            got = lax.ppermute(give.astype(jnp.bfloat16), "clip", pairs)
        else:
            got, got_small = lax.ppermute((give.astype(jnp.bfloat16), small), "clip", pairs)
            small = small + got_small
        data = keep + got.astype(jnp.float32)
    return data, small


def xor_pairs(mask):
    count = lax.axis_size("seq")
    return [(src, src ^ mask) for src in range(count)]


def gather_blocks(block):
    half = lax.axis_size("seq") // 2
    same_core = [block] + [lax.ppermute(block, "seq", xor_pairs(2 * k)) for k in range(1, half)]
    group = jnp.stack(same_core)
    other = lax.ppermute(group, "seq", xor_pairs(1))
    return jnp.concatenate([group, other], axis=0)


def return_blocks(parts):
    half = lax.axis_size("seq") // 2
    got = lax.ppermute(parts[half:], "seq", xor_pairs(1))
    summed = parts[:half].astype(jnp.float32) + got.astype(jnp.float32)
    accum = summed[0]
    for k in range(1, half):
        sent = lax.ppermute(summed[k].astype(jnp.bfloat16), "seq", xor_pairs(2 * k))
        accum = accum + sent.astype(jnp.float32)
    return accum


def per_device(raw_tokens, teacher, keep_rows, w_qkv, w_out, ln_gain):
    shards = lax.axis_size("seq")
    my_index = lax.axis_index("seq")
    row_ids = keep_rows[0]
    list_slots = row_ids.shape[0]
    is_kept = row_ids >= 0
    kept_count = jnp.sum(is_kept.astype(jnp.int32))
    safe_ids = jnp.maximum(row_ids, 0)
    kept_tokens = jnp.where(is_kept[:, None], raw_tokens[0][safe_ids], jnp.zeros((), jnp.bfloat16))
    kept_target = jnp.where(is_kept[:, None], teacher[0][safe_ids], jnp.zeros((), jnp.bfloat16))
    count_table = lax.all_to_all(
        jnp.broadcast_to(kept_count.reshape(1, 1), (shards, 1)), "seq", 0, 0, tiled=True
    ).reshape(shards)
    shard_ids = jnp.arange(shards, dtype=jnp.int32)
    per_peer = -(-list_slots // shards)
    starts = jnp.cumsum(count_table) - count_table
    before = jnp.sum(jnp.where(shard_ids < my_index, count_table, 0))
    slot_ids = jnp.arange(per_peer, dtype=jnp.int32)
    pick = (shard_ids[:, None] - before) % shards + slot_ids[None, :] * shards
    pick_ok = pick < kept_count
    pick_safe = jnp.minimum(pick, list_slots - 1)
    send_tokens = jnp.where(
        pick_ok[:, :, None], kept_tokens[pick_safe], jnp.zeros((), jnp.bfloat16)
    )
    send_target = jnp.where(
        pick_ok[:, :, None], kept_target[pick_safe], jnp.zeros((), jnp.bfloat16)
    )
    got_tokens, got_target = (
        lax.all_to_all(send_tokens, "seq", split_axis=0, concat_axis=0, tiled=True),
        lax.all_to_all(send_target, "seq", split_axis=0, concat_axis=0, tiled=True),
    )
    from_pick = (my_index - starts[:, None]) % shards + slot_ids[None, :] * shards
    from_ok = from_pick < count_table[:, None]
    place = jnp.where(from_ok, (starts[:, None] + from_pick) // shards, TOK_DEV).reshape(-1)
    width = got_tokens.shape[2]
    tokens = (
        jnp.zeros((TOK_DEV, width), jnp.bfloat16)
        .at[place]
        .set(got_tokens.reshape(-1, width), mode="drop")
    )
    target = (
        jnp.zeros((TOK_DEV, width), jnp.bfloat16)
        .at[place]
        .set(got_target.reshape(-1, width), mode="drop")
    )
    rows = tokens.shape[0]
    inner = w_out.shape[0]
    heads = inner // HEAD_DIM
    normed, hidden = layer_norm(tokens, ln_gain)
    queries = (
        jnp.dot(hidden, w_qkv[:, :inner], preferred_element_type=jnp.float32)
        .astype(jnp.bfloat16)
        .reshape(rows, heads, HEAD_DIM)
        .transpose(1, 0, 2)
    )
    pair_cols = jnp.dot(w_qkv[:, inner:].T, hidden.T, preferred_element_type=jnp.float32).astype(
        jnp.bfloat16
    )
    gathered = gather_blocks(pair_cols)
    split_kv = gathered.reshape(shards, heads, 2, HEAD_DIM, rows).transpose(1, 2, 3, 0, 4)
    split_kv = split_kv.reshape(heads, 2, HEAD_DIM, shards * rows)
    keys_t = split_kv[:, 0]
    values_t = split_kv[:, 1]
    scores = jnp.einsum("hqd,hdk->hqk", queries, keys_t, preferred_element_type=jnp.float32) * 0.125
    row_max = jnp.max(scores, axis=2)
    weights = jnp.exp(scores - row_max[:, :, None])
    row_sum = jnp.sum(weights, axis=2)
    blended = jnp.einsum(
        "hqk,hdk->hqd", weights.astype(jnp.bfloat16), values_t, preferred_element_type=jnp.float32
    )
    log_total = row_max + jnp.log(row_sum)
    attended = (
        (blended / row_sum[:, :, None]).transpose(1, 0, 2).reshape(rows, inner).astype(jnp.bfloat16)
    )
    student = tokens.astype(jnp.float32) + jnp.dot(
        attended, w_out, preferred_element_type=jnp.float32
    )
    token_loss, grad_y = align_terms(student, target)
    grad_b = grad_y.astype(jnp.bfloat16)
    grad_wout = jnp.dot(exchange_order(attended).T, grad_b, preferred_element_type=jnp.float32)
    grad_heads = (
        jnp.dot(grad_b, w_out.T, preferred_element_type=jnp.float32)
        .astype(jnp.bfloat16)
        .reshape(rows, heads, HEAD_DIM)
        .transpose(1, 0, 2)
    )
    row_dot = jnp.sum(
        grad_heads.astype(jnp.float32)
        * attended.reshape(rows, heads, HEAD_DIM).transpose(1, 0, 2).astype(jnp.float32),
        axis=2,
    )
    prob_full = jnp.exp(scores - log_total[:, :, None])
    d_value_t = jnp.einsum(
        "hqd,hqk->hdk", grad_heads, prob_full.astype(jnp.bfloat16), preferred_element_type=jnp.float32
    )
    d_prob = jnp.einsum("hqd,hdk->hqk", grad_heads, values_t, preferred_element_type=jnp.float32)
    d_score = (prob_full * (d_prob - row_dot[:, :, None])).astype(jnp.bfloat16)
    d_query = 0.125 * jnp.einsum("hqk,hdk->qhd", d_score, keys_t, preferred_element_type=jnp.float32)
    d_key_t = 0.125 * jnp.einsum("hqd,hqk->hdk", queries, d_score, preferred_element_type=jnp.float32)
    d_pairs = jnp.stack([d_key_t, d_value_t], axis=1).reshape(heads, 2, HEAD_DIM, shards, rows)
    d_pairs = d_pairs.transpose(3, 0, 1, 2, 4).reshape(shards, 2 * inner, rows).astype(jnp.bfloat16)
    accum = return_blocks(d_pairs)
    grad_out, unused = halving_scatter(grad_wout)
    grad_out, accum = lax.optimization_barrier((grad_out, accum))
    d_proj = jnp.concatenate([d_query.reshape(rows, inner), accum.T], axis=1).astype(jnp.bfloat16)
    grad_wqkv = jnp.dot(exchange_order(hidden).T, d_proj, preferred_element_type=jnp.float32)
    d_hidden = jnp.dot(d_proj, w_qkv.T, preferred_element_type=jnp.float32)
    grad_ln = jnp.sum(d_hidden * normed, axis=0)
    loss_part = jnp.sum(token_loss)
    small = jnp.concatenate([grad_ln, loss_part.reshape(1)])
    grad_qkv, small = halving_scatter(grad_wqkv, small)
    count_all = shards * lax.axis_size("clip") * TOK_DEV
    return (small[-1] / count_all, grad_qkv.reshape(-1), grad_out.reshape(-1), small[:-1])


def solution(mesh):
    placed = (P("clip", "seq", None), P("clip", "seq", None), P("clip", "seq"), P(), P(), P())
    return jax.shard_map(
        per_device,
        mesh=mesh,
        in_specs=placed,
        out_specs=(P(), P(("seq", "clip")), P(("seq", "clip")), P()),
        check_vma=False,
    )
```

```python
import jax
import jax.numpy as jnp
from jax import lax
from jax.sharding import PartitionSpec as P

HEAD_DIM = 64
TOK_DEV = 128


def shifted(value, axis, steps):
    count = lax.axis_size(axis)
    pairs = [(source, (source + steps) % count) for source in range(count)]
    return lax.ppermute(value, axis, pairs)


def layer_norm(tokens, ln_gain):
    values = tokens.astype(jnp.float32)
    center = values - jnp.mean(values, axis=-1, keepdims=True)
    spread = jnp.mean(center * center, axis=-1, keepdims=True)
    normed = center * lax.rsqrt(spread + 1e-05)
    return (normed, (normed * ln_gain).astype(jnp.bfloat16))


def align_terms(student, target):
    target_f = target.astype(jnp.float32)
    inv_y = lax.rsqrt(jnp.sum(student * student, axis=-1, keepdims=True) + 1e-06)
    inv_t = lax.rsqrt(jnp.sum(target_f * target_f, axis=-1, keepdims=True) + 1e-06)
    differ = student * inv_y - target_f * inv_t
    token_loss = jnp.sum(differ * differ, axis=-1)
    slopes = 2.0 * differ
    grad_y = inv_y * slopes - student * (inv_y * inv_y * inv_y) * jnp.sum(
        slopes * student, axis=-1, keepdims=True
    )
    return (token_loss, grad_y)


def key_mask(key_count, rows, heads):
    slot_idx = jnp.arange(rows, dtype=jnp.int32)
    halves = slot_idx[None, :] < key_count[:, None]
    return jnp.repeat(halves, heads // 2, axis=0)


def head_scores(queries, pair_rows, key_count):
    rows = pair_rows.shape[0]
    heads = queries.shape[1]
    split_kv = pair_rows.reshape(rows, heads, 2, HEAD_DIM)
    scores = (
        jnp.einsum("qhd,khd->hqk", queries, split_kv[:, :, 0], preferred_element_type=jnp.float32)
        * 0.125
    )
    mask_rows = key_mask(key_count, rows, heads)
    return (jnp.where(mask_rows[:, None, :], scores, -1e30), split_kv)


def absorb(state, queries, pair_rows, key_count):
    row_max, row_sum, blended = state
    scores, split_kv = head_scores(queries, pair_rows, key_count)
    new_max = jnp.maximum(row_max, jnp.max(scores, axis=2))
    rescale = jnp.exp(row_max - new_max)
    weights = jnp.exp(scores - new_max[:, :, None])
    row_sum = row_sum * rescale + jnp.sum(weights, axis=2)
    blended = blended * rescale[:, :, None] + jnp.einsum(
        "hqk,khd->hqd",
        weights.astype(jnp.bfloat16),
        split_kv[:, :, 1],
        preferred_element_type=jnp.float32,
    )
    return (new_max, row_sum, blended)


def contribution(queries, grad_heads, log_total, row_dot, pair_rows, key_count):
    scores, split_kv = head_scores(queries, pair_rows, key_count)
    prob_full = jnp.exp(scores - log_total[:, :, None])
    d_value = jnp.einsum(
        "hqk,qhd->khd",
        prob_full.astype(jnp.bfloat16),
        grad_heads,
        preferred_element_type=jnp.float32,
    )
    d_prob = jnp.einsum(
        "qhd,khd->hqk", grad_heads, split_kv[:, :, 1], preferred_element_type=jnp.float32
    )
    d_score = (prob_full * (d_prob - row_dot[:, :, None])).astype(jnp.bfloat16)
    d_query = 0.125 * jnp.einsum(
        "hqk,khd->qhd", d_score, split_kv[:, :, 0], preferred_element_type=jnp.float32
    )
    d_key = 0.125 * jnp.einsum("hqk,qhd->khd", d_score, queries, preferred_element_type=jnp.float32)
    rows = pair_rows.shape[0]
    return (d_query, jnp.stack([d_key, d_value], axis=2).reshape(rows, -1))


def move_keys(pair_rows):
    moved = shifted(pair_rows, "seq", 1)
    return moved


def move_grads(accum):
    moved = shifted(accum.astype(jnp.bfloat16), "seq", 1).astype(accum.dtype)
    return moved


def exchange_bits():
    seq_bits = lax.axis_size("seq").bit_length() - 1
    clip_bits = lax.axis_size("clip").bit_length() - 1
    assert (1 << seq_bits) == lax.axis_size("seq")
    assert (1 << clip_bits) == lax.axis_size("clip")
    return seq_bits, clip_bits


def exchange_order(values):
    seq_bits, clip_bits = exchange_bits()
    total = seq_bits + clip_bits
    lead = values.shape[0]
    split = values.reshape([lead] + [2] * total + [-1])
    seq_dims = [1 + seq_bits - 1 - bit for bit in range(seq_bits)]
    clip_dims = [1 + seq_bits + clip_bits - 1 - bit for bit in range(clip_bits)]
    perm = [0] + seq_dims + clip_dims + [total + 1]
    return split.transpose(perm).reshape(values.shape)


def halving_scatter(grad, small=None):
    seq_bits, clip_bits = exchange_bits()
    total = seq_bits + clip_bits
    data = grad.reshape([2] * total + [-1, grad.shape[1]])
    order_a = list(range(seq_bits))
    order_b = [0] + list(range(seq_bits - 1, 0, -1))
    core_bit = lax.axis_index("seq") & 1
    left_a = list(range(seq_bits))
    left_b = list(range(seq_bits))
    for step in range(seq_bits):
        bit_a, bit_b = order_a[step], order_b[step]
        dim_a, dim_b = left_a.index(bit_a), left_b.index(bit_b)
        me = lax.axis_index("seq")
        mine_a = (me >> bit_a) & 1
        mine_b = (me >> bit_b) & 1
        pairs = []
        for src in range(lax.axis_size("seq")):
            bit = bit_a if (src & 1) == 0 else bit_b
            pairs.append((src, src ^ (1 << bit)))
        keep = jnp.where(
            core_bit == 0,
            lax.dynamic_index_in_dim(data, mine_a, axis=dim_a, keepdims=False),
            lax.dynamic_index_in_dim(data, mine_b, axis=dim_b, keepdims=False),
        )
        give = jnp.where(
            core_bit == 0,
            lax.dynamic_index_in_dim(data, 1 - mine_a, axis=dim_a, keepdims=False),
            lax.dynamic_index_in_dim(data, 1 - mine_b, axis=dim_b, keepdims=False),
        )
        left_a.pop(dim_a)
        left_b.pop(dim_b)
        if small is None:
            got = lax.ppermute(give.astype(jnp.bfloat16), "seq", pairs)
        else:
            got, got_small = lax.ppermute((give.astype(jnp.bfloat16), small), "seq", pairs)
            small = small + got_small
        data = keep + got.astype(jnp.float32)
    for bit in range(clip_bits):
        mine = (lax.axis_index("clip") >> bit) & 1
        pairs = [(src, src ^ (1 << bit)) for src in range(lax.axis_size("clip"))]
        keep = lax.dynamic_index_in_dim(data, mine, axis=0, keepdims=False)
        give = lax.dynamic_index_in_dim(data, 1 - mine, axis=0, keepdims=False)
        if small is None:
            got = lax.ppermute(give.astype(jnp.bfloat16), "clip", pairs)
        else:
            got, got_small = lax.ppermute((give.astype(jnp.bfloat16), small), "clip", pairs)
            small = small + got_small
        data = keep + got.astype(jnp.float32)
    return data, small


def xor_pairs(mask):
    count = lax.axis_size("seq")
    return [(src, src ^ mask) for src in range(count)]


def gather_blocks(block):
    half = lax.axis_size("seq") // 2
    same_core = [block] + [lax.ppermute(block, "seq", xor_pairs(2 * k)) for k in range(1, half)]
    group = jnp.stack(same_core)
    other = lax.ppermute(group, "seq", xor_pairs(1))
    return jnp.concatenate([group, other], axis=0)


def return_blocks(parts):
    half = lax.axis_size("seq") // 2
    got = lax.ppermute(parts[half:], "seq", xor_pairs(1))
    summed = parts[:half].astype(jnp.float32) + got.astype(jnp.float32)
    accum = summed[0]
    for k in range(1, half):
        sent = lax.ppermute(summed[k].astype(jnp.bfloat16), "seq", xor_pairs(2 * k))
        accum = accum + sent.astype(jnp.float32)
    return accum


def per_device(raw_tokens, teacher, keep_rows, w_qkv, w_out, ln_gain):
    shards = lax.axis_size("seq")
    my_index = lax.axis_index("seq")
    row_ids = keep_rows[0]
    list_slots = row_ids.shape[0]
    is_kept = row_ids >= 0
    kept_count = jnp.sum(is_kept.astype(jnp.int32))
    safe_ids = jnp.maximum(row_ids, 0)
    kept_tokens = jnp.where(is_kept[:, None], raw_tokens[0][safe_ids], jnp.zeros((), jnp.bfloat16))
    kept_target = jnp.where(is_kept[:, None], teacher[0][safe_ids], jnp.zeros((), jnp.bfloat16))
    count_table = lax.all_to_all(
        jnp.broadcast_to(kept_count.reshape(1, 1), (shards, 1)), "seq", 0, 0, tiled=True
    ).reshape(shards)
    shard_ids = jnp.arange(shards, dtype=jnp.int32)
    per_peer = -(-list_slots // shards)
    starts = jnp.cumsum(count_table) - count_table
    before = jnp.sum(jnp.where(shard_ids < my_index, count_table, 0))
    slot_ids = jnp.arange(per_peer, dtype=jnp.int32)
    pick = (shard_ids[:, None] - before) % shards + slot_ids[None, :] * shards
    pick_ok = pick < kept_count
    pick_safe = jnp.minimum(pick, list_slots - 1)
    send_tokens = jnp.where(
        pick_ok[:, :, None], kept_tokens[pick_safe], jnp.zeros((), jnp.bfloat16)
    )
    send_target = jnp.where(
        pick_ok[:, :, None], kept_target[pick_safe], jnp.zeros((), jnp.bfloat16)
    )
    got_tokens, got_target = (
        lax.all_to_all(send_tokens, "seq", split_axis=0, concat_axis=0, tiled=True),
        lax.all_to_all(send_target, "seq", split_axis=0, concat_axis=0, tiled=True),
    )
    from_pick = (my_index - starts[:, None]) % shards + slot_ids[None, :] * shards
    from_ok = from_pick < count_table[:, None]
    place = jnp.where(from_ok, (starts[:, None] + from_pick) // shards, TOK_DEV).reshape(-1)
    width = got_tokens.shape[2]
    tokens = (
        jnp.zeros((TOK_DEV, width), jnp.bfloat16)
        .at[place]
        .set(got_tokens.reshape(-1, width), mode="drop")
    )
    target = (
        jnp.zeros((TOK_DEV, width), jnp.bfloat16)
        .at[place]
        .set(got_target.reshape(-1, width), mode="drop")
    )
    rows = tokens.shape[0]
    inner = w_out.shape[0]
    heads = inner // HEAD_DIM
    normed, hidden = layer_norm(tokens, ln_gain)
    queries = (
        jnp.dot(hidden, w_qkv[:, :inner], preferred_element_type=jnp.float32)
        .astype(jnp.bfloat16)
        .reshape(rows, heads, HEAD_DIM)
        .transpose(1, 0, 2)
    )
    pair_cols = jnp.dot(w_qkv[:, inner:].T, hidden.T, preferred_element_type=jnp.float32).astype(
        jnp.bfloat16
    )
    gathered = gather_blocks(pair_cols)
    split_kv = gathered.reshape(shards, heads, 2, HEAD_DIM, rows)
    keys_b = split_kv[:, :, 0]
    values_b = split_kv[:, :, 1]
    queries_b = jnp.broadcast_to(queries[None], (shards,) + queries.shape)
    scores = (
        jnp.einsum("ihqd,ihdt->ihqt", queries_b, keys_b, preferred_element_type=jnp.float32) * 0.125
    )
    row_max = jnp.max(scores, axis=(0, 3))
    weights = jnp.exp(scores - row_max[None, :, :, None])
    row_sum = jnp.sum(weights, axis=(0, 3))
    blended = jnp.sum(
        jnp.einsum(
            "ihqt,ihdt->ihqd", weights.astype(jnp.bfloat16), values_b, preferred_element_type=jnp.float32
        ),
        axis=0,
    )
    log_total = row_max + jnp.log(row_sum)
    attended = (
        (blended / row_sum[:, :, None]).transpose(1, 0, 2).reshape(rows, inner).astype(jnp.bfloat16)
    )
    student = tokens.astype(jnp.float32) + jnp.dot(
        attended, w_out, preferred_element_type=jnp.float32
    )
    token_loss, grad_y = align_terms(student, target)
    grad_b = grad_y.astype(jnp.bfloat16)
    grad_wout = jnp.dot(exchange_order(attended).T, grad_b, preferred_element_type=jnp.float32)
    grad_heads = (
        jnp.dot(grad_b, w_out.T, preferred_element_type=jnp.float32)
        .astype(jnp.bfloat16)
        .reshape(rows, heads, HEAD_DIM)
        .transpose(1, 0, 2)
    )
    row_dot = jnp.sum(
        grad_heads.astype(jnp.float32)
        * attended.reshape(rows, heads, HEAD_DIM).transpose(1, 0, 2).astype(jnp.float32),
        axis=2,
    )
    prob_full = jnp.exp(scores - log_total[None, :, :, None])
    grad_heads_b = jnp.broadcast_to(grad_heads[None], (shards,) + grad_heads.shape)
    d_value_b = jnp.einsum(
        "ihqd,ihqt->ihdt", grad_heads_b, prob_full.astype(jnp.bfloat16), preferred_element_type=jnp.float32
    )
    d_prob = jnp.einsum("ihqd,ihdt->ihqt", grad_heads_b, values_b, preferred_element_type=jnp.float32)
    d_score = (prob_full * (d_prob - row_dot[None, :, :, None])).astype(jnp.bfloat16)
    d_query = 0.125 * jnp.sum(
        jnp.einsum("ihqt,ihdt->ihqd", d_score, keys_b, preferred_element_type=jnp.float32), axis=0
    ).transpose(1, 0, 2)
    d_key_b = 0.125 * jnp.einsum(
        "ihqd,ihqt->ihdt", queries_b, d_score, preferred_element_type=jnp.float32
    )
    d_pairs = jnp.stack([d_key_b, d_value_b], axis=2).reshape(shards, 2 * inner, rows).astype(jnp.bfloat16)
    accum = return_blocks(d_pairs)
    d_proj = jnp.concatenate([d_query.reshape(rows, inner), accum.T], axis=1).astype(jnp.bfloat16)
    grad_wqkv = jnp.dot(exchange_order(hidden).T, d_proj, preferred_element_type=jnp.float32)
    d_hidden = jnp.dot(d_proj, w_qkv.T, preferred_element_type=jnp.float32)
    grad_ln = jnp.sum(d_hidden * normed, axis=0)
    loss_part = jnp.sum(token_loss)
    small = jnp.concatenate([grad_ln, loss_part.reshape(1)])
    grad_out, unused = halving_scatter(grad_wout)
    grad_qkv, small = halving_scatter(grad_wqkv, small)
    count_all = shards * lax.axis_size("clip") * TOK_DEV
    return (small[-1] / count_all, grad_qkv.reshape(-1), grad_out.reshape(-1), small[:-1])


def solution(mesh):
    placed = (P("clip", "seq", None), P("clip", "seq", None), P("clip", "seq"), P(), P(), P())
    return jax.shard_map(
        per_device,
        mesh=mesh,
        in_specs=placed,
        out_specs=(P(), P(("seq", "clip")), P(("seq", "clip")), P()),
        check_vma=False,
    )
```

```python
import jax
import jax.numpy as jnp
from jax import lax
from jax.sharding import PartitionSpec as P

HEAD_DIM = 64
TOK_DEV = 128


def shifted(value, axis, steps):
    count = lax.axis_size(axis)
    pairs = [(source, (source + steps) % count) for source in range(count)]
    return lax.ppermute(value, axis, pairs)


def layer_norm(tokens, ln_gain):
    values = tokens.astype(jnp.float32)
    center = values - jnp.mean(values, axis=-1, keepdims=True)
    spread = jnp.mean(center * center, axis=-1, keepdims=True)
    normed = center * lax.rsqrt(spread + 1e-05)
    return (normed, (normed * ln_gain).astype(jnp.bfloat16))


def align_terms(student, target):
    target_f = target.astype(jnp.float32)
    inv_y = lax.rsqrt(jnp.sum(student * student, axis=-1, keepdims=True) + 1e-06)
    inv_t = lax.rsqrt(jnp.sum(target_f * target_f, axis=-1, keepdims=True) + 1e-06)
    differ = student * inv_y - target_f * inv_t
    token_loss = jnp.sum(differ * differ, axis=-1)
    slopes = 2.0 * differ
    grad_y = inv_y * slopes - student * (inv_y * inv_y * inv_y) * jnp.sum(
        slopes * student, axis=-1, keepdims=True
    )
    return (token_loss, grad_y)


def key_mask(key_count, rows, heads):
    slot_idx = jnp.arange(rows, dtype=jnp.int32)
    halves = slot_idx[None, :] < key_count[:, None]
    return jnp.repeat(halves, heads // 2, axis=0)


def head_scores(queries, pair_rows, key_count):
    rows = pair_rows.shape[0]
    heads = queries.shape[1]
    split_kv = pair_rows.reshape(rows, heads, 2, HEAD_DIM)
    scores = (
        jnp.einsum("qhd,khd->hqk", queries, split_kv[:, :, 0], preferred_element_type=jnp.float32)
        * 0.125
    )
    mask_rows = key_mask(key_count, rows, heads)
    return (jnp.where(mask_rows[:, None, :], scores, -1e30), split_kv)


def absorb(state, queries, pair_rows, key_count):
    row_max, row_sum, blended = state
    scores, split_kv = head_scores(queries, pair_rows, key_count)
    new_max = jnp.maximum(row_max, jnp.max(scores, axis=2))
    rescale = jnp.exp(row_max - new_max)
    weights = jnp.exp(scores - new_max[:, :, None])
    row_sum = row_sum * rescale + jnp.sum(weights, axis=2)
    blended = blended * rescale[:, :, None] + jnp.einsum(
        "hqk,khd->hqd",
        weights.astype(jnp.bfloat16),
        split_kv[:, :, 1],
        preferred_element_type=jnp.float32,
    )
    return (new_max, row_sum, blended)


def contribution(queries, grad_heads, log_total, row_dot, pair_rows, key_count):
    scores, split_kv = head_scores(queries, pair_rows, key_count)
    prob_full = jnp.exp(scores - log_total[:, :, None])
    d_value = jnp.einsum(
        "hqk,qhd->khd",
        prob_full.astype(jnp.bfloat16),
        grad_heads,
        preferred_element_type=jnp.float32,
    )
    d_prob = jnp.einsum(
        "qhd,khd->hqk", grad_heads, split_kv[:, :, 1], preferred_element_type=jnp.float32
    )
    d_score = (prob_full * (d_prob - row_dot[:, :, None])).astype(jnp.bfloat16)
    d_query = 0.125 * jnp.einsum(
        "hqk,khd->qhd", d_score, split_kv[:, :, 0], preferred_element_type=jnp.float32
    )
    d_key = 0.125 * jnp.einsum("hqk,qhd->khd", d_score, queries, preferred_element_type=jnp.float32)
    rows = pair_rows.shape[0]
    return (d_query, jnp.stack([d_key, d_value], axis=2).reshape(rows, -1))


def move_keys(pair_rows):
    moved = shifted(pair_rows, "seq", 1)
    return moved


def move_grads(accum):
    moved = shifted(accum.astype(jnp.bfloat16), "seq", 1).astype(accum.dtype)
    return moved


def exchange_bits():
    seq_bits = lax.axis_size("seq").bit_length() - 1
    clip_bits = lax.axis_size("clip").bit_length() - 1
    assert (1 << seq_bits) == lax.axis_size("seq")
    assert (1 << clip_bits) == lax.axis_size("clip")
    return seq_bits, clip_bits


def exchange_order(values):
    seq_bits, clip_bits = exchange_bits()
    total = seq_bits + clip_bits
    lead = values.shape[0]
    split = values.reshape([lead] + [2] * total + [-1])
    seq_dims = [1 + seq_bits - 1 - bit for bit in range(seq_bits)]
    clip_dims = [1 + seq_bits + clip_bits - 1 - bit for bit in range(clip_bits)]
    perm = [0] + seq_dims + clip_dims + [total + 1]
    return split.transpose(perm).reshape(values.shape)


def halving_scatter(grad, small=None):
    seq_bits, clip_bits = exchange_bits()
    total = seq_bits + clip_bits
    data = grad.reshape([2] * total + [-1, grad.shape[1]])
    order_a = list(range(seq_bits))
    order_b = [0] + list(range(seq_bits - 1, 0, -1))
    core_bit = lax.axis_index("seq") & 1
    left_a = list(range(seq_bits))
    left_b = list(range(seq_bits))
    for step in range(seq_bits):
        bit_a, bit_b = order_a[step], order_b[step]
        dim_a, dim_b = left_a.index(bit_a), left_b.index(bit_b)
        me = lax.axis_index("seq")
        mine_a = (me >> bit_a) & 1
        mine_b = (me >> bit_b) & 1
        pairs = []
        for src in range(lax.axis_size("seq")):
            bit = bit_a if (src & 1) == 0 else bit_b
            pairs.append((src, src ^ (1 << bit)))
        keep = jnp.where(
            core_bit == 0,
            lax.dynamic_index_in_dim(data, mine_a, axis=dim_a, keepdims=False),
            lax.dynamic_index_in_dim(data, mine_b, axis=dim_b, keepdims=False),
        )
        give = jnp.where(
            core_bit == 0,
            lax.dynamic_index_in_dim(data, 1 - mine_a, axis=dim_a, keepdims=False),
            lax.dynamic_index_in_dim(data, 1 - mine_b, axis=dim_b, keepdims=False),
        )
        left_a.pop(dim_a)
        left_b.pop(dim_b)
        if small is None:
            got = lax.ppermute(give.astype(jnp.bfloat16), "seq", pairs)
        else:
            got, got_small = lax.ppermute((give.astype(jnp.bfloat16), small), "seq", pairs)
            small = small + got_small
        data = keep + got.astype(jnp.float32)
    for bit in range(clip_bits):
        mine = (lax.axis_index("clip") >> bit) & 1
        pairs = [(src, src ^ (1 << bit)) for src in range(lax.axis_size("clip"))]
        keep = lax.dynamic_index_in_dim(data, mine, axis=0, keepdims=False)
        give = lax.dynamic_index_in_dim(data, 1 - mine, axis=0, keepdims=False)
        if small is None:
            got = lax.ppermute(give.astype(jnp.bfloat16), "clip", pairs)
        else:
            got, got_small = lax.ppermute((give.astype(jnp.bfloat16), small), "clip", pairs)
            small = small + got_small
        data = keep + got.astype(jnp.float32)
    return data, small


def xor_pairs(mask):
    count = lax.axis_size("seq")
    return [(src, src ^ mask) for src in range(count)]


def gather_blocks(block):
    half = lax.axis_size("seq") // 2
    same_core = [block] + [lax.ppermute(block, "seq", xor_pairs(2 * k)) for k in range(1, half)]
    group = jnp.stack(same_core)
    other = lax.ppermute(group, "seq", xor_pairs(1))
    return jnp.concatenate([group, other], axis=0)


def return_blocks(parts):
    half = lax.axis_size("seq") // 2
    got = lax.ppermute(parts[half:], "seq", xor_pairs(1))
    summed = parts[:half].astype(jnp.float32) + got.astype(jnp.float32)
    accum = summed[0]
    for k in range(1, half):
        sent = lax.ppermute(summed[k].astype(jnp.bfloat16), "seq", xor_pairs(2 * k))
        accum = accum + sent.astype(jnp.float32)
    return accum


def per_device(raw_tokens, teacher, keep_rows, w_qkv, w_out, ln_gain):
    shards = lax.axis_size("seq")
    my_index = lax.axis_index("seq")
    row_ids = keep_rows[0]
    list_slots = row_ids.shape[0]
    is_kept = row_ids >= 0
    kept_count = jnp.sum(is_kept.astype(jnp.int32))
    safe_ids = jnp.maximum(row_ids, 0)
    kept_tokens = jnp.where(is_kept[:, None], raw_tokens[0][safe_ids], jnp.zeros((), jnp.bfloat16))
    kept_target = jnp.where(is_kept[:, None], teacher[0][safe_ids], jnp.zeros((), jnp.bfloat16))
    count_table = lax.all_to_all(
        jnp.broadcast_to(kept_count.reshape(1, 1), (shards, 1)), "seq", 0, 0, tiled=True
    ).reshape(shards)
    shard_ids = jnp.arange(shards, dtype=jnp.int32)
    per_peer = -(-list_slots // shards)
    starts = jnp.cumsum(count_table) - count_table
    before = jnp.sum(jnp.where(shard_ids < my_index, count_table, 0))
    slot_ids = jnp.arange(per_peer, dtype=jnp.int32)
    pick = (shard_ids[:, None] - before) % shards + slot_ids[None, :] * shards
    pick_ok = pick < kept_count
    pick_safe = jnp.minimum(pick, list_slots - 1)
    send_tokens = jnp.where(
        pick_ok[:, :, None], kept_tokens[pick_safe], jnp.zeros((), jnp.bfloat16)
    )
    send_target = jnp.where(
        pick_ok[:, :, None], kept_target[pick_safe], jnp.zeros((), jnp.bfloat16)
    )
    got_tokens, got_target = (
        lax.all_to_all(send_tokens, "seq", split_axis=0, concat_axis=0, tiled=True),
        lax.all_to_all(send_target, "seq", split_axis=0, concat_axis=0, tiled=True),
    )
    from_pick = (my_index - starts[:, None]) % shards + slot_ids[None, :] * shards
    from_ok = from_pick < count_table[:, None]
    place = jnp.where(from_ok, (starts[:, None] + from_pick) // shards, TOK_DEV).reshape(-1)
    width = got_tokens.shape[2]
    tokens = (
        jnp.zeros((TOK_DEV, width), jnp.bfloat16)
        .at[place]
        .set(got_tokens.reshape(-1, width), mode="drop")
    )
    target = (
        jnp.zeros((TOK_DEV, width), jnp.bfloat16)
        .at[place]
        .set(got_target.reshape(-1, width), mode="drop")
    )
    rows = tokens.shape[0]
    inner = w_out.shape[0]
    heads = inner // HEAD_DIM
    normed, hidden = layer_norm(tokens, ln_gain)
    queries = (
        jnp.dot(hidden, w_qkv[:, :inner], preferred_element_type=jnp.float32)
        .astype(jnp.bfloat16)
        .reshape(rows, heads, HEAD_DIM)
        .transpose(1, 0, 2)
    )
    pair_cols = jnp.dot(w_qkv[:, inner:].T, hidden.T, preferred_element_type=jnp.float32).astype(
        jnp.bfloat16
    )
    gathered = gather_blocks(pair_cols)
    split_kv = gathered.reshape(shards, heads, 2, HEAD_DIM, rows)
    keys_b = split_kv[:, :, 0]
    values_b = split_kv[:, :, 1]
    queries_b = jnp.broadcast_to(queries[None], (shards,) + queries.shape)
    scores = (
        jnp.einsum("ihqd,ihdt->ihqt", queries_b, keys_b, preferred_element_type=jnp.float32) * 0.125
    )
    row_max = jnp.max(scores, axis=(0, 3))
    weights = jnp.exp(scores - row_max[None, :, :, None])
    row_sum = jnp.sum(weights, axis=(0, 3))
    blended = jnp.sum(
        jnp.einsum(
            "ihqt,ihdt->ihqd", weights.astype(jnp.bfloat16), values_b, preferred_element_type=jnp.float32
        ),
        axis=0,
    )
    log_total = row_max + jnp.log(row_sum)
    attended = (
        (blended / row_sum[:, :, None]).transpose(1, 0, 2).reshape(rows, inner).astype(jnp.bfloat16)
    )
    student = tokens.astype(jnp.float32) + jnp.dot(
        attended, w_out, preferred_element_type=jnp.float32
    )
    token_loss, grad_y = align_terms(student, target)
    grad_b = grad_y.astype(jnp.bfloat16)
    grad_wout = jnp.dot(exchange_order(attended).T, grad_b, preferred_element_type=jnp.float32)
    grad_heads = (
        jnp.dot(grad_b, w_out.T, preferred_element_type=jnp.float32)
        .astype(jnp.bfloat16)
        .reshape(rows, heads, HEAD_DIM)
        .transpose(1, 0, 2)
    )
    row_dot = jnp.sum(
        grad_heads.astype(jnp.float32)
        * attended.reshape(rows, heads, HEAD_DIM).transpose(1, 0, 2).astype(jnp.float32),
        axis=2,
    )
    prob_full = jnp.exp(scores - log_total[None, :, :, None])
    grad_heads_b = jnp.broadcast_to(grad_heads[None], (shards,) + grad_heads.shape)
    d_value_b = jnp.einsum(
        "ihqd,ihqt->ihdt", grad_heads_b, prob_full.astype(jnp.bfloat16), preferred_element_type=jnp.float32
    )
    d_prob = jnp.einsum("ihqd,ihdt->ihqt", grad_heads_b, values_b, preferred_element_type=jnp.float32)
    d_score = (prob_full * (d_prob - row_dot[None, :, :, None])).astype(jnp.bfloat16)
    d_query_t = 0.125 * jnp.sum(
        jnp.einsum("ihqt,ihdt->ihdq", d_score, keys_b, preferred_element_type=jnp.float32), axis=0
    )
    d_key_b = 0.125 * jnp.einsum(
        "ihqd,ihqt->ihdt", queries_b, d_score, preferred_element_type=jnp.float32
    )
    d_pairs = jnp.stack([d_key_b, d_value_b], axis=2).reshape(shards, 2 * inner, rows).astype(jnp.bfloat16)
    accum = return_blocks(d_pairs)
    d_proj_t = jnp.concatenate([d_query_t.reshape(inner, rows), accum], axis=0).astype(jnp.bfloat16)
    grad_wqkv = jnp.einsum(
        "tf,ct->fc", exchange_order(hidden), d_proj_t, preferred_element_type=jnp.float32
    )
    d_hidden = jnp.einsum("ct,fc->tf", d_proj_t, w_qkv, preferred_element_type=jnp.float32)
    grad_ln = jnp.sum(d_hidden * normed, axis=0)
    loss_part = jnp.sum(token_loss)
    small = jnp.concatenate([grad_ln, loss_part.reshape(1)])
    grad_out, unused = halving_scatter(grad_wout)
    grad_qkv, small = halving_scatter(grad_wqkv, small)
    count_all = shards * lax.axis_size("clip") * TOK_DEV
    return (small[-1] / count_all, grad_qkv.reshape(-1), grad_out.reshape(-1), small[:-1])


def solution(mesh):
    placed = (P("clip", "seq", None), P("clip", "seq", None), P("clip", "seq"), P(), P(), P())
    return jax.shard_map(
        per_device,
        mesh=mesh,
        in_specs=placed,
        out_specs=(P(), P(("seq", "clip")), P(("seq", "clip")), P()),
        check_vma=False,
    )
```

```python
import jax
import jax.numpy as jnp
from jax import lax
from jax.sharding import PartitionSpec as P

HEAD_DIM = 64
TOK_DEV = 128


def shifted(value, axis, steps):
    count = lax.axis_size(axis)
    pairs = [(source, (source + steps) % count) for source in range(count)]
    return lax.ppermute(value, axis, pairs)


def layer_norm(tokens, ln_gain):
    values = tokens.astype(jnp.float32)
    center = values - jnp.mean(values, axis=-1, keepdims=True)
    spread = jnp.mean(center * center, axis=-1, keepdims=True)
    normed = center * lax.rsqrt(spread + 1e-05)
    return (normed, (normed * ln_gain).astype(jnp.bfloat16))


def align_terms(student, target):
    target_f = target.astype(jnp.float32)
    inv_y = lax.rsqrt(jnp.sum(student * student, axis=-1, keepdims=True) + 1e-06)
    inv_t = lax.rsqrt(jnp.sum(target_f * target_f, axis=-1, keepdims=True) + 1e-06)
    differ = student * inv_y - target_f * inv_t
    token_loss = jnp.sum(differ * differ, axis=-1)
    slopes = 2.0 * differ
    grad_y = inv_y * slopes - student * (inv_y * inv_y * inv_y) * jnp.sum(
        slopes * student, axis=-1, keepdims=True
    )
    return (token_loss, grad_y)


def key_mask(key_count, rows, heads):
    slot_idx = jnp.arange(rows, dtype=jnp.int32)
    halves = slot_idx[None, :] < key_count[:, None]
    return jnp.repeat(halves, heads // 2, axis=0)


def head_scores(queries, pair_rows, key_count):
    rows = pair_rows.shape[0]
    heads = queries.shape[1]
    split_kv = pair_rows.reshape(rows, heads, 2, HEAD_DIM)
    scores = (
        jnp.einsum("qhd,khd->hqk", queries, split_kv[:, :, 0], preferred_element_type=jnp.float32)
        * 0.125
    )
    mask_rows = key_mask(key_count, rows, heads)
    return (jnp.where(mask_rows[:, None, :], scores, -1e30), split_kv)


def absorb(state, queries, pair_rows, key_count):
    row_max, row_sum, blended = state
    scores, split_kv = head_scores(queries, pair_rows, key_count)
    new_max = jnp.maximum(row_max, jnp.max(scores, axis=2))
    rescale = jnp.exp(row_max - new_max)
    weights = jnp.exp(scores - new_max[:, :, None])
    row_sum = row_sum * rescale + jnp.sum(weights, axis=2)
    blended = blended * rescale[:, :, None] + jnp.einsum(
        "hqk,khd->hqd",
        weights.astype(jnp.bfloat16),
        split_kv[:, :, 1],
        preferred_element_type=jnp.float32,
    )
    return (new_max, row_sum, blended)


def contribution(queries, grad_heads, log_total, row_dot, pair_rows, key_count):
    scores, split_kv = head_scores(queries, pair_rows, key_count)
    prob_full = jnp.exp(scores - log_total[:, :, None])
    d_value = jnp.einsum(
        "hqk,qhd->khd",
        prob_full.astype(jnp.bfloat16),
        grad_heads,
        preferred_element_type=jnp.float32,
    )
    d_prob = jnp.einsum(
        "qhd,khd->hqk", grad_heads, split_kv[:, :, 1], preferred_element_type=jnp.float32
    )
    d_score = (prob_full * (d_prob - row_dot[:, :, None])).astype(jnp.bfloat16)
    d_query = 0.125 * jnp.einsum(
        "hqk,khd->qhd", d_score, split_kv[:, :, 0], preferred_element_type=jnp.float32
    )
    d_key = 0.125 * jnp.einsum("hqk,qhd->khd", d_score, queries, preferred_element_type=jnp.float32)
    rows = pair_rows.shape[0]
    return (d_query, jnp.stack([d_key, d_value], axis=2).reshape(rows, -1))


def move_keys(pair_rows):
    moved = shifted(pair_rows, "seq", 1)
    return moved


def move_grads(accum):
    moved = shifted(accum.astype(jnp.bfloat16), "seq", 1).astype(accum.dtype)
    return moved


def exchange_bits():
    seq_bits = lax.axis_size("seq").bit_length() - 1
    clip_bits = lax.axis_size("clip").bit_length() - 1
    assert (1 << seq_bits) == lax.axis_size("seq")
    assert (1 << clip_bits) == lax.axis_size("clip")
    return seq_bits, clip_bits


def exchange_order(values):
    seq_bits, clip_bits = exchange_bits()
    total = seq_bits + clip_bits
    lead = values.shape[0]
    split = values.reshape([lead] + [2] * total + [-1])
    seq_dims = [1 + seq_bits - 1 - bit for bit in range(seq_bits)]
    clip_dims = [1 + seq_bits + clip_bits - 1 - bit for bit in range(clip_bits)]
    perm = [0] + seq_dims + clip_dims + [total + 1]
    return split.transpose(perm).reshape(values.shape)


def split_wide(values):
    high = values.astype(jnp.bfloat16)
    low = (values - high.astype(jnp.float32)).astype(jnp.bfloat16)
    return high, low


def halving_round(datas, small, axis, pairs, pick):
    keeps = [pick(data, True) for data in datas]
    gives = [pick(data, False) for data in datas]
    high, low = split_wide(small)
    sizes = [give.size for give in gives]
    packet = jnp.concatenate([give.astype(jnp.bfloat16).reshape(-1) for give in gives] + [high, low])
    got = lax.ppermute(packet, axis, pairs)
    out = []
    start = 0
    for keep, size in zip(keeps, sizes):
        out.append(keep + got[start:start + size].reshape(keep.shape).astype(jnp.float32))
        start += size
    width = small.shape[0]
    mine = high.astype(jnp.float32) + low.astype(jnp.float32)
    theirs = got[start:start + width].astype(jnp.float32) + got[start + width:].astype(jnp.float32)
    return out, mine + theirs


def halving_scatter(grads, small):
    seq_bits, clip_bits = exchange_bits()
    total = seq_bits + clip_bits
    datas = [grad.reshape([2] * total + [-1, grad.shape[1]]) for grad in grads]
    order_a = list(range(seq_bits))
    order_b = [0] + list(range(seq_bits - 1, 0, -1))
    me = lax.axis_index("seq")
    core_bit = me & 1
    left_a = list(range(seq_bits))
    left_b = list(range(seq_bits))
    for step in range(seq_bits):
        bit_a, bit_b = order_a[step], order_b[step]
        dim_a, dim_b = left_a.index(bit_a), left_b.index(bit_b)
        mine_a = (me >> bit_a) & 1
        mine_b = (me >> bit_b) & 1
        pairs = []
        for src in range(lax.axis_size("seq")):
            bit = bit_a if (src & 1) == 0 else bit_b
            pairs.append((src, src ^ (1 << bit)))

        def pick(data, keep, dim_a=dim_a, dim_b=dim_b, mine_a=mine_a, mine_b=mine_b):
            side_a = mine_a if keep else 1 - mine_a
            side_b = mine_b if keep else 1 - mine_b
            return jnp.where(
                core_bit == 0,
                lax.dynamic_index_in_dim(data, side_a, axis=dim_a, keepdims=False),
                lax.dynamic_index_in_dim(data, side_b, axis=dim_b, keepdims=False),
            )

        left_a.pop(dim_a)
        left_b.pop(dim_b)
        datas, small = halving_round(datas, small, "seq", pairs, pick)
    for bit in range(clip_bits):
        mine = (lax.axis_index("clip") >> bit) & 1
        pairs = [(src, src ^ (1 << bit)) for src in range(lax.axis_size("clip"))]

        def pick(data, keep, mine=mine):
            side = mine if keep else 1 - mine
            return lax.dynamic_index_in_dim(data, side, axis=0, keepdims=False)

        datas, small = halving_round(datas, small, "clip", pairs, pick)
    return datas, small


def xor_pairs(mask):
    count = lax.axis_size("seq")
    return [(src, src ^ mask) for src in range(count)]


def gather_blocks(block):
    half = lax.axis_size("seq") // 2
    same_core = [block] + [lax.ppermute(block, "seq", xor_pairs(2 * k)) for k in range(1, half)]
    group = jnp.stack(same_core)
    other = lax.ppermute(group, "seq", xor_pairs(1))
    return jnp.concatenate([group, other], axis=0)


def return_blocks(parts):
    half = lax.axis_size("seq") // 2
    got = lax.ppermute(parts[half:], "seq", xor_pairs(1))
    summed = parts[:half].astype(jnp.float32) + got.astype(jnp.float32)
    accum = summed[0]
    for k in range(1, half):
        sent = lax.ppermute(summed[k].astype(jnp.bfloat16), "seq", xor_pairs(2 * k))
        accum = accum + sent.astype(jnp.float32)
    return accum


def per_device(raw_tokens, teacher, keep_rows, w_qkv, w_out, ln_gain):
    shards = lax.axis_size("seq")
    my_index = lax.axis_index("seq")
    row_ids = keep_rows[0]
    list_slots = row_ids.shape[0]
    is_kept = row_ids >= 0
    kept_count = jnp.sum(is_kept.astype(jnp.int32))
    safe_ids = jnp.maximum(row_ids, 0)
    kept_tokens = jnp.where(is_kept[:, None], raw_tokens[0][safe_ids], jnp.zeros((), jnp.bfloat16))
    kept_target = jnp.where(is_kept[:, None], teacher[0][safe_ids], jnp.zeros((), jnp.bfloat16))
    count_table = lax.all_to_all(
        jnp.broadcast_to(kept_count.reshape(1, 1), (shards, 1)), "seq", 0, 0, tiled=True
    ).reshape(shards)
    shard_ids = jnp.arange(shards, dtype=jnp.int32)
    per_peer = -(-list_slots // shards)
    starts = jnp.cumsum(count_table) - count_table
    before = jnp.sum(jnp.where(shard_ids < my_index, count_table, 0))
    slot_ids = jnp.arange(per_peer, dtype=jnp.int32)
    pick = (shard_ids[:, None] - before) % shards + slot_ids[None, :] * shards
    pick_ok = pick < kept_count
    pick_safe = jnp.minimum(pick, list_slots - 1)
    send_tokens = jnp.where(
        pick_ok[:, :, None], kept_tokens[pick_safe], jnp.zeros((), jnp.bfloat16)
    )
    send_target = jnp.where(
        pick_ok[:, :, None], kept_target[pick_safe], jnp.zeros((), jnp.bfloat16)
    )
    got_tokens, got_target = (
        lax.all_to_all(send_tokens, "seq", split_axis=0, concat_axis=0, tiled=True),
        lax.all_to_all(send_target, "seq", split_axis=0, concat_axis=0, tiled=True),
    )
    from_pick = (my_index - starts[:, None]) % shards + slot_ids[None, :] * shards
    from_ok = from_pick < count_table[:, None]
    place = jnp.where(from_ok, (starts[:, None] + from_pick) // shards, TOK_DEV).reshape(-1)
    width = got_tokens.shape[2]
    tokens = (
        jnp.zeros((TOK_DEV, width), jnp.bfloat16)
        .at[place]
        .set(got_tokens.reshape(-1, width), mode="drop")
    )
    target = (
        jnp.zeros((TOK_DEV, width), jnp.bfloat16)
        .at[place]
        .set(got_target.reshape(-1, width), mode="drop")
    )
    rows = tokens.shape[0]
    inner = w_out.shape[0]
    heads = inner // HEAD_DIM
    normed, hidden = layer_norm(tokens, ln_gain)
    queries = (
        jnp.dot(hidden, w_qkv[:, :inner], preferred_element_type=jnp.float32)
        .astype(jnp.bfloat16)
        .reshape(rows, heads, HEAD_DIM)
        .transpose(1, 0, 2)
    )
    pair_cols = jnp.dot(w_qkv[:, inner:].T, hidden.T, preferred_element_type=jnp.float32).astype(
        jnp.bfloat16
    )
    gathered = gather_blocks(pair_cols)
    split_kv = gathered.reshape(shards, heads, 2, HEAD_DIM, rows)
    keys_b = split_kv[:, :, 0]
    values_b = split_kv[:, :, 1]
    queries_b = jnp.broadcast_to(queries[None], (shards,) + queries.shape)
    scores = (
        jnp.einsum("ihqd,ihdt->ihqt", queries_b, keys_b, preferred_element_type=jnp.float32) * 0.125
    )
    row_max = jnp.max(scores, axis=(0, 3))
    weights = jnp.exp(scores - row_max[None, :, :, None])
    row_sum = jnp.sum(weights, axis=(0, 3))
    blended = jnp.sum(
        jnp.einsum(
            "ihqt,ihdt->ihqd", weights.astype(jnp.bfloat16), values_b, preferred_element_type=jnp.float32
        ),
        axis=0,
    )
    log_total = row_max + jnp.log(row_sum)
    attended = (
        (blended / row_sum[:, :, None]).transpose(1, 0, 2).reshape(rows, inner).astype(jnp.bfloat16)
    )
    student = tokens.astype(jnp.float32) + jnp.dot(
        attended, w_out, preferred_element_type=jnp.float32
    )
    token_loss, grad_y = align_terms(student, target)
    grad_b = grad_y.astype(jnp.bfloat16)
    grad_wout = jnp.dot(exchange_order(attended).T, grad_b, preferred_element_type=jnp.float32)
    grad_heads = (
        jnp.dot(grad_b, w_out.T, preferred_element_type=jnp.float32)
        .astype(jnp.bfloat16)
        .reshape(rows, heads, HEAD_DIM)
        .transpose(1, 0, 2)
    )
    row_dot = jnp.sum(
        grad_heads.astype(jnp.float32)
        * attended.reshape(rows, heads, HEAD_DIM).transpose(1, 0, 2).astype(jnp.float32),
        axis=2,
    )
    prob_full = jnp.exp(scores - log_total[None, :, :, None])
    grad_heads_b = jnp.broadcast_to(grad_heads[None], (shards,) + grad_heads.shape)
    d_value_b = jnp.einsum(
        "ihqd,ihqt->ihdt", grad_heads_b, prob_full.astype(jnp.bfloat16), preferred_element_type=jnp.float32
    )
    d_prob = jnp.einsum("ihqd,ihdt->ihqt", grad_heads_b, values_b, preferred_element_type=jnp.float32)
    d_score = (prob_full * (d_prob - row_dot[None, :, :, None])).astype(jnp.bfloat16)
    d_query_t = 0.125 * jnp.sum(
        jnp.einsum("ihqt,ihdt->ihdq", d_score, keys_b, preferred_element_type=jnp.float32), axis=0
    )
    d_key_b = 0.125 * jnp.einsum(
        "ihqd,ihqt->ihdt", queries_b, d_score, preferred_element_type=jnp.float32
    )
    d_pairs = jnp.stack([d_key_b, d_value_b], axis=2).reshape(shards, 2 * inner, rows).astype(jnp.bfloat16)
    accum = return_blocks(d_pairs)
    d_proj_t = jnp.concatenate([d_query_t.reshape(inner, rows), accum], axis=0).astype(jnp.bfloat16)
    grad_wqkv = jnp.einsum(
        "tf,ct->fc", exchange_order(hidden), d_proj_t, preferred_element_type=jnp.float32
    )
    d_hidden = jnp.einsum("ct,fc->tf", d_proj_t, w_qkv, preferred_element_type=jnp.float32)
    grad_ln = jnp.sum(d_hidden * normed, axis=0)
    loss_part = jnp.sum(token_loss)
    small = jnp.concatenate([grad_ln, loss_part.reshape(1)])
    (grad_qkv, grad_out), small = halving_scatter([grad_wqkv, grad_wout], small)
    count_all = shards * lax.axis_size("clip") * TOK_DEV
    return (small[-1] / count_all, grad_qkv.reshape(-1), grad_out.reshape(-1), small[:-1])


def solution(mesh):
    placed = (P("clip", "seq", None), P("clip", "seq", None), P("clip", "seq"), P(), P(), P())
    return jax.shard_map(
        per_device,
        mesh=mesh,
        in_specs=placed,
        out_specs=(P(), P(("seq", "clip")), P(("seq", "clip")), P()),
        check_vma=False,
    )
```

```python
import jax
import jax.numpy as jnp
from jax import lax
from jax.sharding import PartitionSpec as P

HEAD_DIM = 64
TOK_DEV = 128


def shifted(value, axis, steps):
    count = lax.axis_size(axis)
    pairs = [(source, (source + steps) % count) for source in range(count)]
    return lax.ppermute(value, axis, pairs)


def layer_norm(tokens, ln_gain):
    values = tokens.astype(jnp.float32)
    center = values - jnp.mean(values, axis=-1, keepdims=True)
    spread = jnp.mean(center * center, axis=-1, keepdims=True)
    normed = center * lax.rsqrt(spread + 1e-05)
    return (normed, (normed * ln_gain).astype(jnp.bfloat16))


def align_terms(student, target):
    target_f = target.astype(jnp.float32)
    inv_y = lax.rsqrt(jnp.sum(student * student, axis=-1, keepdims=True) + 1e-06)
    inv_t = lax.rsqrt(jnp.sum(target_f * target_f, axis=-1, keepdims=True) + 1e-06)
    differ = student * inv_y - target_f * inv_t
    token_loss = jnp.sum(differ * differ, axis=-1)
    slopes = 2.0 * differ
    grad_y = inv_y * slopes - student * (inv_y * inv_y * inv_y) * jnp.sum(
        slopes * student, axis=-1, keepdims=True
    )
    return (token_loss, grad_y)


def key_mask(key_count, rows, heads):
    slot_idx = jnp.arange(rows, dtype=jnp.int32)
    halves = slot_idx[None, :] < key_count[:, None]
    return jnp.repeat(halves, heads // 2, axis=0)


def head_scores(queries, pair_rows, key_count):
    rows = pair_rows.shape[0]
    heads = queries.shape[1]
    split_kv = pair_rows.reshape(rows, heads, 2, HEAD_DIM)
    scores = (
        jnp.einsum("qhd,khd->hqk", queries, split_kv[:, :, 0], preferred_element_type=jnp.float32)
        * 0.125
    )
    mask_rows = key_mask(key_count, rows, heads)
    return (jnp.where(mask_rows[:, None, :], scores, -1e30), split_kv)


def absorb(state, queries, pair_rows, key_count):
    row_max, row_sum, blended = state
    scores, split_kv = head_scores(queries, pair_rows, key_count)
    new_max = jnp.maximum(row_max, jnp.max(scores, axis=2))
    rescale = jnp.exp(row_max - new_max)
    weights = jnp.exp(scores - new_max[:, :, None])
    row_sum = row_sum * rescale + jnp.sum(weights, axis=2)
    blended = blended * rescale[:, :, None] + jnp.einsum(
        "hqk,khd->hqd",
        weights.astype(jnp.bfloat16),
        split_kv[:, :, 1],
        preferred_element_type=jnp.float32,
    )
    return (new_max, row_sum, blended)


def contribution(queries, grad_heads, log_total, row_dot, pair_rows, key_count):
    scores, split_kv = head_scores(queries, pair_rows, key_count)
    prob_full = jnp.exp(scores - log_total[:, :, None])
    d_value = jnp.einsum(
        "hqk,qhd->khd",
        prob_full.astype(jnp.bfloat16),
        grad_heads,
        preferred_element_type=jnp.float32,
    )
    d_prob = jnp.einsum(
        "qhd,khd->hqk", grad_heads, split_kv[:, :, 1], preferred_element_type=jnp.float32
    )
    d_score = (prob_full * (d_prob - row_dot[:, :, None])).astype(jnp.bfloat16)
    d_query = 0.125 * jnp.einsum(
        "hqk,khd->qhd", d_score, split_kv[:, :, 0], preferred_element_type=jnp.float32
    )
    d_key = 0.125 * jnp.einsum("hqk,qhd->khd", d_score, queries, preferred_element_type=jnp.float32)
    rows = pair_rows.shape[0]
    return (d_query, jnp.stack([d_key, d_value], axis=2).reshape(rows, -1))


def move_keys(pair_rows):
    moved = shifted(pair_rows, "seq", 1)
    return moved


def move_grads(accum):
    moved = shifted(accum.astype(jnp.bfloat16), "seq", 1).astype(accum.dtype)
    return moved


def exchange_bits():
    seq_bits = lax.axis_size("seq").bit_length() - 1
    clip_bits = lax.axis_size("clip").bit_length() - 1
    assert (1 << seq_bits) == lax.axis_size("seq")
    assert (1 << clip_bits) == lax.axis_size("clip")
    return seq_bits, clip_bits


def exchange_order(values):
    seq_bits, clip_bits = exchange_bits()
    total = seq_bits + clip_bits
    lead = values.shape[0]
    split = values.reshape([lead] + [2] * total + [-1])
    seq_dims = [1 + seq_bits - 1 - bit for bit in range(seq_bits)]
    clip_dims = [1 + seq_bits + clip_bits - 1 - bit for bit in range(clip_bits)]
    perm = [0] + seq_dims + clip_dims + [total + 1]
    return split.transpose(perm).reshape(values.shape)


def halving_scatter(grad, small=None):
    seq_bits, clip_bits = exchange_bits()
    total = seq_bits + clip_bits
    data = grad.reshape([2] * total + [-1, grad.shape[1]])
    order_a = list(range(seq_bits))
    order_b = [0] + list(range(seq_bits - 1, 0, -1))
    core_bit = lax.axis_index("seq") & 1
    left_a = list(range(seq_bits))
    left_b = list(range(seq_bits))
    for step in range(seq_bits):
        bit_a, bit_b = order_a[step], order_b[step]
        dim_a, dim_b = left_a.index(bit_a), left_b.index(bit_b)
        me = lax.axis_index("seq")
        mine_a = (me >> bit_a) & 1
        mine_b = (me >> bit_b) & 1
        pairs = []
        for src in range(lax.axis_size("seq")):
            bit = bit_a if (src & 1) == 0 else bit_b
            pairs.append((src, src ^ (1 << bit)))
        keep = jnp.where(
            core_bit == 0,
            lax.dynamic_index_in_dim(data, mine_a, axis=dim_a, keepdims=False),
            lax.dynamic_index_in_dim(data, mine_b, axis=dim_b, keepdims=False),
        )
        give = jnp.where(
            core_bit == 0,
            lax.dynamic_index_in_dim(data, 1 - mine_a, axis=dim_a, keepdims=False),
            lax.dynamic_index_in_dim(data, 1 - mine_b, axis=dim_b, keepdims=False),
        )
        left_a.pop(dim_a)
        left_b.pop(dim_b)
        if small is None:
            got = lax.ppermute(give.astype(jnp.bfloat16), "seq", pairs)
        else:
            got, got_small = lax.ppermute((give.astype(jnp.bfloat16), small), "seq", pairs)
            small = small + got_small
        data = keep + got.astype(jnp.float32)
    for bit in range(clip_bits):
        mine = (lax.axis_index("clip") >> bit) & 1
        pairs = [(src, src ^ (1 << bit)) for src in range(lax.axis_size("clip"))]
        keep = lax.dynamic_index_in_dim(data, mine, axis=0, keepdims=False)
        give = lax.dynamic_index_in_dim(data, 1 - mine, axis=0, keepdims=False)
        if small is None:
            got = lax.ppermute(give.astype(jnp.bfloat16), "clip", pairs)
        else:
            got, got_small = lax.ppermute((give.astype(jnp.bfloat16), small), "clip", pairs)
            small = small + got_small
        data = keep + got.astype(jnp.float32)
    return data, small


def xor_pairs(mask):
    count = lax.axis_size("seq")
    return [(src, src ^ mask) for src in range(count)]


def gather_blocks(block):
    half = lax.axis_size("seq") // 2
    same_core = [block] + [lax.ppermute(block, "seq", xor_pairs(2 * k)) for k in range(1, half)]
    group = jnp.stack(same_core)
    other = lax.ppermute(group, "seq", xor_pairs(1))
    return jnp.concatenate([group, other], axis=0)


def return_blocks(own_parts, other_parts):
    half = lax.axis_size("seq") // 2
    got = lax.ppermute(other_parts, "seq", xor_pairs(1))
    summed = own_parts.astype(jnp.bfloat16).astype(jnp.float32) + got.astype(jnp.float32)
    accum = summed[0]
    for k in range(1, half):
        sent = lax.ppermute(summed[k].astype(jnp.bfloat16), "seq", xor_pairs(2 * k))
        accum = accum + sent.astype(jnp.float32)
    return accum


def per_device(raw_tokens, teacher, keep_rows, w_qkv, w_out, ln_gain):
    shards = lax.axis_size("seq")
    my_index = lax.axis_index("seq")
    row_ids = keep_rows[0]
    list_slots = row_ids.shape[0]
    is_kept = row_ids >= 0
    kept_count = jnp.sum(is_kept.astype(jnp.int32))
    safe_ids = jnp.maximum(row_ids, 0)
    kept_tokens = jnp.where(is_kept[:, None], raw_tokens[0][safe_ids], jnp.zeros((), jnp.bfloat16))
    kept_target = jnp.where(is_kept[:, None], teacher[0][safe_ids], jnp.zeros((), jnp.bfloat16))
    count_table = lax.all_to_all(
        jnp.broadcast_to(kept_count.reshape(1, 1), (shards, 1)), "seq", 0, 0, tiled=True
    ).reshape(shards)
    shard_ids = jnp.arange(shards, dtype=jnp.int32)
    per_peer = -(-list_slots // shards)
    starts = jnp.cumsum(count_table) - count_table
    before = jnp.sum(jnp.where(shard_ids < my_index, count_table, 0))
    slot_ids = jnp.arange(per_peer, dtype=jnp.int32)
    pick = (shard_ids[:, None] - before) % shards + slot_ids[None, :] * shards
    pick_ok = pick < kept_count
    pick_safe = jnp.minimum(pick, list_slots - 1)
    send_tokens = jnp.where(
        pick_ok[:, :, None], kept_tokens[pick_safe], jnp.zeros((), jnp.bfloat16)
    )
    send_target = jnp.where(
        pick_ok[:, :, None], kept_target[pick_safe], jnp.zeros((), jnp.bfloat16)
    )
    got_tokens = lax.all_to_all(send_tokens, "seq", split_axis=0, concat_axis=0, tiled=True)
    from_pick = (my_index - starts[:, None]) % shards + slot_ids[None, :] * shards
    from_ok = from_pick < count_table[:, None]
    place = jnp.where(from_ok, (starts[:, None] + from_pick) // shards, TOK_DEV).reshape(-1)
    width = got_tokens.shape[2]
    tokens = (
        jnp.zeros((TOK_DEV, width), jnp.bfloat16)
        .at[place]
        .set(got_tokens.reshape(-1, width), mode="drop")
    )
    rows = tokens.shape[0]
    inner = w_out.shape[0]
    heads = inner // HEAD_DIM
    normed, hidden = layer_norm(tokens, ln_gain)
    queries = (
        jnp.dot(hidden, w_qkv[:, :inner], preferred_element_type=jnp.float32)
        .astype(jnp.bfloat16)
        .reshape(rows, heads, HEAD_DIM)
        .transpose(1, 0, 2)
    )
    pair_cols = jnp.dot(w_qkv[:, inner:].T, hidden.T, preferred_element_type=jnp.float32).astype(
        jnp.bfloat16
    )
    gathered = gather_blocks(pair_cols)
    send_target, gathered = lax.optimization_barrier((send_target, gathered))
    got_target = lax.all_to_all(send_target, "seq", split_axis=0, concat_axis=0, tiled=True)
    target = (
        jnp.zeros((TOK_DEV, width), jnp.bfloat16)
        .at[place]
        .set(got_target.reshape(-1, width), mode="drop")
    )
    split_kv = gathered.reshape(shards, heads, 2, HEAD_DIM, rows)
    keys_b = split_kv[:, :, 0]
    values_b = split_kv[:, :, 1]
    queries_b = jnp.broadcast_to(queries[None], (shards,) + queries.shape)
    scores = (
        jnp.einsum("ihqd,ihdt->ihqt", queries_b, keys_b, preferred_element_type=jnp.float32) * 0.125
    )
    row_max = jnp.max(scores, axis=(0, 3))
    weights = jnp.exp(scores - row_max[None, :, :, None])
    row_sum = jnp.sum(weights, axis=(0, 3))
    blended = jnp.sum(
        jnp.einsum(
            "ihqt,ihdt->ihqd", weights.astype(jnp.bfloat16), values_b, preferred_element_type=jnp.float32
        ),
        axis=0,
    )
    log_total = row_max + jnp.log(row_sum)
    attended = (
        (blended / row_sum[:, :, None]).transpose(1, 0, 2).reshape(rows, inner).astype(jnp.bfloat16)
    )
    student = tokens.astype(jnp.float32) + jnp.dot(
        attended, w_out, preferred_element_type=jnp.float32
    )
    token_loss, grad_y = align_terms(student, target)
    grad_b = grad_y.astype(jnp.bfloat16)
    grad_wout = jnp.dot(exchange_order(attended).T, grad_b, preferred_element_type=jnp.float32)
    grad_heads = (
        jnp.dot(grad_b, w_out.T, preferred_element_type=jnp.float32)
        .astype(jnp.bfloat16)
        .reshape(rows, heads, HEAD_DIM)
        .transpose(1, 0, 2)
    )
    row_dot = jnp.sum(
        grad_heads.astype(jnp.float32)
        * attended.reshape(rows, heads, HEAD_DIM).transpose(1, 0, 2).astype(jnp.float32),
        axis=2,
    )
    prob_full = jnp.exp(scores - log_total[None, :, :, None])
    grad_heads_b = jnp.broadcast_to(grad_heads[None], (shards,) + grad_heads.shape)
    d_value_b = jnp.einsum(
        "ihqd,ihqt->ihdt", grad_heads_b, prob_full.astype(jnp.bfloat16), preferred_element_type=jnp.float32
    )
    d_prob = jnp.einsum("ihqd,ihdt->ihqt", grad_heads_b, values_b, preferred_element_type=jnp.float32)
    d_score = (prob_full * (d_prob - row_dot[None, :, :, None])).astype(jnp.bfloat16)
    d_query_t = 0.125 * jnp.sum(
        jnp.einsum("ihqt,ihdt->ihdq", d_score, keys_b, preferred_element_type=jnp.float32), axis=0
    )
    d_key_b = 0.125 * jnp.einsum(
        "ihqd,ihqt->ihdt", queries_b, d_score, preferred_element_type=jnp.float32
    )
    half = shards // 2
    own_pairs = jnp.stack([d_key_b[:half], d_value_b[:half]], axis=2).reshape(half, 2 * inner, rows)
    other_pairs = jnp.stack([d_key_b[half:], d_value_b[half:]], axis=2).reshape(half, 2 * inner, rows)
    accum = return_blocks(own_pairs, other_pairs.astype(jnp.bfloat16))
    d_proj_t = jnp.concatenate([d_query_t.reshape(inner, rows), accum], axis=0).astype(jnp.bfloat16)
    grad_wqkv = jnp.einsum(
        "tf,ct->fc", exchange_order(hidden), d_proj_t, preferred_element_type=jnp.float32
    )
    d_hidden = jnp.einsum("ct,fc->tf", d_proj_t, w_qkv, preferred_element_type=jnp.float32)
    grad_ln = jnp.sum(d_hidden * normed, axis=0)
    loss_part = jnp.sum(token_loss)
    small = jnp.concatenate([grad_ln, loss_part.reshape(1)])
    grad_out, unused = halving_scatter(grad_wout)
    grad_qkv, small = halving_scatter(grad_wqkv, small)
    count_all = shards * lax.axis_size("clip") * TOK_DEV
    return (small[-1] / count_all, grad_qkv.reshape(-1), grad_out.reshape(-1), small[:-1])


def solution(mesh):
    placed = (P("clip", "seq", None), P("clip", "seq", None), P("clip", "seq"), P(), P(), P())
    return jax.shard_map(
        per_device,
        mesh=mesh,
        in_specs=placed,
        out_specs=(P(), P(("seq", "clip")), P(("seq", "clip")), P()),
        check_vma=False,
    )
```

```python
import jax
import jax.numpy as jnp
from jax import lax
from jax.sharding import PartitionSpec as P
from jax.experimental.layout import Layout, with_layout_constraint

HEAD_DIM = 64
TOK_DEV = 128


def shifted(value, axis, steps):
    count = lax.axis_size(axis)
    pairs = [(source, (source + steps) % count) for source in range(count)]
    return lax.ppermute(value, axis, pairs)


def layer_norm(tokens, ln_gain):
    values = tokens.astype(jnp.float32)
    center = values - jnp.mean(values, axis=-1, keepdims=True)
    spread = jnp.mean(center * center, axis=-1, keepdims=True)
    normed = center * lax.rsqrt(spread + 1e-05)
    return (normed, (normed * ln_gain).astype(jnp.bfloat16))


def align_terms(student, target):
    target_f = target.astype(jnp.float32)
    inv_y = lax.rsqrt(jnp.sum(student * student, axis=-1, keepdims=True) + 1e-06)
    inv_t = lax.rsqrt(jnp.sum(target_f * target_f, axis=-1, keepdims=True) + 1e-06)
    differ = student * inv_y - target_f * inv_t
    token_loss = jnp.sum(differ * differ, axis=-1)
    slopes = 2.0 * differ
    grad_y = inv_y * slopes - student * (inv_y * inv_y * inv_y) * jnp.sum(
        slopes * student, axis=-1, keepdims=True
    )
    return (token_loss, grad_y)


def key_mask(key_count, rows, heads):
    slot_idx = jnp.arange(rows, dtype=jnp.int32)
    halves = slot_idx[None, :] < key_count[:, None]
    return jnp.repeat(halves, heads // 2, axis=0)


def head_scores(queries, pair_rows, key_count):
    rows = pair_rows.shape[0]
    heads = queries.shape[1]
    split_kv = pair_rows.reshape(rows, heads, 2, HEAD_DIM)
    scores = (
        jnp.einsum("qhd,khd->hqk", queries, split_kv[:, :, 0], preferred_element_type=jnp.float32)
        * 0.125
    )
    mask_rows = key_mask(key_count, rows, heads)
    return (jnp.where(mask_rows[:, None, :], scores, -1e30), split_kv)


def absorb(state, queries, pair_rows, key_count):
    row_max, row_sum, blended = state
    scores, split_kv = head_scores(queries, pair_rows, key_count)
    new_max = jnp.maximum(row_max, jnp.max(scores, axis=2))
    rescale = jnp.exp(row_max - new_max)
    weights = jnp.exp(scores - new_max[:, :, None])
    row_sum = row_sum * rescale + jnp.sum(weights, axis=2)
    blended = blended * rescale[:, :, None] + jnp.einsum(
        "hqk,khd->hqd",
        weights.astype(jnp.bfloat16),
        split_kv[:, :, 1],
        preferred_element_type=jnp.float32,
    )
    return (new_max, row_sum, blended)


def contribution(queries, grad_heads, log_total, row_dot, pair_rows, key_count):
    scores, split_kv = head_scores(queries, pair_rows, key_count)
    prob_full = jnp.exp(scores - log_total[:, :, None])
    d_value = jnp.einsum(
        "hqk,qhd->khd",
        prob_full.astype(jnp.bfloat16),
        grad_heads,
        preferred_element_type=jnp.float32,
    )
    d_prob = jnp.einsum(
        "qhd,khd->hqk", grad_heads, split_kv[:, :, 1], preferred_element_type=jnp.float32
    )
    d_score = (prob_full * (d_prob - row_dot[:, :, None])).astype(jnp.bfloat16)
    d_query = 0.125 * jnp.einsum(
        "hqk,khd->qhd", d_score, split_kv[:, :, 0], preferred_element_type=jnp.float32
    )
    d_key = 0.125 * jnp.einsum("hqk,qhd->khd", d_score, queries, preferred_element_type=jnp.float32)
    rows = pair_rows.shape[0]
    return (d_query, jnp.stack([d_key, d_value], axis=2).reshape(rows, -1))


def move_keys(pair_rows):
    moved = shifted(pair_rows, "seq", 1)
    return moved


def move_grads(accum):
    moved = shifted(accum.astype(jnp.bfloat16), "seq", 1).astype(accum.dtype)
    return moved


def exchange_bits():
    seq_bits = lax.axis_size("seq").bit_length() - 1
    clip_bits = lax.axis_size("clip").bit_length() - 1
    assert (1 << seq_bits) == lax.axis_size("seq")
    assert (1 << clip_bits) == lax.axis_size("clip")
    return seq_bits, clip_bits


def exchange_order(values):
    seq_bits, clip_bits = exchange_bits()
    total = seq_bits + clip_bits
    lead = values.shape[0]
    split = values.reshape([lead] + [2] * total + [-1])
    seq_dims = [1 + seq_bits - 1 - bit for bit in range(seq_bits)]
    clip_dims = [1 + seq_bits + clip_bits - 1 - bit for bit in range(clip_bits)]
    perm = [0] + seq_dims + clip_dims + [total + 1]
    return split.transpose(perm).reshape(values.shape)


def halving_scatter(grad, small=None):
    seq_bits, clip_bits = exchange_bits()
    total = seq_bits + clip_bits
    data = grad.reshape([2] * total + [-1, grad.shape[1]])
    order_a = list(range(seq_bits))
    order_b = [0] + list(range(seq_bits - 1, 0, -1))
    core_bit = lax.axis_index("seq") & 1
    left_a = list(range(seq_bits))
    left_b = list(range(seq_bits))
    for step in range(seq_bits):
        bit_a, bit_b = order_a[step], order_b[step]
        dim_a, dim_b = left_a.index(bit_a), left_b.index(bit_b)
        me = lax.axis_index("seq")
        mine_a = (me >> bit_a) & 1
        mine_b = (me >> bit_b) & 1
        pairs = []
        for src in range(lax.axis_size("seq")):
            bit = bit_a if (src & 1) == 0 else bit_b
            pairs.append((src, src ^ (1 << bit)))
        keep = jnp.where(
            core_bit == 0,
            lax.dynamic_index_in_dim(data, mine_a, axis=dim_a, keepdims=False),
            lax.dynamic_index_in_dim(data, mine_b, axis=dim_b, keepdims=False),
        )
        give = jnp.where(
            core_bit == 0,
            lax.dynamic_index_in_dim(data, 1 - mine_a, axis=dim_a, keepdims=False),
            lax.dynamic_index_in_dim(data, 1 - mine_b, axis=dim_b, keepdims=False),
        )
        left_a.pop(dim_a)
        left_b.pop(dim_b)
        if small is None:
            got = lax.ppermute(give.astype(jnp.bfloat16), "seq", pairs)
        else:
            got, got_small = lax.ppermute((give.astype(jnp.bfloat16), small), "seq", pairs)
            small = small + got_small
        data = keep + got.astype(jnp.float32)
    for bit in range(clip_bits):
        mine = (lax.axis_index("clip") >> bit) & 1
        pairs = [(src, src ^ (1 << bit)) for src in range(lax.axis_size("clip"))]
        keep = lax.dynamic_index_in_dim(data, mine, axis=0, keepdims=False)
        give = lax.dynamic_index_in_dim(data, 1 - mine, axis=0, keepdims=False)
        if small is None:
            got = lax.ppermute(give.astype(jnp.bfloat16), "clip", pairs)
        else:
            got, got_small = lax.ppermute((give.astype(jnp.bfloat16), small), "clip", pairs)
            small = small + got_small
        data = keep + got.astype(jnp.float32)
    return data, small


def xor_pairs(mask):
    count = lax.axis_size("seq")
    return [(src, src ^ mask) for src in range(count)]


def gather_blocks(block):
    half = lax.axis_size("seq") // 2
    same_core = [block] + [lax.ppermute(block, "seq", xor_pairs(2 * k)) for k in range(1, half)]
    group = jnp.stack(same_core)
    other = lax.ppermute(group, "seq", xor_pairs(1))
    return jnp.concatenate([group, other], axis=0)


def return_blocks(own_parts, other_parts):
    half = lax.axis_size("seq") // 2
    got = lax.ppermute(other_parts, "seq", xor_pairs(1))
    summed = own_parts.astype(jnp.bfloat16).astype(jnp.float32) + got.astype(jnp.float32)
    accum = summed[0]
    for k in range(1, half):
        sent = lax.ppermute(summed[k].astype(jnp.bfloat16), "seq", xor_pairs(2 * k))
        accum = accum + sent.astype(jnp.float32)
    return accum


def per_device(raw_tokens, teacher, keep_rows, w_qkv, w_out, ln_gain):
    shards = lax.axis_size("seq")
    my_index = lax.axis_index("seq")
    row_ids = keep_rows[0]
    list_slots = row_ids.shape[0]
    is_kept = row_ids >= 0
    kept_count = jnp.sum(is_kept.astype(jnp.int32))
    safe_ids = jnp.maximum(row_ids, 0)
    kept_tokens = jnp.where(is_kept[:, None], raw_tokens[0][safe_ids], jnp.zeros((), jnp.bfloat16))
    kept_target = jnp.where(is_kept[:, None], teacher[0][safe_ids], jnp.zeros((), jnp.bfloat16))
    count_table = lax.all_to_all(
        jnp.broadcast_to(kept_count.reshape(1, 1), (shards, 1)), "seq", 0, 0, tiled=True
    ).reshape(shards)
    shard_ids = jnp.arange(shards, dtype=jnp.int32)
    per_peer = -(-list_slots // shards)
    starts = jnp.cumsum(count_table) - count_table
    before = jnp.sum(jnp.where(shard_ids < my_index, count_table, 0))
    slot_ids = jnp.arange(per_peer, dtype=jnp.int32)
    pick = (shard_ids[:, None] - before) % shards + slot_ids[None, :] * shards
    pick_ok = pick < kept_count
    pick_safe = jnp.minimum(pick, list_slots - 1)
    send_tokens = jnp.where(
        pick_ok[:, :, None], kept_tokens[pick_safe], jnp.zeros((), jnp.bfloat16)
    )
    send_target = jnp.where(
        pick_ok[:, :, None], kept_target[pick_safe], jnp.zeros((), jnp.bfloat16)
    )
    got_tokens = lax.all_to_all(send_tokens, "seq", split_axis=0, concat_axis=0, tiled=True)
    from_pick = (my_index - starts[:, None]) % shards + slot_ids[None, :] * shards
    from_ok = from_pick < count_table[:, None]
    place = jnp.where(from_ok, (starts[:, None] + from_pick) // shards, TOK_DEV).reshape(-1)
    width = got_tokens.shape[2]
    tokens = (
        jnp.zeros((TOK_DEV, width), jnp.bfloat16)
        .at[place]
        .set(got_tokens.reshape(-1, width), mode="drop")
    )
    rows = tokens.shape[0]
    inner = w_out.shape[0]
    heads = inner // HEAD_DIM
    normed, hidden = layer_norm(tokens, ln_gain)
    queries = (
        jnp.dot(hidden, w_qkv[:, :inner], preferred_element_type=jnp.float32)
        .astype(jnp.bfloat16)
        .reshape(rows, heads, HEAD_DIM)
        .transpose(1, 0, 2)
    )
    pair_cols = jnp.dot(w_qkv[:, inner:].T, hidden.T, preferred_element_type=jnp.float32).astype(
        jnp.bfloat16
    )
    pair_cols = with_layout_constraint(pair_cols, Layout(major_to_minor=(0, 1)))
    gathered = gather_blocks(pair_cols)
    send_target, gathered = lax.optimization_barrier((send_target, gathered))
    got_target = lax.all_to_all(send_target, "seq", split_axis=0, concat_axis=0, tiled=True)
    target = (
        jnp.zeros((TOK_DEV, width), jnp.bfloat16)
        .at[place]
        .set(got_target.reshape(-1, width), mode="drop")
    )
    split_kv = gathered.reshape(shards, heads, 2, HEAD_DIM, rows)
    keys_b = split_kv[:, :, 0]
    values_b = split_kv[:, :, 1]
    queries_b = jnp.broadcast_to(queries[None], (shards,) + queries.shape)
    scores = (
        jnp.einsum("ihqd,ihdt->ihqt", queries_b, keys_b, preferred_element_type=jnp.float32) * 0.125
    )
    row_max = jnp.max(scores, axis=(0, 3))
    weights = jnp.exp(scores - row_max[None, :, :, None])
    row_sum = jnp.sum(weights, axis=(0, 3))
    blended = jnp.sum(
        jnp.einsum(
            "ihqt,ihdt->ihqd", weights.astype(jnp.bfloat16), values_b, preferred_element_type=jnp.float32
        ),
        axis=0,
    )
    log_total = row_max + jnp.log(row_sum)
    attended = (
        (blended / row_sum[:, :, None]).transpose(1, 0, 2).reshape(rows, inner).astype(jnp.bfloat16)
    )
    student = tokens.astype(jnp.float32) + jnp.dot(
        attended, w_out, preferred_element_type=jnp.float32
    )
    token_loss, grad_y = align_terms(student, target)
    grad_b = grad_y.astype(jnp.bfloat16)
    grad_wout = jnp.dot(exchange_order(attended).T, grad_b, preferred_element_type=jnp.float32)
    grad_heads = (
        jnp.dot(grad_b, w_out.T, preferred_element_type=jnp.float32)
        .astype(jnp.bfloat16)
        .reshape(rows, heads, HEAD_DIM)
        .transpose(1, 0, 2)
    )
    row_dot = jnp.sum(
        grad_heads.astype(jnp.float32)
        * attended.reshape(rows, heads, HEAD_DIM).transpose(1, 0, 2).astype(jnp.float32),
        axis=2,
    )
    prob_full = jnp.exp(scores - log_total[None, :, :, None])
    grad_heads_b = jnp.broadcast_to(grad_heads[None], (shards,) + grad_heads.shape)
    d_value_b = jnp.einsum(
        "ihqd,ihqt->ihdt", grad_heads_b, prob_full.astype(jnp.bfloat16), preferred_element_type=jnp.float32
    )
    d_prob = jnp.einsum("ihqd,ihdt->ihqt", grad_heads_b, values_b, preferred_element_type=jnp.float32)
    d_score = (prob_full * (d_prob - row_dot[None, :, :, None])).astype(jnp.bfloat16)
    d_query_t = 0.125 * jnp.sum(
        jnp.einsum("ihqt,ihdt->ihdq", d_score, keys_b, preferred_element_type=jnp.float32), axis=0
    )
    d_key_b = 0.125 * jnp.einsum(
        "ihqd,ihqt->ihdt", queries_b, d_score, preferred_element_type=jnp.float32
    )
    half = shards // 2
    own_pairs = jnp.stack([d_key_b[:half], d_value_b[:half]], axis=2).reshape(half, 2 * inner, rows)
    other_pairs = jnp.stack([d_key_b[half:], d_value_b[half:]], axis=2).reshape(half, 2 * inner, rows)
    accum = return_blocks(own_pairs, other_pairs.astype(jnp.bfloat16))
    d_proj_t = jnp.concatenate([d_query_t.reshape(inner, rows), accum], axis=0).astype(jnp.bfloat16)
    grad_wqkv = jnp.einsum(
        "tf,ct->fc", exchange_order(hidden), d_proj_t, preferred_element_type=jnp.float32
    )
    d_hidden = jnp.einsum("ct,fc->tf", d_proj_t, w_qkv, preferred_element_type=jnp.float32)
    grad_ln = jnp.sum(d_hidden * normed, axis=0)
    loss_part = jnp.sum(token_loss)
    small = jnp.concatenate([grad_ln, loss_part.reshape(1)])
    grad_out, unused = halving_scatter(grad_wout)
    grad_qkv, small = halving_scatter(grad_wqkv, small)
    count_all = shards * lax.axis_size("clip") * TOK_DEV
    return (small[-1] / count_all, grad_qkv.reshape(-1), grad_out.reshape(-1), small[:-1])


def solution(mesh):
    placed = (P("clip", "seq", None), P("clip", "seq", None), P("clip", "seq"), P(), P(), P())
    return jax.shard_map(
        per_device,
        mesh=mesh,
        in_specs=placed,
        out_specs=(P(), P(("seq", "clip")), P(("seq", "clip")), P()),
        check_vma=False,
    )
```

```python
import jax
import jax.numpy as jnp
from jax import lax
from jax.sharding import PartitionSpec as P

HEAD_DIM = 64
TOK_DEV = 128


def shifted(value, axis, steps):
    count = lax.axis_size(axis)
    pairs = [(source, (source + steps) % count) for source in range(count)]
    return lax.ppermute(value, axis, pairs)


def layer_norm(tokens, ln_gain):
    values = tokens.astype(jnp.float32)
    center = values - jnp.mean(values, axis=-1, keepdims=True)
    spread = jnp.mean(center * center, axis=-1, keepdims=True)
    normed = center * lax.rsqrt(spread + 1e-05)
    return (normed, (normed * ln_gain).astype(jnp.bfloat16))


def align_terms(student, target):
    target_f = target.astype(jnp.float32)
    inv_y = lax.rsqrt(jnp.sum(student * student, axis=-1, keepdims=True) + 1e-06)
    inv_t = lax.rsqrt(jnp.sum(target_f * target_f, axis=-1, keepdims=True) + 1e-06)
    differ = student * inv_y - target_f * inv_t
    token_loss = jnp.sum(differ * differ, axis=-1)
    slopes = 2.0 * differ
    grad_y = inv_y * slopes - student * (inv_y * inv_y * inv_y) * jnp.sum(
        slopes * student, axis=-1, keepdims=True
    )
    return (token_loss, grad_y)


def key_mask(key_count, rows, heads):
    slot_idx = jnp.arange(rows, dtype=jnp.int32)
    halves = slot_idx[None, :] < key_count[:, None]
    return jnp.repeat(halves, heads // 2, axis=0)


def head_scores(queries, pair_rows, key_count):
    rows = pair_rows.shape[0]
    heads = queries.shape[1]
    split_kv = pair_rows.reshape(rows, heads, 2, HEAD_DIM)
    scores = (
        jnp.einsum("qhd,khd->hqk", queries, split_kv[:, :, 0], preferred_element_type=jnp.float32)
        * 0.125
    )
    mask_rows = key_mask(key_count, rows, heads)
    return (jnp.where(mask_rows[:, None, :], scores, -1e30), split_kv)


def absorb(state, queries, pair_rows, key_count):
    row_max, row_sum, blended = state
    scores, split_kv = head_scores(queries, pair_rows, key_count)
    new_max = jnp.maximum(row_max, jnp.max(scores, axis=2))
    rescale = jnp.exp(row_max - new_max)
    weights = jnp.exp(scores - new_max[:, :, None])
    row_sum = row_sum * rescale + jnp.sum(weights, axis=2)
    blended = blended * rescale[:, :, None] + jnp.einsum(
        "hqk,khd->hqd",
        weights.astype(jnp.bfloat16),
        split_kv[:, :, 1],
        preferred_element_type=jnp.float32,
    )
    return (new_max, row_sum, blended)


def contribution(queries, grad_heads, log_total, row_dot, pair_rows, key_count):
    scores, split_kv = head_scores(queries, pair_rows, key_count)
    prob_full = jnp.exp(scores - log_total[:, :, None])
    d_value = jnp.einsum(
        "hqk,qhd->khd",
        prob_full.astype(jnp.bfloat16),
        grad_heads,
        preferred_element_type=jnp.float32,
    )
    d_prob = jnp.einsum(
        "qhd,khd->hqk", grad_heads, split_kv[:, :, 1], preferred_element_type=jnp.float32
    )
    d_score = (prob_full * (d_prob - row_dot[:, :, None])).astype(jnp.bfloat16)
    d_query = 0.125 * jnp.einsum(
        "hqk,khd->qhd", d_score, split_kv[:, :, 0], preferred_element_type=jnp.float32
    )
    d_key = 0.125 * jnp.einsum("hqk,qhd->khd", d_score, queries, preferred_element_type=jnp.float32)
    rows = pair_rows.shape[0]
    return (d_query, jnp.stack([d_key, d_value], axis=2).reshape(rows, -1))


def move_keys(pair_rows):
    moved = shifted(pair_rows, "seq", 1)
    return moved


def move_grads(accum):
    moved = shifted(accum.astype(jnp.bfloat16), "seq", 1).astype(accum.dtype)
    return moved


def exchange_bits():
    seq_bits = lax.axis_size("seq").bit_length() - 1
    clip_bits = lax.axis_size("clip").bit_length() - 1
    assert (1 << seq_bits) == lax.axis_size("seq")
    assert (1 << clip_bits) == lax.axis_size("clip")
    return seq_bits, clip_bits


def exchange_order(values):
    seq_bits, clip_bits = exchange_bits()
    total = seq_bits + clip_bits
    lead = values.shape[0]
    split = values.reshape([lead] + [2] * total + [-1])
    seq_dims = [1 + seq_bits - 1 - bit for bit in range(seq_bits)]
    clip_dims = [1 + seq_bits + clip_bits - 1 - bit for bit in range(clip_bits)]
    perm = [0] + seq_dims + clip_dims + [total + 1]
    return split.transpose(perm).reshape(values.shape)


def halving_scatter(grad, small=None):
    seq_bits, clip_bits = exchange_bits()
    total = seq_bits + clip_bits
    data = grad.reshape([2] * total + [-1, grad.shape[1]])
    order_a = list(range(seq_bits))
    order_b = [0] + list(range(seq_bits - 1, 0, -1))
    core_bit = lax.axis_index("seq") & 1
    left_a = list(range(seq_bits))
    left_b = list(range(seq_bits))
    for step in range(seq_bits):
        bit_a, bit_b = order_a[step], order_b[step]
        dim_a, dim_b = left_a.index(bit_a), left_b.index(bit_b)
        me = lax.axis_index("seq")
        mine_a = (me >> bit_a) & 1
        mine_b = (me >> bit_b) & 1
        pairs = []
        for src in range(lax.axis_size("seq")):
            bit = bit_a if (src & 1) == 0 else bit_b
            pairs.append((src, src ^ (1 << bit)))
        keep = jnp.where(
            core_bit == 0,
            lax.dynamic_index_in_dim(data, mine_a, axis=dim_a, keepdims=False),
            lax.dynamic_index_in_dim(data, mine_b, axis=dim_b, keepdims=False),
        )
        give = jnp.where(
            core_bit == 0,
            lax.dynamic_index_in_dim(data, 1 - mine_a, axis=dim_a, keepdims=False),
            lax.dynamic_index_in_dim(data, 1 - mine_b, axis=dim_b, keepdims=False),
        )
        left_a.pop(dim_a)
        left_b.pop(dim_b)
        if small is None:
            got = lax.ppermute(give.astype(jnp.bfloat16), "seq", pairs)
        else:
            got, got_small = lax.ppermute((give.astype(jnp.bfloat16), small), "seq", pairs)
            small = small + got_small
        data = keep + got.astype(jnp.float32)
    for bit in range(clip_bits):
        mine = (lax.axis_index("clip") >> bit) & 1
        pairs = [(src, src ^ (1 << bit)) for src in range(lax.axis_size("clip"))]
        keep = lax.dynamic_index_in_dim(data, mine, axis=0, keepdims=False)
        give = lax.dynamic_index_in_dim(data, 1 - mine, axis=0, keepdims=False)
        if small is None:
            got = lax.ppermute(give.astype(jnp.bfloat16), "clip", pairs)
        else:
            got, got_small = lax.ppermute((give.astype(jnp.bfloat16), small), "clip", pairs)
            small = small + got_small
        data = keep + got.astype(jnp.float32)
    return data, small


def xor_pairs(mask):
    count = lax.axis_size("seq")
    return [(src, src ^ mask) for src in range(count)]


def gather_blocks(block):
    half = lax.axis_size("seq") // 2
    same_core = [block] + [lax.ppermute(block, "seq", xor_pairs(2 * k)) for k in range(1, half)]
    group = jnp.stack(same_core)
    other = lax.ppermute(group, "seq", xor_pairs(1))
    return jnp.concatenate([group, other], axis=0)


def return_blocks(own_parts, other_parts):
    half = lax.axis_size("seq") // 2
    got = lax.ppermute(other_parts, "seq", xor_pairs(1))
    summed = own_parts.astype(jnp.bfloat16).astype(jnp.float32) + got.astype(jnp.float32)
    accum = summed[0]
    for k in range(1, half):
        sent = lax.ppermute(summed[k].astype(jnp.bfloat16), "seq", xor_pairs(2 * k))
        accum = accum + sent.astype(jnp.float32)
    return accum


def per_device(raw_tokens, teacher, keep_rows, w_qkv, w_out, ln_gain):
    shards = lax.axis_size("seq")
    my_index = lax.axis_index("seq")
    row_ids = keep_rows[0]
    list_slots = row_ids.shape[0]
    is_kept = row_ids >= 0
    kept_count = jnp.sum(is_kept.astype(jnp.int32))
    safe_ids = jnp.maximum(row_ids, 0)
    kept_tokens = jnp.where(is_kept[:, None], raw_tokens[0][safe_ids], jnp.zeros((), jnp.bfloat16))
    kept_target = jnp.where(is_kept[:, None], teacher[0][safe_ids], jnp.zeros((), jnp.bfloat16))
    count_table = lax.all_to_all(
        jnp.broadcast_to(kept_count.reshape(1, 1), (shards, 1)), "seq", 0, 0, tiled=True
    ).reshape(shards)
    shard_ids = jnp.arange(shards, dtype=jnp.int32)
    per_peer = -(-list_slots // shards)
    starts = jnp.cumsum(count_table) - count_table
    before = jnp.sum(jnp.where(shard_ids < my_index, count_table, 0))
    slot_ids = jnp.arange(per_peer, dtype=jnp.int32)
    pick = (shard_ids[:, None] - before) % shards + slot_ids[None, :] * shards
    pick_ok = pick < kept_count
    pick_safe = jnp.minimum(pick, list_slots - 1)
    send_tokens = jnp.where(
        pick_ok[:, :, None], kept_tokens[pick_safe], jnp.zeros((), jnp.bfloat16)
    )
    send_target = jnp.where(
        pick_ok[:, :, None], kept_target[pick_safe], jnp.zeros((), jnp.bfloat16)
    )
    got_tokens = lax.all_to_all(send_tokens, "seq", split_axis=0, concat_axis=0, tiled=True)
    from_pick = (my_index - starts[:, None]) % shards + slot_ids[None, :] * shards
    from_ok = from_pick < count_table[:, None]
    place = jnp.where(from_ok, (starts[:, None] + from_pick) // shards, TOK_DEV).reshape(-1)
    width = got_tokens.shape[2]
    tokens = (
        jnp.zeros((TOK_DEV, width), jnp.bfloat16)
        .at[place]
        .set(got_tokens.reshape(-1, width), mode="drop")
    )
    rows = tokens.shape[0]
    inner = w_out.shape[0]
    heads = inner // HEAD_DIM
    normed, hidden = layer_norm(tokens, ln_gain)
    queries = (
        jnp.dot(hidden, w_qkv[:, :inner], preferred_element_type=jnp.float32)
        .astype(jnp.bfloat16)
        .reshape(rows, heads, HEAD_DIM)
        .transpose(1, 0, 2)
    )
    pair_cols = jnp.dot(w_qkv[:, inner:].T, hidden.T, preferred_element_type=jnp.float32).astype(
        jnp.bfloat16
    )
    gathered = gather_blocks(pair_cols)
    split_kv = gathered.reshape(shards, heads, 2, HEAD_DIM, rows)
    keys_b = split_kv[:, :, 0]
    values_b = split_kv[:, :, 1]
    queries_b = jnp.broadcast_to(queries[None], (shards,) + queries.shape)
    scores = (
        jnp.einsum("ihqd,ihdt->ihqt", queries_b, keys_b, preferred_element_type=jnp.float32) * 0.125
    )
    send_target, scores = lax.optimization_barrier((send_target, scores))
    got_target = lax.all_to_all(send_target, "seq", split_axis=0, concat_axis=0, tiled=True)
    target = (
        jnp.zeros((TOK_DEV, width), jnp.bfloat16)
        .at[place]
        .set(got_target.reshape(-1, width), mode="drop")
    )
    row_max = jnp.max(scores, axis=(0, 3))
    weights = jnp.exp(scores - row_max[None, :, :, None])
    row_sum = jnp.sum(weights, axis=(0, 3))
    blended = jnp.sum(
        jnp.einsum(
            "ihqt,ihdt->ihqd", weights.astype(jnp.bfloat16), values_b, preferred_element_type=jnp.float32
        ),
        axis=0,
    )
    log_total = row_max + jnp.log(row_sum)
    attended = (
        (blended / row_sum[:, :, None]).transpose(1, 0, 2).reshape(rows, inner).astype(jnp.bfloat16)
    )
    student = tokens.astype(jnp.float32) + jnp.dot(
        attended, w_out, preferred_element_type=jnp.float32
    )
    token_loss, grad_y = align_terms(student, target)
    grad_b = grad_y.astype(jnp.bfloat16)
    grad_wout = jnp.dot(exchange_order(attended).T, grad_b, preferred_element_type=jnp.float32)
    grad_heads = (
        jnp.dot(grad_b, w_out.T, preferred_element_type=jnp.float32)
        .astype(jnp.bfloat16)
        .reshape(rows, heads, HEAD_DIM)
        .transpose(1, 0, 2)
    )
    row_dot = jnp.sum(
        grad_heads.astype(jnp.float32)
        * attended.reshape(rows, heads, HEAD_DIM).transpose(1, 0, 2).astype(jnp.float32),
        axis=2,
    )
    prob_full = jnp.exp(scores - log_total[None, :, :, None])
    grad_heads_b = jnp.broadcast_to(grad_heads[None], (shards,) + grad_heads.shape)
    d_value_b = jnp.einsum(
        "ihqd,ihqt->ihdt", grad_heads_b, prob_full.astype(jnp.bfloat16), preferred_element_type=jnp.float32
    )
    d_prob = jnp.einsum("ihqd,ihdt->ihqt", grad_heads_b, values_b, preferred_element_type=jnp.float32)
    d_score = (prob_full * (d_prob - row_dot[None, :, :, None])).astype(jnp.bfloat16)
    d_query_t = 0.125 * jnp.sum(
        jnp.einsum("ihqt,ihdt->ihdq", d_score, keys_b, preferred_element_type=jnp.float32), axis=0
    )
    d_key_b = 0.125 * jnp.einsum(
        "ihqd,ihqt->ihdt", queries_b, d_score, preferred_element_type=jnp.float32
    )
    half = shards // 2
    own_pairs = jnp.stack([d_key_b[:half], d_value_b[:half]], axis=2).reshape(half, 2 * inner, rows)
    other_pairs = jnp.stack([d_key_b[half:], d_value_b[half:]], axis=2).reshape(half, 2 * inner, rows)
    accum = return_blocks(own_pairs, other_pairs.astype(jnp.bfloat16))
    d_proj_t = jnp.concatenate([d_query_t.reshape(inner, rows), accum], axis=0).astype(jnp.bfloat16)
    grad_wqkv = jnp.einsum(
        "tf,ct->fc", exchange_order(hidden), d_proj_t, preferred_element_type=jnp.float32
    )
    d_hidden = jnp.einsum("ct,fc->tf", d_proj_t, w_qkv, preferred_element_type=jnp.float32)
    grad_ln = jnp.sum(d_hidden * normed, axis=0)
    loss_part = jnp.sum(token_loss)
    small = jnp.concatenate([grad_ln, loss_part.reshape(1)])
    grad_out, unused = halving_scatter(grad_wout)
    grad_qkv, small = halving_scatter(grad_wqkv, small)
    count_all = shards * lax.axis_size("clip") * TOK_DEV
    return (small[-1] / count_all, grad_qkv.reshape(-1), grad_out.reshape(-1), small[:-1])


def solution(mesh):
    placed = (P("clip", "seq", None), P("clip", "seq", None), P("clip", "seq"), P(), P(), P())
    return jax.shard_map(
        per_device,
        mesh=mesh,
        in_specs=placed,
        out_specs=(P(), P(("seq", "clip")), P(("seq", "clip")), P()),
        check_vma=False,
    )
```

```python
import jax
import jax.numpy as jnp
from jax import lax
from jax.sharding import PartitionSpec as P

HEAD_DIM = 64
TOK_DEV = 128


def shifted(value, axis, steps):
    count = lax.axis_size(axis)
    pairs = [(source, (source + steps) % count) for source in range(count)]
    return lax.ppermute(value, axis, pairs)


def layer_norm(tokens, ln_gain):
    values = tokens.astype(jnp.float32)
    center = values - jnp.mean(values, axis=-1, keepdims=True)
    spread = jnp.mean(center * center, axis=-1, keepdims=True)
    normed = center * lax.rsqrt(spread + 1e-05)
    return (normed, (normed * ln_gain).astype(jnp.bfloat16))


def align_terms(student, target):
    target_f = target.astype(jnp.float32)
    inv_y = lax.rsqrt(jnp.sum(student * student, axis=-1, keepdims=True) + 1e-06)
    inv_t = lax.rsqrt(jnp.sum(target_f * target_f, axis=-1, keepdims=True) + 1e-06)
    differ = student * inv_y - target_f * inv_t
    token_loss = jnp.sum(differ * differ, axis=-1)
    slopes = 2.0 * differ
    grad_y = inv_y * slopes - student * (inv_y * inv_y * inv_y) * jnp.sum(
        slopes * student, axis=-1, keepdims=True
    )
    return (token_loss, grad_y)


def key_mask(key_count, rows, heads):
    slot_idx = jnp.arange(rows, dtype=jnp.int32)
    halves = slot_idx[None, :] < key_count[:, None]
    return jnp.repeat(halves, heads // 2, axis=0)


def head_scores(queries, pair_rows, key_count):
    rows = pair_rows.shape[0]
    heads = queries.shape[1]
    split_kv = pair_rows.reshape(rows, heads, 2, HEAD_DIM)
    scores = (
        jnp.einsum("qhd,khd->hqk", queries, split_kv[:, :, 0], preferred_element_type=jnp.float32)
        * 0.125
    )
    mask_rows = key_mask(key_count, rows, heads)
    return (jnp.where(mask_rows[:, None, :], scores, -1e30), split_kv)


def absorb(state, queries, pair_rows, key_count):
    row_max, row_sum, blended = state
    scores, split_kv = head_scores(queries, pair_rows, key_count)
    new_max = jnp.maximum(row_max, jnp.max(scores, axis=2))
    rescale = jnp.exp(row_max - new_max)
    weights = jnp.exp(scores - new_max[:, :, None])
    row_sum = row_sum * rescale + jnp.sum(weights, axis=2)
    blended = blended * rescale[:, :, None] + jnp.einsum(
        "hqk,khd->hqd",
        weights.astype(jnp.bfloat16),
        split_kv[:, :, 1],
        preferred_element_type=jnp.float32,
    )
    return (new_max, row_sum, blended)


def contribution(queries, grad_heads, log_total, row_dot, pair_rows, key_count):
    scores, split_kv = head_scores(queries, pair_rows, key_count)
    prob_full = jnp.exp(scores - log_total[:, :, None])
    d_value = jnp.einsum(
        "hqk,qhd->khd",
        prob_full.astype(jnp.bfloat16),
        grad_heads,
        preferred_element_type=jnp.float32,
    )
    d_prob = jnp.einsum(
        "qhd,khd->hqk", grad_heads, split_kv[:, :, 1], preferred_element_type=jnp.float32
    )
    d_score = (prob_full * (d_prob - row_dot[:, :, None])).astype(jnp.bfloat16)
    d_query = 0.125 * jnp.einsum(
        "hqk,khd->qhd", d_score, split_kv[:, :, 0], preferred_element_type=jnp.float32
    )
    d_key = 0.125 * jnp.einsum("hqk,qhd->khd", d_score, queries, preferred_element_type=jnp.float32)
    rows = pair_rows.shape[0]
    return (d_query, jnp.stack([d_key, d_value], axis=2).reshape(rows, -1))


def move_keys(pair_rows):
    moved = shifted(pair_rows, "seq", 1)
    return moved


def move_grads(accum):
    moved = shifted(accum.astype(jnp.bfloat16), "seq", 1).astype(accum.dtype)
    return moved


def exchange_bits():
    seq_bits = lax.axis_size("seq").bit_length() - 1
    clip_bits = lax.axis_size("clip").bit_length() - 1
    assert (1 << seq_bits) == lax.axis_size("seq")
    assert (1 << clip_bits) == lax.axis_size("clip")
    return seq_bits, clip_bits


def exchange_order(values):
    seq_bits, clip_bits = exchange_bits()
    total = seq_bits + clip_bits
    lead = values.shape[0]
    split = values.reshape([lead] + [2] * total + [-1])
    seq_dims = [1 + seq_bits - 1 - bit for bit in range(seq_bits)]
    clip_dims = [1 + seq_bits + clip_bits - 1 - bit for bit in range(clip_bits)]
    perm = [0] + seq_dims + clip_dims + [total + 1]
    return split.transpose(perm).reshape(values.shape)


def halving_scatter(grad, small=None):
    seq_bits, clip_bits = exchange_bits()
    total = seq_bits + clip_bits
    data = grad.reshape([2] * total + [-1, grad.shape[1]])
    order_a = list(range(seq_bits))
    order_b = [0] + list(range(seq_bits - 1, 0, -1))
    core_bit = lax.axis_index("seq") & 1
    left_a = list(range(seq_bits))
    left_b = list(range(seq_bits))
    for step in range(seq_bits):
        bit_a, bit_b = order_a[step], order_b[step]
        dim_a, dim_b = left_a.index(bit_a), left_b.index(bit_b)
        me = lax.axis_index("seq")
        mine_a = (me >> bit_a) & 1
        mine_b = (me >> bit_b) & 1
        pairs = []
        for src in range(lax.axis_size("seq")):
            bit = bit_a if (src & 1) == 0 else bit_b
            pairs.append((src, src ^ (1 << bit)))
        keep = jnp.where(
            core_bit == 0,
            lax.dynamic_index_in_dim(data, mine_a, axis=dim_a, keepdims=False),
            lax.dynamic_index_in_dim(data, mine_b, axis=dim_b, keepdims=False),
        )
        give = jnp.where(
            core_bit == 0,
            lax.dynamic_index_in_dim(data, 1 - mine_a, axis=dim_a, keepdims=False),
            lax.dynamic_index_in_dim(data, 1 - mine_b, axis=dim_b, keepdims=False),
        )
        left_a.pop(dim_a)
        left_b.pop(dim_b)
        if small is None:
            got = lax.ppermute(give.astype(jnp.bfloat16), "seq", pairs)
        else:
            got, got_small = lax.ppermute((give.astype(jnp.bfloat16), small), "seq", pairs)
            small = small + got_small
        data = keep + got.astype(jnp.float32)
    for bit in range(clip_bits):
        mine = (lax.axis_index("clip") >> bit) & 1
        pairs = [(src, src ^ (1 << bit)) for src in range(lax.axis_size("clip"))]
        keep = lax.dynamic_index_in_dim(data, mine, axis=0, keepdims=False)
        give = lax.dynamic_index_in_dim(data, 1 - mine, axis=0, keepdims=False)
        if small is None:
            got = lax.ppermute(give.astype(jnp.bfloat16), "clip", pairs)
        else:
            got, got_small = lax.ppermute((give.astype(jnp.bfloat16), small), "clip", pairs)
            small = small + got_small
        data = keep + got.astype(jnp.float32)
    return data, small


def xor_pairs(mask):
    count = lax.axis_size("seq")
    return [(src, src ^ mask) for src in range(count)]


def gather_blocks(block):
    half = lax.axis_size("seq") // 2
    same_core = [block] + [lax.ppermute(block, "seq", xor_pairs(2 * k)) for k in range(1, half)]
    group = jnp.stack(same_core)
    other = lax.ppermute(group, "seq", xor_pairs(1))
    return jnp.concatenate([group, other], axis=0)


def return_blocks(own_parts, other_parts):
    half = lax.axis_size("seq") // 2
    got = lax.ppermute(other_parts, "seq", xor_pairs(1))
    summed = own_parts.astype(jnp.bfloat16).astype(jnp.float32) + got.astype(jnp.float32)
    accum = summed[0]
    for k in range(1, half):
        sent = lax.ppermute(summed[k].astype(jnp.bfloat16), "seq", xor_pairs(2 * k))
        accum = accum + sent.astype(jnp.float32)
    return accum


def per_device(raw_tokens, teacher, keep_rows, w_qkv, w_out, ln_gain):
    shards = lax.axis_size("seq")
    my_index = lax.axis_index("seq")
    row_ids = keep_rows[0]
    list_slots = row_ids.shape[0]
    is_kept = row_ids >= 0
    kept_count = jnp.sum(is_kept.astype(jnp.int32))
    safe_ids = jnp.maximum(row_ids, 0)
    kept_tokens = jnp.where(is_kept[:, None], raw_tokens[0][safe_ids], jnp.zeros((), jnp.bfloat16))
    kept_target = jnp.where(is_kept[:, None], teacher[0][safe_ids], jnp.zeros((), jnp.bfloat16))
    count_table = lax.all_to_all(
        jnp.broadcast_to(kept_count.reshape(1, 1), (shards, 1)), "seq", 0, 0, tiled=True
    ).reshape(shards)
    shard_ids = jnp.arange(shards, dtype=jnp.int32)
    per_peer = -(-list_slots // shards)
    starts = jnp.cumsum(count_table) - count_table
    before = jnp.sum(jnp.where(shard_ids < my_index, count_table, 0))
    slot_ids = jnp.arange(per_peer, dtype=jnp.int32)
    pick = (shard_ids[:, None] - before) % shards + slot_ids[None, :] * shards
    pick_ok = pick < kept_count
    pick_safe = jnp.minimum(pick, list_slots - 1)
    send_tokens = jnp.where(
        pick_ok[:, :, None], kept_tokens[pick_safe], jnp.zeros((), jnp.bfloat16)
    )
    send_target = jnp.where(
        pick_ok[:, :, None], kept_target[pick_safe], jnp.zeros((), jnp.bfloat16)
    )
    got_both = lax.all_to_all(
        jnp.concatenate([send_tokens, send_target], axis=2), "seq", split_axis=0, concat_axis=0, tiled=True
    )
    from_pick = (my_index - starts[:, None]) % shards + slot_ids[None, :] * shards
    from_ok = from_pick < count_table[:, None]
    place = jnp.where(from_ok, (starts[:, None] + from_pick) // shards, TOK_DEV).reshape(-1)
    width = send_tokens.shape[2]
    both = (
        jnp.zeros((TOK_DEV, 2 * width), jnp.bfloat16)
        .at[place]
        .set(got_both.reshape(-1, 2 * width), mode="drop")
    )
    tokens = both[:, :width]
    target = both[:, width:]
    rows = tokens.shape[0]
    inner = w_out.shape[0]
    heads = inner // HEAD_DIM
    normed, hidden = layer_norm(tokens, ln_gain)
    queries = (
        jnp.dot(hidden, w_qkv[:, :inner], preferred_element_type=jnp.float32)
        .astype(jnp.bfloat16)
        .reshape(rows, heads, HEAD_DIM)
        .transpose(1, 0, 2)
    )
    pair_cols = jnp.dot(w_qkv[:, inner:].T, hidden.T, preferred_element_type=jnp.float32).astype(
        jnp.bfloat16
    )
    gathered = gather_blocks(pair_cols)
    split_kv = gathered.reshape(shards, heads, 2, HEAD_DIM, rows)
    keys_b = split_kv[:, :, 0]
    values_b = split_kv[:, :, 1]
    queries_b = jnp.broadcast_to(queries[None], (shards,) + queries.shape)
    scores = (
        jnp.einsum("ihqd,ihdt->ihqt", queries_b, keys_b, preferred_element_type=jnp.float32) * 0.125
    )
    row_max = jnp.max(scores, axis=(0, 3))
    weights = jnp.exp(scores - row_max[None, :, :, None])
    row_sum = jnp.sum(weights, axis=(0, 3))
    blended = jnp.sum(
        jnp.einsum(
            "ihqt,ihdt->ihqd", weights.astype(jnp.bfloat16), values_b, preferred_element_type=jnp.float32
        ),
        axis=0,
    )
    log_total = row_max + jnp.log(row_sum)
    attended = (
        (blended / row_sum[:, :, None]).transpose(1, 0, 2).reshape(rows, inner).astype(jnp.bfloat16)
    )
    student = tokens.astype(jnp.float32) + jnp.dot(
        attended, w_out, preferred_element_type=jnp.float32
    )
    token_loss, grad_y = align_terms(student, target)
    grad_b = grad_y.astype(jnp.bfloat16)
    grad_wout = jnp.dot(exchange_order(attended).T, grad_b, preferred_element_type=jnp.float32)
    grad_heads = (
        jnp.dot(grad_b, w_out.T, preferred_element_type=jnp.float32)
        .astype(jnp.bfloat16)
        .reshape(rows, heads, HEAD_DIM)
        .transpose(1, 0, 2)
    )
    row_dot = jnp.sum(
        grad_heads.astype(jnp.float32)
        * attended.reshape(rows, heads, HEAD_DIM).transpose(1, 0, 2).astype(jnp.float32),
        axis=2,
    )
    prob_full = jnp.exp(scores - log_total[None, :, :, None])
    grad_heads_b = jnp.broadcast_to(grad_heads[None], (shards,) + grad_heads.shape)
    d_value_b = jnp.einsum(
        "ihqd,ihqt->ihdt", grad_heads_b, prob_full.astype(jnp.bfloat16), preferred_element_type=jnp.float32
    )
    d_prob = jnp.einsum("ihqd,ihdt->ihqt", grad_heads_b, values_b, preferred_element_type=jnp.float32)
    d_score = (prob_full * (d_prob - row_dot[None, :, :, None])).astype(jnp.bfloat16)
    d_query_t = 0.125 * jnp.sum(
        jnp.einsum("ihqt,ihdt->ihdq", d_score, keys_b, preferred_element_type=jnp.float32), axis=0
    )
    d_key_b = 0.125 * jnp.einsum(
        "ihqd,ihqt->ihdt", queries_b, d_score, preferred_element_type=jnp.float32
    )
    half = shards // 2
    own_pairs = jnp.stack([d_key_b[:half], d_value_b[:half]], axis=2).reshape(half, 2 * inner, rows)
    other_pairs = jnp.stack([d_key_b[half:], d_value_b[half:]], axis=2).reshape(half, 2 * inner, rows)
    accum = return_blocks(own_pairs, other_pairs.astype(jnp.bfloat16))
    d_proj_t = jnp.concatenate([d_query_t.reshape(inner, rows), accum], axis=0).astype(jnp.bfloat16)
    grad_wqkv = jnp.einsum(
        "tf,ct->fc", exchange_order(hidden), d_proj_t, preferred_element_type=jnp.float32
    )
    d_hidden = jnp.einsum("ct,fc->tf", d_proj_t, w_qkv, preferred_element_type=jnp.float32)
    grad_ln = jnp.sum(d_hidden * normed, axis=0)
    loss_part = jnp.sum(token_loss)
    small = jnp.concatenate([grad_ln, loss_part.reshape(1)])
    grad_out, unused = halving_scatter(grad_wout)
    grad_qkv, small = halving_scatter(grad_wqkv, small)
    count_all = shards * lax.axis_size("clip") * TOK_DEV
    return (small[-1] / count_all, grad_qkv.reshape(-1), grad_out.reshape(-1), small[:-1])


def solution(mesh):
    placed = (P("clip", "seq", None), P("clip", "seq", None), P("clip", "seq"), P(), P(), P())
    return jax.shard_map(
        per_device,
        mesh=mesh,
        in_specs=placed,
        out_specs=(P(), P(("seq", "clip")), P(("seq", "clip")), P()),
        check_vma=False,
    )
```

```python
import jax
import jax.numpy as jnp
from jax import lax
from jax.sharding import PartitionSpec as P

HEAD_DIM = 64
TOK_DEV = 128


def shifted(value, axis, steps):
    count = lax.axis_size(axis)
    pairs = [(source, (source + steps) % count) for source in range(count)]
    return lax.ppermute(value, axis, pairs)


def layer_norm(tokens, ln_gain):
    values = tokens.astype(jnp.float32)
    center = values - jnp.mean(values, axis=-1, keepdims=True)
    spread = jnp.mean(center * center, axis=-1, keepdims=True)
    normed = center * lax.rsqrt(spread + 1e-05)
    return (normed, (normed * ln_gain).astype(jnp.bfloat16))


def align_terms(student, target):
    target_f = target.astype(jnp.float32)
    inv_y = lax.rsqrt(jnp.sum(student * student, axis=-1, keepdims=True) + 1e-06)
    inv_t = lax.rsqrt(jnp.sum(target_f * target_f, axis=-1, keepdims=True) + 1e-06)
    differ = student * inv_y - target_f * inv_t
    token_loss = jnp.sum(differ * differ, axis=-1)
    slopes = 2.0 * differ
    grad_y = inv_y * slopes - student * (inv_y * inv_y * inv_y) * jnp.sum(
        slopes * student, axis=-1, keepdims=True
    )
    return (token_loss, grad_y)


def key_mask(key_count, rows, heads):
    slot_idx = jnp.arange(rows, dtype=jnp.int32)
    halves = slot_idx[None, :] < key_count[:, None]
    return jnp.repeat(halves, heads // 2, axis=0)


def head_scores(queries, pair_rows, key_count):
    rows = pair_rows.shape[0]
    heads = queries.shape[1]
    split_kv = pair_rows.reshape(rows, heads, 2, HEAD_DIM)
    scores = (
        jnp.einsum("qhd,khd->hqk", queries, split_kv[:, :, 0], preferred_element_type=jnp.float32)
        * 0.125
    )
    mask_rows = key_mask(key_count, rows, heads)
    return (jnp.where(mask_rows[:, None, :], scores, -1e30), split_kv)


def absorb(state, queries, pair_rows, key_count):
    row_max, row_sum, blended = state
    scores, split_kv = head_scores(queries, pair_rows, key_count)
    new_max = jnp.maximum(row_max, jnp.max(scores, axis=2))
    rescale = jnp.exp(row_max - new_max)
    weights = jnp.exp(scores - new_max[:, :, None])
    row_sum = row_sum * rescale + jnp.sum(weights, axis=2)
    blended = blended * rescale[:, :, None] + jnp.einsum(
        "hqk,khd->hqd",
        weights.astype(jnp.bfloat16),
        split_kv[:, :, 1],
        preferred_element_type=jnp.float32,
    )
    return (new_max, row_sum, blended)


def contribution(queries, grad_heads, log_total, row_dot, pair_rows, key_count):
    scores, split_kv = head_scores(queries, pair_rows, key_count)
    prob_full = jnp.exp(scores - log_total[:, :, None])
    d_value = jnp.einsum(
        "hqk,qhd->khd",
        prob_full.astype(jnp.bfloat16),
        grad_heads,
        preferred_element_type=jnp.float32,
    )
    d_prob = jnp.einsum(
        "qhd,khd->hqk", grad_heads, split_kv[:, :, 1], preferred_element_type=jnp.float32
    )
    d_score = (prob_full * (d_prob - row_dot[:, :, None])).astype(jnp.bfloat16)
    d_query = 0.125 * jnp.einsum(
        "hqk,khd->qhd", d_score, split_kv[:, :, 0], preferred_element_type=jnp.float32
    )
    d_key = 0.125 * jnp.einsum("hqk,qhd->khd", d_score, queries, preferred_element_type=jnp.float32)
    rows = pair_rows.shape[0]
    return (d_query, jnp.stack([d_key, d_value], axis=2).reshape(rows, -1))


def move_keys(pair_rows):
    moved = shifted(pair_rows, "seq", 1)
    return moved


def move_grads(accum):
    moved = shifted(accum.astype(jnp.bfloat16), "seq", 1).astype(accum.dtype)
    return moved


def exchange_bits():
    seq_bits = lax.axis_size("seq").bit_length() - 1
    clip_bits = lax.axis_size("clip").bit_length() - 1
    assert (1 << seq_bits) == lax.axis_size("seq")
    assert (1 << clip_bits) == lax.axis_size("clip")
    return seq_bits, clip_bits


def exchange_order(values):
    seq_bits, clip_bits = exchange_bits()
    total = seq_bits + clip_bits
    lead = values.shape[0]
    split = values.reshape([lead] + [2] * total + [-1])
    seq_dims = [1 + seq_bits - 1 - bit for bit in range(seq_bits)]
    clip_dims = [1 + seq_bits + clip_bits - 1 - bit for bit in range(clip_bits)]
    perm = [0] + seq_dims + clip_dims + [total + 1]
    return split.transpose(perm).reshape(values.shape)


def halving_scatter(grad, small=None):
    seq_bits, clip_bits = exchange_bits()
    total = seq_bits + clip_bits
    data = grad.reshape([2] * total + [-1, grad.shape[1]])
    order_a = list(range(seq_bits))
    order_b = [0] + list(range(seq_bits - 1, 0, -1))
    core_bit = lax.axis_index("seq") & 1
    left_a = list(range(seq_bits))
    left_b = list(range(seq_bits))
    for step in range(seq_bits):
        bit_a, bit_b = order_a[step], order_b[step]
        dim_a, dim_b = left_a.index(bit_a), left_b.index(bit_b)
        me = lax.axis_index("seq")
        mine_a = (me >> bit_a) & 1
        mine_b = (me >> bit_b) & 1
        pairs = []
        for src in range(lax.axis_size("seq")):
            bit = bit_a if (src & 1) == 0 else bit_b
            pairs.append((src, src ^ (1 << bit)))
        keep = jnp.where(
            core_bit == 0,
            lax.dynamic_index_in_dim(data, mine_a, axis=dim_a, keepdims=False),
            lax.dynamic_index_in_dim(data, mine_b, axis=dim_b, keepdims=False),
        )
        give = jnp.where(
            core_bit == 0,
            lax.dynamic_index_in_dim(data, 1 - mine_a, axis=dim_a, keepdims=False),
            lax.dynamic_index_in_dim(data, 1 - mine_b, axis=dim_b, keepdims=False),
        )
        left_a.pop(dim_a)
        left_b.pop(dim_b)
        if small is None:
            got = lax.ppermute(give.astype(jnp.bfloat16), "seq", pairs)
        else:
            got, got_small = lax.ppermute((give.astype(jnp.bfloat16), small), "seq", pairs)
            small = small + got_small
        data = keep + got.astype(jnp.float32)
    for bit in range(clip_bits):
        mine = (lax.axis_index("clip") >> bit) & 1
        pairs = [(src, src ^ (1 << bit)) for src in range(lax.axis_size("clip"))]
        keep = lax.dynamic_index_in_dim(data, mine, axis=0, keepdims=False)
        give = lax.dynamic_index_in_dim(data, 1 - mine, axis=0, keepdims=False)
        if small is None:
            got = lax.ppermute(give.astype(jnp.bfloat16), "clip", pairs)
        else:
            got, got_small = lax.ppermute((give.astype(jnp.bfloat16), small), "clip", pairs)
            small = small + got_small
        data = keep + got.astype(jnp.float32)
    return data, small


def xor_pairs(mask):
    count = lax.axis_size("seq")
    return [(src, src ^ mask) for src in range(count)]


def gather_blocks(block):
    half = lax.axis_size("seq") // 2
    early = lax.ppermute(block, "seq", xor_pairs(1))
    received = [lax.ppermute(block, "seq", xor_pairs(2 * k)) for k in range(1, half)]
    late = lax.ppermute(jnp.stack(received), "seq", xor_pairs(1))
    return jnp.concatenate([jnp.stack([block] + received), early[None], late], axis=0)


def return_blocks(own_parts, other_parts):
    half = lax.axis_size("seq") // 2
    got = lax.ppermute(other_parts, "seq", xor_pairs(1))
    summed = own_parts + got.astype(jnp.float32)
    accum = summed[0]
    for k in range(1, half):
        sent = lax.ppermute(summed[k].astype(jnp.bfloat16), "seq", xor_pairs(2 * k))
        accum = accum + sent.astype(jnp.float32)
    return accum


def per_device(raw_tokens, teacher, keep_rows, w_qkv, w_out, ln_gain):
    shards = lax.axis_size("seq")
    my_index = lax.axis_index("seq")
    row_ids = keep_rows[0]
    list_slots = row_ids.shape[0]
    is_kept = row_ids >= 0
    kept_count = jnp.sum(is_kept.astype(jnp.int32))
    safe_ids = jnp.maximum(row_ids, 0)
    kept_tokens = jnp.where(is_kept[:, None], raw_tokens[0][safe_ids], jnp.zeros((), jnp.bfloat16))
    kept_target = jnp.where(is_kept[:, None], teacher[0][safe_ids], jnp.zeros((), jnp.bfloat16))
    count_table = lax.all_to_all(
        jnp.broadcast_to(kept_count.reshape(1, 1), (shards, 1)), "seq", 0, 0, tiled=True
    ).reshape(shards)
    shard_ids = jnp.arange(shards, dtype=jnp.int32)
    per_peer = -(-list_slots // shards)
    starts = jnp.cumsum(count_table) - count_table
    before = jnp.sum(jnp.where(shard_ids < my_index, count_table, 0))
    slot_ids = jnp.arange(per_peer, dtype=jnp.int32)
    pick = (shard_ids[:, None] - before) % shards + slot_ids[None, :] * shards
    pick_ok = pick < kept_count
    pick_safe = jnp.minimum(pick, list_slots - 1)
    send_tokens = jnp.where(
        pick_ok[:, :, None], kept_tokens[pick_safe], jnp.zeros((), jnp.bfloat16)
    )
    send_target = jnp.where(
        pick_ok[:, :, None], kept_target[pick_safe], jnp.zeros((), jnp.bfloat16)
    )
    got_both = lax.all_to_all(
        jnp.concatenate([send_tokens, send_target], axis=2), "seq", split_axis=0, concat_axis=0, tiled=True
    )
    from_pick = (my_index - starts[:, None]) % shards + slot_ids[None, :] * shards
    from_ok = from_pick < count_table[:, None]
    place = jnp.where(from_ok, (starts[:, None] + from_pick) // shards, TOK_DEV).reshape(-1)
    width = send_tokens.shape[2]
    both = (
        jnp.zeros((TOK_DEV, 2 * width), jnp.bfloat16)
        .at[place]
        .set(got_both.reshape(-1, 2 * width), mode="drop")
    )
    tokens = both[:, :width]
    target = both[:, width:]
    rows = tokens.shape[0]
    inner = w_out.shape[0]
    heads = inner // HEAD_DIM
    normed, hidden = layer_norm(tokens, ln_gain)
    queries = (
        jnp.dot(hidden, w_qkv[:, :inner], preferred_element_type=jnp.float32)
        .astype(jnp.bfloat16)
        .reshape(rows, heads, HEAD_DIM)
        .transpose(1, 0, 2)
    )
    pair_cols = jnp.dot(w_qkv[:, inner:].T, hidden.T, preferred_element_type=jnp.float32).astype(
        jnp.bfloat16
    )
    gathered = gather_blocks(pair_cols)
    split_kv = gathered.reshape(shards, heads, 2, HEAD_DIM, rows)
    keys_b = split_kv[:, :, 0]
    values_b = split_kv[:, :, 1]
    queries_b = jnp.broadcast_to(queries[None], (shards,) + queries.shape)
    scores = (
        jnp.einsum("ihqd,ihdt->ihqt", queries_b, keys_b, preferred_element_type=jnp.float32) * 0.125
    )
    row_max = jnp.max(scores, axis=(0, 3))
    weights = jnp.exp(scores - row_max[None, :, :, None])
    row_sum = jnp.sum(weights, axis=(0, 3))
    blended = jnp.sum(
        jnp.einsum(
            "ihqt,ihdt->ihqd", weights.astype(jnp.bfloat16), values_b, preferred_element_type=jnp.float32
        ),
        axis=0,
    )
    log_total = row_max + jnp.log(row_sum)
    attended = (
        (blended / row_sum[:, :, None]).transpose(1, 0, 2).reshape(rows, inner).astype(jnp.bfloat16)
    )
    student = tokens.astype(jnp.float32) + jnp.dot(
        attended, w_out, preferred_element_type=jnp.float32
    )
    token_loss, grad_y = align_terms(student, target)
    grad_b = grad_y.astype(jnp.bfloat16)
    grad_wout = jnp.dot(exchange_order(attended).T, grad_b, preferred_element_type=jnp.float32)
    grad_heads = (
        jnp.dot(grad_b, w_out.T, preferred_element_type=jnp.float32)
        .astype(jnp.bfloat16)
        .reshape(rows, heads, HEAD_DIM)
        .transpose(1, 0, 2)
    )
    row_dot = jnp.sum(
        grad_heads.astype(jnp.float32)
        * attended.reshape(rows, heads, HEAD_DIM).transpose(1, 0, 2).astype(jnp.float32),
        axis=2,
    )
    prob_full = jnp.exp(scores - log_total[None, :, :, None])
    grad_heads_b = jnp.broadcast_to(grad_heads[None], (shards,) + grad_heads.shape)
    d_value_b = jnp.einsum(
        "ihqd,ihqt->ihdt", grad_heads_b, prob_full.astype(jnp.bfloat16), preferred_element_type=jnp.float32
    )
    d_prob = jnp.einsum("ihqd,ihdt->ihqt", grad_heads_b, values_b, preferred_element_type=jnp.float32)
    d_score = (prob_full * (d_prob - row_dot[None, :, :, None])).astype(jnp.bfloat16)
    d_query_t = 0.125 * jnp.sum(
        jnp.einsum("ihqt,ihdt->ihdq", d_score, keys_b, preferred_element_type=jnp.float32), axis=0
    )
    d_key_b = 0.125 * jnp.einsum(
        "ihqd,ihqt->ihdt", queries_b, d_score, preferred_element_type=jnp.float32
    )
    half = shards // 2
    own_pairs = jnp.stack([d_key_b[:half], d_value_b[:half]], axis=2).reshape(half, 2 * inner, rows)
    other_pairs = jnp.stack([d_key_b[half:], d_value_b[half:]], axis=2).reshape(half, 2 * inner, rows)
    accum = return_blocks(own_pairs, other_pairs.astype(jnp.bfloat16))
    d_proj_t = jnp.concatenate([d_query_t.reshape(inner, rows), accum], axis=0).astype(jnp.bfloat16)
    grad_wqkv = jnp.einsum(
        "tf,ct->fc", exchange_order(hidden), d_proj_t, preferred_element_type=jnp.float32
    )
    d_hidden = jnp.einsum("ct,fc->tf", d_proj_t, w_qkv, preferred_element_type=jnp.float32)
    grad_ln = jnp.sum(d_hidden * normed, axis=0)
    loss_part = jnp.sum(token_loss)
    small = jnp.concatenate([grad_ln, loss_part.reshape(1)])
    grad_out, unused = halving_scatter(grad_wout)
    grad_qkv, small = halving_scatter(grad_wqkv, small)
    count_all = shards * lax.axis_size("clip") * TOK_DEV
    return (small[-1] / count_all, grad_qkv.reshape(-1), grad_out.reshape(-1), small[:-1])


def solution(mesh):
    placed = (P("clip", "seq", None), P("clip", "seq", None), P("clip", "seq"), P(), P(), P())
    return jax.shard_map(
        per_device,
        mesh=mesh,
        in_specs=placed,
        out_specs=(P(), P(("seq", "clip")), P(("seq", "clip")), P()),
        check_vma=False,
    )
```

```python
import jax
import jax.numpy as jnp
from jax import lax
from jax.sharding import PartitionSpec as P

HEAD_DIM = 64
TOK_DEV = 128


def shifted(value, axis, steps):
    count = lax.axis_size(axis)
    pairs = [(source, (source + steps) % count) for source in range(count)]
    return lax.ppermute(value, axis, pairs)


def layer_norm(tokens, ln_gain):
    values = tokens.astype(jnp.float32)
    center = values - jnp.mean(values, axis=-1, keepdims=True)
    spread = jnp.mean(center * center, axis=-1, keepdims=True)
    normed = center * lax.rsqrt(spread + 1e-05)
    return (normed, (normed * ln_gain).astype(jnp.bfloat16))


def align_terms(student, target):
    target_f = target.astype(jnp.float32)
    inv_y = lax.rsqrt(jnp.sum(student * student, axis=-1, keepdims=True) + 1e-06)
    inv_t = lax.rsqrt(jnp.sum(target_f * target_f, axis=-1, keepdims=True) + 1e-06)
    differ = student * inv_y - target_f * inv_t
    token_loss = jnp.sum(differ * differ, axis=-1)
    slopes = 2.0 * differ
    grad_y = inv_y * slopes - student * (inv_y * inv_y * inv_y) * jnp.sum(
        slopes * student, axis=-1, keepdims=True
    )
    return (token_loss, grad_y)


def key_mask(key_count, rows, heads):
    slot_idx = jnp.arange(rows, dtype=jnp.int32)
    halves = slot_idx[None, :] < key_count[:, None]
    return jnp.repeat(halves, heads // 2, axis=0)


def head_scores(queries, pair_rows, key_count):
    rows = pair_rows.shape[0]
    heads = queries.shape[1]
    split_kv = pair_rows.reshape(rows, heads, 2, HEAD_DIM)
    scores = (
        jnp.einsum("qhd,khd->hqk", queries, split_kv[:, :, 0], preferred_element_type=jnp.float32)
        * 0.125
    )
    mask_rows = key_mask(key_count, rows, heads)
    return (jnp.where(mask_rows[:, None, :], scores, -1e30), split_kv)


def absorb(state, queries, pair_rows, key_count):
    row_max, row_sum, blended = state
    scores, split_kv = head_scores(queries, pair_rows, key_count)
    new_max = jnp.maximum(row_max, jnp.max(scores, axis=2))
    rescale = jnp.exp(row_max - new_max)
    weights = jnp.exp(scores - new_max[:, :, None])
    row_sum = row_sum * rescale + jnp.sum(weights, axis=2)
    blended = blended * rescale[:, :, None] + jnp.einsum(
        "hqk,khd->hqd",
        weights.astype(jnp.bfloat16),
        split_kv[:, :, 1],
        preferred_element_type=jnp.float32,
    )
    return (new_max, row_sum, blended)


def contribution(queries, grad_heads, log_total, row_dot, pair_rows, key_count):
    scores, split_kv = head_scores(queries, pair_rows, key_count)
    prob_full = jnp.exp(scores - log_total[:, :, None])
    d_value = jnp.einsum(
        "hqk,qhd->khd",
        prob_full.astype(jnp.bfloat16),
        grad_heads,
        preferred_element_type=jnp.float32,
    )
    d_prob = jnp.einsum(
        "qhd,khd->hqk", grad_heads, split_kv[:, :, 1], preferred_element_type=jnp.float32
    )
    d_score = (prob_full * (d_prob - row_dot[:, :, None])).astype(jnp.bfloat16)
    d_query = 0.125 * jnp.einsum(
        "hqk,khd->qhd", d_score, split_kv[:, :, 0], preferred_element_type=jnp.float32
    )
    d_key = 0.125 * jnp.einsum("hqk,qhd->khd", d_score, queries, preferred_element_type=jnp.float32)
    rows = pair_rows.shape[0]
    return (d_query, jnp.stack([d_key, d_value], axis=2).reshape(rows, -1))


def move_keys(pair_rows):
    moved = shifted(pair_rows, "seq", 1)
    return moved


def move_grads(accum):
    moved = shifted(accum.astype(jnp.bfloat16), "seq", 1).astype(accum.dtype)
    return moved


def exchange_bits():
    seq_bits = lax.axis_size("seq").bit_length() - 1
    clip_bits = lax.axis_size("clip").bit_length() - 1
    assert (1 << seq_bits) == lax.axis_size("seq")
    assert (1 << clip_bits) == lax.axis_size("clip")
    return seq_bits, clip_bits


def exchange_order(values):
    seq_bits, clip_bits = exchange_bits()
    total = seq_bits + clip_bits
    lead = values.shape[0]
    split = values.reshape([lead] + [2] * total + [-1])
    seq_dims = [1 + seq_bits - 1 - bit for bit in range(seq_bits)]
    clip_dims = [1 + seq_bits + clip_bits - 1 - bit for bit in range(clip_bits)]
    perm = [0] + seq_dims + clip_dims + [total + 1]
    return split.transpose(perm).reshape(values.shape)


def halving_scatter(grad, small=None):
    seq_bits, clip_bits = exchange_bits()
    total = seq_bits + clip_bits
    data = grad.reshape([2] * total + [-1, grad.shape[1]])
    order_a = list(range(seq_bits))
    order_b = [0] + list(range(seq_bits - 1, 0, -1))
    core_bit = lax.axis_index("seq") & 1
    left_a = list(range(seq_bits))
    left_b = list(range(seq_bits))
    for step in range(seq_bits):
        bit_a, bit_b = order_a[step], order_b[step]
        dim_a, dim_b = left_a.index(bit_a), left_b.index(bit_b)
        me = lax.axis_index("seq")
        mine_a = (me >> bit_a) & 1
        mine_b = (me >> bit_b) & 1
        pairs = []
        for src in range(lax.axis_size("seq")):
            bit = bit_a if (src & 1) == 0 else bit_b
            pairs.append((src, src ^ (1 << bit)))
        keep = jnp.where(
            core_bit == 0,
            lax.dynamic_index_in_dim(data, mine_a, axis=dim_a, keepdims=False),
            lax.dynamic_index_in_dim(data, mine_b, axis=dim_b, keepdims=False),
        )
        give = jnp.where(
            core_bit == 0,
            lax.dynamic_index_in_dim(data, 1 - mine_a, axis=dim_a, keepdims=False),
            lax.dynamic_index_in_dim(data, 1 - mine_b, axis=dim_b, keepdims=False),
        )
        left_a.pop(dim_a)
        left_b.pop(dim_b)
        if small is None:
            got = lax.ppermute(give.astype(jnp.bfloat16), "seq", pairs)
        else:
            got, got_small = lax.ppermute((give.astype(jnp.bfloat16), small), "seq", pairs)
            small = small + got_small
        data = keep + got.astype(jnp.float32)
    for bit in range(clip_bits):
        mine = (lax.axis_index("clip") >> bit) & 1
        pairs = [(src, src ^ (1 << bit)) for src in range(lax.axis_size("clip"))]
        keep = lax.dynamic_index_in_dim(data, mine, axis=0, keepdims=False)
        give = lax.dynamic_index_in_dim(data, 1 - mine, axis=0, keepdims=False)
        if small is None:
            got = lax.ppermute(give.astype(jnp.bfloat16), "clip", pairs)
        else:
            got, got_small = lax.ppermute((give.astype(jnp.bfloat16), small), "clip", pairs)
            small = small + got_small
        data = keep + got.astype(jnp.float32)
    return data, small


def xor_pairs(mask):
    count = lax.axis_size("seq")
    return [(src, src ^ mask) for src in range(count)]


def gather_blocks(block):
    half = lax.axis_size("seq") // 2
    same_core = [block] + [lax.ppermute(block, "seq", xor_pairs(2 * k)) for k in range(1, half)]
    group = jnp.stack(same_core)
    other = lax.ppermute(group, "seq", xor_pairs(1))
    return jnp.concatenate([group, other], axis=0)


def return_blocks(own_parts, other_parts):
    half = lax.axis_size("seq") // 2
    got = lax.ppermute(other_parts, "seq", xor_pairs(1))
    summed = own_parts.astype(jnp.bfloat16).astype(jnp.float32) + got.astype(jnp.float32)
    accum = summed[0]
    for k in range(1, half):
        sent = lax.ppermute(summed[k].astype(jnp.bfloat16), "seq", xor_pairs(2 * k))
        accum = accum + sent.astype(jnp.float32)
    return accum


def per_device(raw_tokens, teacher, keep_rows, w_qkv, w_out, ln_gain):
    shards = lax.axis_size("seq")
    my_index = lax.axis_index("seq")
    row_ids = keep_rows[0]
    list_slots = row_ids.shape[0]
    is_kept = row_ids >= 0
    kept_count = jnp.sum(is_kept.astype(jnp.int32))
    safe_ids = jnp.maximum(row_ids, 0)
    kept_tokens = jnp.where(is_kept[:, None], raw_tokens[0][safe_ids], jnp.zeros((), jnp.bfloat16))
    kept_target = jnp.where(is_kept[:, None], teacher[0][safe_ids], jnp.zeros((), jnp.bfloat16))
    kept_tokens, kept_target, kept_count = lax.optimization_barrier(
        (kept_tokens, kept_target, kept_count)
    )
    count_table = lax.all_to_all(
        jnp.broadcast_to(kept_count.reshape(1, 1), (shards, 1)), "seq", 0, 0, tiled=True
    ).reshape(shards)
    shard_ids = jnp.arange(shards, dtype=jnp.int32)
    per_peer = -(-list_slots // shards)
    starts = jnp.cumsum(count_table) - count_table
    before = jnp.sum(jnp.where(shard_ids < my_index, count_table, 0))
    slot_ids = jnp.arange(per_peer, dtype=jnp.int32)
    pick = (shard_ids[:, None] - before) % shards + slot_ids[None, :] * shards
    pick_ok = pick < kept_count
    pick_safe = jnp.minimum(pick, list_slots - 1)
    send_tokens = jnp.where(
        pick_ok[:, :, None], kept_tokens[pick_safe], jnp.zeros((), jnp.bfloat16)
    )
    send_target = jnp.where(
        pick_ok[:, :, None], kept_target[pick_safe], jnp.zeros((), jnp.bfloat16)
    )
    got_both = lax.all_to_all(
        jnp.concatenate([send_tokens, send_target], axis=2), "seq", split_axis=0, concat_axis=0, tiled=True
    )
    from_pick = (my_index - starts[:, None]) % shards + slot_ids[None, :] * shards
    from_ok = from_pick < count_table[:, None]
    place = jnp.where(from_ok, (starts[:, None] + from_pick) // shards, TOK_DEV).reshape(-1)
    width = send_tokens.shape[2]
    both = (
        jnp.zeros((TOK_DEV, 2 * width), jnp.bfloat16)
        .at[place]
        .set(got_both.reshape(-1, 2 * width), mode="drop")
    )
    tokens = both[:, :width]
    target = both[:, width:]
    rows = tokens.shape[0]
    inner = w_out.shape[0]
    heads = inner // HEAD_DIM
    normed, hidden = layer_norm(tokens, ln_gain)
    queries = (
        jnp.dot(hidden, w_qkv[:, :inner], preferred_element_type=jnp.float32)
        .astype(jnp.bfloat16)
        .reshape(rows, heads, HEAD_DIM)
        .transpose(1, 0, 2)
    )
    pair_cols = jnp.dot(w_qkv[:, inner:].T, hidden.T, preferred_element_type=jnp.float32).astype(
        jnp.bfloat16
    )
    gathered = gather_blocks(pair_cols)
    split_kv = gathered.reshape(shards, heads, 2, HEAD_DIM, rows)
    keys_b = split_kv[:, :, 0]
    values_b = split_kv[:, :, 1]
    queries_b = jnp.broadcast_to(queries[None], (shards,) + queries.shape)
    scores = (
        jnp.einsum("ihqd,ihdt->ihqt", queries_b, keys_b, preferred_element_type=jnp.float32) * 0.125
    )
    row_max = jnp.max(scores, axis=(0, 3))
    weights = jnp.exp(scores - row_max[None, :, :, None])
    row_sum = jnp.sum(weights, axis=(0, 3))
    blended = jnp.sum(
        jnp.einsum(
            "ihqt,ihdt->ihqd", weights.astype(jnp.bfloat16), values_b, preferred_element_type=jnp.float32
        ),
        axis=0,
    )
    log_total = row_max + jnp.log(row_sum)
    attended = (
        (blended / row_sum[:, :, None]).transpose(1, 0, 2).reshape(rows, inner).astype(jnp.bfloat16)
    )
    student = tokens.astype(jnp.float32) + jnp.dot(
        attended, w_out, preferred_element_type=jnp.float32
    )
    token_loss, grad_y = align_terms(student, target)
    grad_b = grad_y.astype(jnp.bfloat16)
    grad_wout = jnp.dot(exchange_order(attended).T, grad_b, preferred_element_type=jnp.float32)
    grad_heads = (
        jnp.dot(grad_b, w_out.T, preferred_element_type=jnp.float32)
        .astype(jnp.bfloat16)
        .reshape(rows, heads, HEAD_DIM)
        .transpose(1, 0, 2)
    )
    row_dot = jnp.sum(
        grad_heads.astype(jnp.float32)
        * attended.reshape(rows, heads, HEAD_DIM).transpose(1, 0, 2).astype(jnp.float32),
        axis=2,
    )
    prob_full = jnp.exp(scores - log_total[None, :, :, None])
    grad_heads_b = jnp.broadcast_to(grad_heads[None], (shards,) + grad_heads.shape)
    d_value_b = jnp.einsum(
        "ihqd,ihqt->ihdt", grad_heads_b, prob_full.astype(jnp.bfloat16), preferred_element_type=jnp.float32
    )
    d_prob = jnp.einsum("ihqd,ihdt->ihqt", grad_heads_b, values_b, preferred_element_type=jnp.float32)
    d_score = (prob_full * (d_prob - row_dot[None, :, :, None])).astype(jnp.bfloat16)
    d_query_t = 0.125 * jnp.sum(
        jnp.einsum("ihqt,ihdt->ihdq", d_score, keys_b, preferred_element_type=jnp.float32), axis=0
    )
    d_key_b = 0.125 * jnp.einsum(
        "ihqd,ihqt->ihdt", queries_b, d_score, preferred_element_type=jnp.float32
    )
    half = shards // 2
    own_pairs = jnp.stack([d_key_b[:half], d_value_b[:half]], axis=2).reshape(half, 2 * inner, rows)
    other_pairs = jnp.stack([d_key_b[half:], d_value_b[half:]], axis=2).reshape(half, 2 * inner, rows)
    accum = return_blocks(own_pairs, other_pairs.astype(jnp.bfloat16))
    d_proj_t = jnp.concatenate([d_query_t.reshape(inner, rows), accum], axis=0).astype(jnp.bfloat16)
    grad_wqkv = jnp.einsum(
        "tf,ct->fc", exchange_order(hidden), d_proj_t, preferred_element_type=jnp.float32
    )
    d_hidden = jnp.einsum("ct,fc->tf", d_proj_t, w_qkv, preferred_element_type=jnp.float32)
    grad_ln = jnp.sum(d_hidden * normed, axis=0)
    loss_part = jnp.sum(token_loss)
    small = jnp.concatenate([grad_ln, loss_part.reshape(1)])
    grad_out, unused = halving_scatter(grad_wout)
    grad_qkv, small = halving_scatter(grad_wqkv, small)
    count_all = shards * lax.axis_size("clip") * TOK_DEV
    return (small[-1] / count_all, grad_qkv.reshape(-1), grad_out.reshape(-1), small[:-1])


def solution(mesh):
    placed = (P("clip", "seq", None), P("clip", "seq", None), P("clip", "seq"), P(), P(), P())
    return jax.shard_map(
        per_device,
        mesh=mesh,
        in_specs=placed,
        out_specs=(P(), P(("seq", "clip")), P(("seq", "clip")), P()),
        check_vma=False,
    )
```

```python
import jax
import jax.numpy as jnp
from jax import lax
from jax.sharding import PartitionSpec as P

HEAD_DIM = 64
TOK_DEV = 128


def shifted(value, axis, steps):
    count = lax.axis_size(axis)
    pairs = [(source, (source + steps) % count) for source in range(count)]
    return lax.ppermute(value, axis, pairs)


def layer_norm(tokens, ln_gain):
    values = tokens.astype(jnp.float32)
    center = values - jnp.mean(values, axis=-1, keepdims=True)
    spread = jnp.mean(center * center, axis=-1, keepdims=True)
    normed = center * lax.rsqrt(spread + 1e-05)
    return (normed, (normed * ln_gain).astype(jnp.bfloat16))


def align_terms(student, target):
    target_f = target.astype(jnp.float32)
    inv_y = lax.rsqrt(jnp.sum(student * student, axis=-1, keepdims=True) + 1e-06)
    inv_t = lax.rsqrt(jnp.sum(target_f * target_f, axis=-1, keepdims=True) + 1e-06)
    differ = student * inv_y - target_f * inv_t
    token_loss = jnp.sum(differ * differ, axis=-1)
    slopes = 2.0 * differ
    grad_y = inv_y * slopes - student * (inv_y * inv_y * inv_y) * jnp.sum(
        slopes * student, axis=-1, keepdims=True
    )
    return (token_loss, grad_y)


def key_mask(key_count, rows, heads):
    slot_idx = jnp.arange(rows, dtype=jnp.int32)
    halves = slot_idx[None, :] < key_count[:, None]
    return jnp.repeat(halves, heads // 2, axis=0)


def head_scores(queries, pair_rows, key_count):
    rows = pair_rows.shape[0]
    heads = queries.shape[1]
    split_kv = pair_rows.reshape(rows, heads, 2, HEAD_DIM)
    scores = (
        jnp.einsum("qhd,khd->hqk", queries, split_kv[:, :, 0], preferred_element_type=jnp.float32)
        * 0.125
    )
    mask_rows = key_mask(key_count, rows, heads)
    return (jnp.where(mask_rows[:, None, :], scores, -1e30), split_kv)


def absorb(state, queries, pair_rows, key_count):
    row_max, row_sum, blended = state
    scores, split_kv = head_scores(queries, pair_rows, key_count)
    new_max = jnp.maximum(row_max, jnp.max(scores, axis=2))
    rescale = jnp.exp(row_max - new_max)
    weights = jnp.exp(scores - new_max[:, :, None])
    row_sum = row_sum * rescale + jnp.sum(weights, axis=2)
    blended = blended * rescale[:, :, None] + jnp.einsum(
        "hqk,khd->hqd",
        weights.astype(jnp.bfloat16),
        split_kv[:, :, 1],
        preferred_element_type=jnp.float32,
    )
    return (new_max, row_sum, blended)


def contribution(queries, grad_heads, log_total, row_dot, pair_rows, key_count):
    scores, split_kv = head_scores(queries, pair_rows, key_count)
    prob_full = jnp.exp(scores - log_total[:, :, None])
    d_value = jnp.einsum(
        "hqk,qhd->khd",
        prob_full.astype(jnp.bfloat16),
        grad_heads,
        preferred_element_type=jnp.float32,
    )
    d_prob = jnp.einsum(
        "qhd,khd->hqk", grad_heads, split_kv[:, :, 1], preferred_element_type=jnp.float32
    )
    d_score = (prob_full * (d_prob - row_dot[:, :, None])).astype(jnp.bfloat16)
    d_query = 0.125 * jnp.einsum(
        "hqk,khd->qhd", d_score, split_kv[:, :, 0], preferred_element_type=jnp.float32
    )
    d_key = 0.125 * jnp.einsum("hqk,qhd->khd", d_score, queries, preferred_element_type=jnp.float32)
    rows = pair_rows.shape[0]
    return (d_query, jnp.stack([d_key, d_value], axis=2).reshape(rows, -1))


def move_keys(pair_rows):
    moved = shifted(pair_rows, "seq", 1)
    return moved


def move_grads(accum):
    moved = shifted(accum.astype(jnp.bfloat16), "seq", 1).astype(accum.dtype)
    return moved


def exchange_bits():
    seq_bits = lax.axis_size("seq").bit_length() - 1
    clip_bits = lax.axis_size("clip").bit_length() - 1
    assert (1 << seq_bits) == lax.axis_size("seq")
    assert (1 << clip_bits) == lax.axis_size("clip")
    return seq_bits, clip_bits


def exchange_order(values):
    seq_bits, clip_bits = exchange_bits()
    total = seq_bits + clip_bits
    lead = values.shape[0]
    split = values.reshape([lead] + [2] * total + [-1])
    seq_dims = [1 + seq_bits - 1 - bit for bit in range(seq_bits)]
    clip_dims = [1 + seq_bits + clip_bits - 1 - bit for bit in range(clip_bits)]
    perm = [0] + seq_dims + clip_dims + [total + 1]
    return split.transpose(perm).reshape(values.shape)


def halving_scatter(grad, small=None):
    seq_bits, clip_bits = exchange_bits()
    total = seq_bits + clip_bits
    seq_n = lax.axis_size("seq")
    clip_n = lax.axis_size("clip")
    data = grad.reshape([2] * total + [-1, grad.shape[1]])
    seq_keys = [("seq", bit) for bit in range(seq_bits)]
    clip_keys = [("clip", bit) for bit in range(clip_bits)]
    order_a = seq_keys + clip_keys
    order_b = [seq_keys[0]] + seq_keys[1:][::-1][:1] + clip_keys[:1] + seq_keys[1:][::-1][1:] + clip_keys[1:]
    me_seq = lax.axis_index("seq")
    me_clip = lax.axis_index("clip")
    core_bit = me_seq & 1
    left_a = list(order_a)
    left_b = list(order_a)

    def own_bit(key):
        axis, bit = key
        return ((me_seq if axis == "seq" else me_clip) >> bit) & 1

    def flip(seq_i, clip_i, key):
        axis, bit = key
        if axis == "seq":
            return (seq_i ^ (1 << bit)) * clip_n + clip_i
        return seq_i * clip_n + (clip_i ^ (1 << bit))

    for step in range(total):
        key_a, key_b = order_a[step], order_b[step]
        dim_a, dim_b = left_a.index(key_a), left_b.index(key_b)
        mine_a, mine_b = own_bit(key_a), own_bit(key_b)
        pairs = []
        for seq_i in range(seq_n):
            for clip_i in range(clip_n):
                key = key_a if (seq_i & 1) == 0 else key_b
                pairs.append((seq_i * clip_n + clip_i, flip(seq_i, clip_i, key)))
        keep = jnp.where(
            core_bit == 0,
            lax.dynamic_index_in_dim(data, mine_a, axis=dim_a, keepdims=False),
            lax.dynamic_index_in_dim(data, mine_b, axis=dim_b, keepdims=False),
        )
        give = jnp.where(
            core_bit == 0,
            lax.dynamic_index_in_dim(data, 1 - mine_a, axis=dim_a, keepdims=False),
            lax.dynamic_index_in_dim(data, 1 - mine_b, axis=dim_b, keepdims=False),
        )
        left_a.pop(dim_a)
        left_b.pop(dim_b)
        if small is None:
            got = lax.ppermute(give.astype(jnp.bfloat16), ("seq", "clip"), pairs)
        else:
            got, got_small = lax.ppermute((give.astype(jnp.bfloat16), small), ("seq", "clip"), pairs)
            small = small + got_small
        data = keep + got.astype(jnp.float32)
    return data, small


def xor_pairs(mask):
    count = lax.axis_size("seq")
    return [(src, src ^ mask) for src in range(count)]


def gather_blocks(block):
    half = lax.axis_size("seq") // 2
    same_core = [block] + [lax.ppermute(block, "seq", xor_pairs(2 * k)) for k in range(1, half)]
    group = jnp.stack(same_core)
    other = lax.ppermute(group, "seq", xor_pairs(1))
    return jnp.concatenate([group, other], axis=0)


def return_blocks(own_parts, other_parts):
    half = lax.axis_size("seq") // 2
    got = lax.ppermute(other_parts, "seq", xor_pairs(1))
    summed = own_parts.astype(jnp.bfloat16).astype(jnp.float32) + got.astype(jnp.float32)
    accum = summed[0]
    for k in range(1, half):
        sent = lax.ppermute(summed[k].astype(jnp.bfloat16), "seq", xor_pairs(2 * k))
        accum = accum + sent.astype(jnp.float32)
    return accum


def per_device(raw_tokens, teacher, keep_rows, w_qkv, w_out, ln_gain):
    shards = lax.axis_size("seq")
    my_index = lax.axis_index("seq")
    row_ids = keep_rows[0]
    list_slots = row_ids.shape[0]
    is_kept = row_ids >= 0
    kept_count = jnp.sum(is_kept.astype(jnp.int32))
    safe_ids = jnp.maximum(row_ids, 0)
    kept_tokens = jnp.where(is_kept[:, None], raw_tokens[0][safe_ids], jnp.zeros((), jnp.bfloat16))
    kept_target = jnp.where(is_kept[:, None], teacher[0][safe_ids], jnp.zeros((), jnp.bfloat16))
    count_table = lax.all_to_all(
        jnp.broadcast_to(kept_count.reshape(1, 1), (shards, 1)), "seq", 0, 0, tiled=True
    ).reshape(shards)
    shard_ids = jnp.arange(shards, dtype=jnp.int32)
    per_peer = -(-list_slots // shards)
    starts = jnp.cumsum(count_table) - count_table
    before = jnp.sum(jnp.where(shard_ids < my_index, count_table, 0))
    slot_ids = jnp.arange(per_peer, dtype=jnp.int32)
    pick = (shard_ids[:, None] - before) % shards + slot_ids[None, :] * shards
    pick_ok = pick < kept_count
    pick_safe = jnp.minimum(pick, list_slots - 1)
    send_tokens = jnp.where(
        pick_ok[:, :, None], kept_tokens[pick_safe], jnp.zeros((), jnp.bfloat16)
    )
    send_target = jnp.where(
        pick_ok[:, :, None], kept_target[pick_safe], jnp.zeros((), jnp.bfloat16)
    )
    got_both = lax.all_to_all(
        jnp.concatenate([send_tokens, send_target], axis=2), "seq", split_axis=0, concat_axis=0, tiled=True
    )
    from_pick = (my_index - starts[:, None]) % shards + slot_ids[None, :] * shards
    from_ok = from_pick < count_table[:, None]
    place = jnp.where(from_ok, (starts[:, None] + from_pick) // shards, TOK_DEV).reshape(-1)
    width = send_tokens.shape[2]
    both = (
        jnp.zeros((TOK_DEV, 2 * width), jnp.bfloat16)
        .at[place]
        .set(got_both.reshape(-1, 2 * width), mode="drop")
    )
    tokens = both[:, :width]
    target = both[:, width:]
    rows = tokens.shape[0]
    inner = w_out.shape[0]
    heads = inner // HEAD_DIM
    normed, hidden = layer_norm(tokens, ln_gain)
    queries = (
        jnp.dot(hidden, w_qkv[:, :inner], preferred_element_type=jnp.float32)
        .astype(jnp.bfloat16)
        .reshape(rows, heads, HEAD_DIM)
        .transpose(1, 0, 2)
    )
    pair_cols = jnp.dot(w_qkv[:, inner:].T, hidden.T, preferred_element_type=jnp.float32).astype(
        jnp.bfloat16
    )
    gathered = gather_blocks(pair_cols)
    split_kv = gathered.reshape(shards, heads, 2, HEAD_DIM, rows)
    keys_b = split_kv[:, :, 0]
    values_b = split_kv[:, :, 1]
    queries_b = jnp.broadcast_to(queries[None], (shards,) + queries.shape)
    scores = (
        jnp.einsum("ihqd,ihdt->ihqt", queries_b, keys_b, preferred_element_type=jnp.float32) * 0.125
    )
    row_max = jnp.max(scores, axis=(0, 3))
    weights = jnp.exp(scores - row_max[None, :, :, None])
    row_sum = jnp.sum(weights, axis=(0, 3))
    blended = jnp.sum(
        jnp.einsum(
            "ihqt,ihdt->ihqd", weights.astype(jnp.bfloat16), values_b, preferred_element_type=jnp.float32
        ),
        axis=0,
    )
    log_total = row_max + jnp.log(row_sum)
    attended = (
        (blended / row_sum[:, :, None]).transpose(1, 0, 2).reshape(rows, inner).astype(jnp.bfloat16)
    )
    student = tokens.astype(jnp.float32) + jnp.dot(
        attended, w_out, preferred_element_type=jnp.float32
    )
    token_loss, grad_y = align_terms(student, target)
    grad_b = grad_y.astype(jnp.bfloat16)
    grad_wout = jnp.dot(exchange_order(attended).T, grad_b, preferred_element_type=jnp.float32)
    grad_heads = (
        jnp.dot(grad_b, w_out.T, preferred_element_type=jnp.float32)
        .astype(jnp.bfloat16)
        .reshape(rows, heads, HEAD_DIM)
        .transpose(1, 0, 2)
    )
    row_dot = jnp.sum(
        grad_heads.astype(jnp.float32)
        * attended.reshape(rows, heads, HEAD_DIM).transpose(1, 0, 2).astype(jnp.float32),
        axis=2,
    )
    prob_full = jnp.exp(scores - log_total[None, :, :, None])
    grad_heads_b = jnp.broadcast_to(grad_heads[None], (shards,) + grad_heads.shape)
    d_value_b = jnp.einsum(
        "ihqd,ihqt->ihdt", grad_heads_b, prob_full.astype(jnp.bfloat16), preferred_element_type=jnp.float32
    )
    d_prob = jnp.einsum("ihqd,ihdt->ihqt", grad_heads_b, values_b, preferred_element_type=jnp.float32)
    d_score = (prob_full * (d_prob - row_dot[None, :, :, None])).astype(jnp.bfloat16)
    d_query_t = 0.125 * jnp.sum(
        jnp.einsum("ihqt,ihdt->ihdq", d_score, keys_b, preferred_element_type=jnp.float32), axis=0
    )
    d_key_b = 0.125 * jnp.einsum(
        "ihqd,ihqt->ihdt", queries_b, d_score, preferred_element_type=jnp.float32
    )
    half = shards // 2
    own_pairs = jnp.stack([d_key_b[:half], d_value_b[:half]], axis=2).reshape(half, 2 * inner, rows)
    other_pairs = jnp.stack([d_key_b[half:], d_value_b[half:]], axis=2).reshape(half, 2 * inner, rows)
    accum = return_blocks(own_pairs, other_pairs.astype(jnp.bfloat16))
    d_proj_t = jnp.concatenate([d_query_t.reshape(inner, rows), accum], axis=0).astype(jnp.bfloat16)
    grad_wqkv = jnp.einsum(
        "tf,ct->fc", exchange_order(hidden), d_proj_t, preferred_element_type=jnp.float32
    )
    d_hidden = jnp.einsum("ct,fc->tf", d_proj_t, w_qkv, preferred_element_type=jnp.float32)
    grad_ln = jnp.sum(d_hidden * normed, axis=0)
    loss_part = jnp.sum(token_loss)
    small = jnp.concatenate([grad_ln, loss_part.reshape(1)])
    grad_out, unused = halving_scatter(grad_wout)
    grad_qkv, small = halving_scatter(grad_wqkv, small)
    count_all = shards * lax.axis_size("clip") * TOK_DEV
    return (small[-1] / count_all, grad_qkv.reshape(-1), grad_out.reshape(-1), small[:-1])


def solution(mesh):
    placed = (P("clip", "seq", None), P("clip", "seq", None), P("clip", "seq"), P(), P(), P())
    return jax.shard_map(
        per_device,
        mesh=mesh,
        in_specs=placed,
        out_specs=(P(), P(("seq", "clip")), P(("seq", "clip")), P()),
        check_vma=False,
    )
```

```python
import jax
import jax.numpy as jnp
from jax import lax
from jax.sharding import PartitionSpec as P

HEAD_DIM = 64
TOK_DEV = 128


def shifted(value, axis, steps):
    count = lax.axis_size(axis)
    pairs = [(source, (source + steps) % count) for source in range(count)]
    return lax.ppermute(value, axis, pairs)


def layer_norm(tokens, ln_gain):
    values = tokens.astype(jnp.float32)
    center = values - jnp.mean(values, axis=-1, keepdims=True)
    spread = jnp.mean(center * center, axis=-1, keepdims=True)
    normed = center * lax.rsqrt(spread + 1e-05)
    return (normed, (normed * ln_gain).astype(jnp.bfloat16))


def align_terms(student, target):
    target_f = target.astype(jnp.float32)
    inv_y = lax.rsqrt(jnp.sum(student * student, axis=-1, keepdims=True) + 1e-06)
    inv_t = lax.rsqrt(jnp.sum(target_f * target_f, axis=-1, keepdims=True) + 1e-06)
    differ = student * inv_y - target_f * inv_t
    token_loss = jnp.sum(differ * differ, axis=-1)
    slopes = 2.0 * differ
    grad_y = inv_y * slopes - student * (inv_y * inv_y * inv_y) * jnp.sum(
        slopes * student, axis=-1, keepdims=True
    )
    return (token_loss, grad_y)


def key_mask(key_count, rows, heads):
    slot_idx = jnp.arange(rows, dtype=jnp.int32)
    halves = slot_idx[None, :] < key_count[:, None]
    return jnp.repeat(halves, heads // 2, axis=0)


def head_scores(queries, pair_rows, key_count):
    rows = pair_rows.shape[0]
    heads = queries.shape[1]
    split_kv = pair_rows.reshape(rows, heads, 2, HEAD_DIM)
    scores = (
        jnp.einsum("qhd,khd->hqk", queries, split_kv[:, :, 0], preferred_element_type=jnp.float32)
        * 0.125
    )
    mask_rows = key_mask(key_count, rows, heads)
    return (jnp.where(mask_rows[:, None, :], scores, -1e30), split_kv)


def absorb(state, queries, pair_rows, key_count):
    row_max, row_sum, blended = state
    scores, split_kv = head_scores(queries, pair_rows, key_count)
    new_max = jnp.maximum(row_max, jnp.max(scores, axis=2))
    rescale = jnp.exp(row_max - new_max)
    weights = jnp.exp(scores - new_max[:, :, None])
    row_sum = row_sum * rescale + jnp.sum(weights, axis=2)
    blended = blended * rescale[:, :, None] + jnp.einsum(
        "hqk,khd->hqd",
        weights.astype(jnp.bfloat16),
        split_kv[:, :, 1],
        preferred_element_type=jnp.float32,
    )
    return (new_max, row_sum, blended)


def contribution(queries, grad_heads, log_total, row_dot, pair_rows, key_count):
    scores, split_kv = head_scores(queries, pair_rows, key_count)
    prob_full = jnp.exp(scores - log_total[:, :, None])
    d_value = jnp.einsum(
        "hqk,qhd->khd",
        prob_full.astype(jnp.bfloat16),
        grad_heads,
        preferred_element_type=jnp.float32,
    )
    d_prob = jnp.einsum(
        "qhd,khd->hqk", grad_heads, split_kv[:, :, 1], preferred_element_type=jnp.float32
    )
    d_score = (prob_full * (d_prob - row_dot[:, :, None])).astype(jnp.bfloat16)
    d_query = 0.125 * jnp.einsum(
        "hqk,khd->qhd", d_score, split_kv[:, :, 0], preferred_element_type=jnp.float32
    )
    d_key = 0.125 * jnp.einsum("hqk,qhd->khd", d_score, queries, preferred_element_type=jnp.float32)
    rows = pair_rows.shape[0]
    return (d_query, jnp.stack([d_key, d_value], axis=2).reshape(rows, -1))


def move_keys(pair_rows):
    moved = shifted(pair_rows, "seq", 1)
    return moved


def move_grads(accum):
    moved = shifted(accum.astype(jnp.bfloat16), "seq", 1).astype(accum.dtype)
    return moved


def exchange_bits():
    seq_bits = lax.axis_size("seq").bit_length() - 1
    clip_bits = lax.axis_size("clip").bit_length() - 1
    assert (1 << seq_bits) == lax.axis_size("seq")
    assert (1 << clip_bits) == lax.axis_size("clip")
    return seq_bits, clip_bits


def exchange_order(values):
    seq_bits, clip_bits = exchange_bits()
    total = seq_bits + clip_bits
    lead = values.shape[0]
    split = values.reshape([lead] + [2] * total + [-1])
    seq_dims = [1 + seq_bits - 1 - bit for bit in range(seq_bits)]
    clip_dims = [1 + seq_bits + clip_bits - 1 - bit for bit in range(clip_bits)]
    perm = [0] + seq_dims + clip_dims + [total + 1]
    return split.transpose(perm).reshape(values.shape)


def halving_scatter(grad, small=None):
    seq_bits, clip_bits = exchange_bits()
    total = seq_bits + clip_bits
    seq_n = lax.axis_size("seq")
    clip_n = lax.axis_size("clip")
    data = grad.reshape([2] * total + [-1, grad.shape[1]])
    seq_keys = [("seq", bit) for bit in range(seq_bits)]
    clip_keys = [("clip", bit) for bit in range(clip_bits)]
    order_a = seq_keys + clip_keys
    order_b = [seq_keys[0]] + seq_keys[1:][::-1][:1] + clip_keys[:1] + seq_keys[1:][::-1][1:] + clip_keys[1:]
    me_seq = lax.axis_index("seq")
    me_clip = lax.axis_index("clip")
    core_bit = me_seq & 1
    left_a = list(order_a)
    left_b = list(order_a)

    def own_bit(key):
        axis, bit = key
        return ((me_seq if axis == "seq" else me_clip) >> bit) & 1

    def flip(seq_i, clip_i, key):
        axis, bit = key
        if axis == "seq":
            return (seq_i ^ (1 << bit)) * clip_n + clip_i
        return seq_i * clip_n + (clip_i ^ (1 << bit))

    for step in range(total):
        key_a, key_b = order_a[step], order_b[step]
        dim_a, dim_b = left_a.index(key_a), left_b.index(key_b)
        mine_a, mine_b = own_bit(key_a), own_bit(key_b)
        pairs = []
        for seq_i in range(seq_n):
            for clip_i in range(clip_n):
                key = key_a if (seq_i & 1) == 0 else key_b
                pairs.append((seq_i * clip_n + clip_i, flip(seq_i, clip_i, key)))
        keep = jnp.where(
            core_bit == 0,
            lax.dynamic_index_in_dim(data, mine_a, axis=dim_a, keepdims=False),
            lax.dynamic_index_in_dim(data, mine_b, axis=dim_b, keepdims=False),
        )
        give = jnp.where(
            core_bit == 0,
            lax.dynamic_index_in_dim(data, 1 - mine_a, axis=dim_a, keepdims=False),
            lax.dynamic_index_in_dim(data, 1 - mine_b, axis=dim_b, keepdims=False),
        )
        left_a.pop(dim_a)
        left_b.pop(dim_b)
        if small is None:
            got = lax.ppermute(give.astype(jnp.bfloat16), ("seq", "clip"), pairs)
        else:
            got, got_small = lax.ppermute((give.astype(jnp.bfloat16), small), ("seq", "clip"), pairs)
            small = small + got_small
        data = keep + got.astype(jnp.float32)
    return data, small


def xor_pairs(mask):
    count = lax.axis_size("seq")
    return [(src, src ^ mask) for src in range(count)]


def gather_blocks(block):
    half = lax.axis_size("seq") // 2
    same_core = [block] + [lax.ppermute(block, "seq", xor_pairs(2 * k)) for k in range(1, half)]
    group = jnp.stack(same_core)
    other = lax.ppermute(group, "seq", xor_pairs(1))
    return jnp.concatenate([group, other], axis=0)


def return_blocks(own_parts, other_parts):
    half = lax.axis_size("seq") // 2
    got = lax.ppermute(other_parts, "seq", xor_pairs(1))
    summed = own_parts.astype(jnp.bfloat16).astype(jnp.float32) + got.astype(jnp.float32)
    accum = summed[0]
    for k in range(1, half):
        sent = lax.ppermute(summed[k].astype(jnp.bfloat16), "seq", xor_pairs(2 * k))
        accum = accum + sent.astype(jnp.float32)
    return accum


def per_device(raw_tokens, teacher, keep_rows, w_qkv, w_out, ln_gain):
    shards = lax.axis_size("seq")
    my_index = lax.axis_index("seq")
    row_ids = keep_rows[0]
    list_slots = row_ids.shape[0]
    is_kept = row_ids >= 0
    kept_count = jnp.sum(is_kept.astype(jnp.int32))
    safe_ids = jnp.maximum(row_ids, 0)
    kept_tokens = jnp.where(is_kept[:, None], raw_tokens[0][safe_ids], jnp.zeros((), jnp.bfloat16))
    kept_target = jnp.where(is_kept[:, None], teacher[0][safe_ids], jnp.zeros((), jnp.bfloat16))
    count_table = lax.all_to_all(
        jnp.broadcast_to(kept_count.reshape(1, 1), (shards, 1)), "seq", 0, 0, tiled=True
    ).reshape(shards)
    shard_ids = jnp.arange(shards, dtype=jnp.int32)
    per_peer = -(-list_slots // shards)
    starts = jnp.cumsum(count_table) - count_table
    before = jnp.sum(jnp.where(shard_ids < my_index, count_table, 0))
    slot_ids = jnp.arange(per_peer, dtype=jnp.int32)
    pick = (shard_ids[:, None] - before) % shards + slot_ids[None, :] * shards
    pick_ok = pick < kept_count
    pick_safe = jnp.minimum(pick, list_slots - 1)
    send_tokens = jnp.where(
        pick_ok[:, :, None], kept_tokens[pick_safe], jnp.zeros((), jnp.bfloat16)
    )
    send_target = jnp.where(
        pick_ok[:, :, None], kept_target[pick_safe], jnp.zeros((), jnp.bfloat16)
    )
    got_both = lax.all_to_all(
        jnp.concatenate([send_tokens, send_target], axis=2), "seq", split_axis=0, concat_axis=0, tiled=True
    )
    from_pick = (my_index - starts[:, None]) % shards + slot_ids[None, :] * shards
    from_ok = from_pick < count_table[:, None]
    place = jnp.where(from_ok, (starts[:, None] + from_pick) // shards, TOK_DEV).reshape(-1)
    width = send_tokens.shape[2]
    both = (
        jnp.zeros((TOK_DEV, 2 * width), jnp.bfloat16)
        .at[place]
        .set(got_both.reshape(-1, 2 * width), mode="drop")
    )
    tokens = both[:, :width]
    target = both[:, width:]
    rows = tokens.shape[0]
    inner = w_out.shape[0]
    heads = inner // HEAD_DIM
    normed, hidden = layer_norm(tokens, ln_gain)
    queries = (
        jnp.dot(hidden, w_qkv[:, :inner], preferred_element_type=jnp.float32)
        .astype(jnp.bfloat16)
        .reshape(rows, heads, HEAD_DIM)
        .transpose(1, 0, 2)
    )
    pair_cols = jnp.dot(w_qkv[:, inner:].T, hidden.T, preferred_element_type=jnp.float32).astype(
        jnp.bfloat16
    )
    gathered = gather_blocks(pair_cols)
    split_kv = gathered.reshape(shards, heads, 2, HEAD_DIM, rows)
    keys_b = split_kv[:, :, 0]
    values_b = split_kv[:, :, 1]
    queries_b = jnp.broadcast_to(queries[None], (shards,) + queries.shape)
    scores = (
        jnp.einsum("ihqd,ihdt->ihqt", queries_b, keys_b, preferred_element_type=jnp.float32) * 0.125
    )
    row_max = jnp.max(scores, axis=(0, 3))
    weights = jnp.exp(scores - row_max[None, :, :, None])
    row_sum = jnp.sum(weights, axis=(0, 3))
    blended = jnp.sum(
        jnp.einsum(
            "ihqt,ihdt->ihqd", weights.astype(jnp.bfloat16), values_b, preferred_element_type=jnp.float32
        ),
        axis=0,
    )
    log_total = row_max + jnp.log(row_sum)
    attended = (
        (blended / row_sum[:, :, None]).transpose(1, 0, 2).reshape(rows, inner).astype(jnp.bfloat16)
    )
    student = tokens.astype(jnp.float32) + jnp.dot(
        attended, w_out, preferred_element_type=jnp.float32
    )
    token_loss, grad_y = align_terms(student, target)
    grad_b = grad_y.astype(jnp.bfloat16)
    grad_wout = jnp.dot(exchange_order(attended).T, grad_b, preferred_element_type=jnp.float32)
    grad_heads = (
        jnp.dot(grad_b, w_out.T, preferred_element_type=jnp.float32)
        .astype(jnp.bfloat16)
        .reshape(rows, heads, HEAD_DIM)
        .transpose(1, 0, 2)
    )
    row_dot = jnp.sum(
        grad_heads.astype(jnp.float32)
        * attended.reshape(rows, heads, HEAD_DIM).transpose(1, 0, 2).astype(jnp.float32),
        axis=2,
    )
    prob_full = jnp.exp(scores - log_total[None, :, :, None])
    grad_heads_b = jnp.broadcast_to(grad_heads[None], (shards,) + grad_heads.shape)
    d_value_b = jnp.einsum(
        "ihqd,ihqt->ihdt", grad_heads_b, prob_full.astype(jnp.bfloat16), preferred_element_type=jnp.float32
    )
    d_prob = jnp.einsum("ihqd,ihdt->ihqt", grad_heads_b, values_b, preferred_element_type=jnp.float32)
    d_score = (prob_full * (d_prob - row_dot[None, :, :, None])).astype(jnp.bfloat16)
    d_query_t = 0.125 * jnp.sum(
        jnp.einsum("ihqt,ihdt->ihdq", d_score, keys_b, preferred_element_type=jnp.float32), axis=0
    )
    d_key_b = 0.125 * jnp.einsum(
        "ihqd,ihqt->ihdt", queries_b, d_score, preferred_element_type=jnp.float32
    )
    half = shards // 2
    own_pairs = jnp.stack([d_key_b[:half], d_value_b[:half]], axis=2).reshape(half, 2 * inner, rows)
    other_pairs = jnp.stack([d_key_b[half:], d_value_b[half:]], axis=2).reshape(half, 2 * inner, rows)
    accum = return_blocks(own_pairs, other_pairs.astype(jnp.bfloat16))
    d_proj_t = jnp.concatenate([d_query_t.reshape(inner, rows), accum], axis=0).astype(jnp.bfloat16)
    grad_wqkv = jnp.einsum(
        "tf,ct->fc", exchange_order(hidden), d_proj_t, preferred_element_type=jnp.float32
    )
    d_hidden = jnp.einsum("ct,fc->tf", d_proj_t, w_qkv, preferred_element_type=jnp.float32)
    grad_ln = jnp.sum(d_hidden * normed, axis=0)
    loss_part = jnp.sum(token_loss)
    small = jnp.concatenate([grad_ln, loss_part.reshape(1)])
    blocks = shards * lax.axis_size("clip")
    width = grad_wout.shape[1]
    extra = jnp.zeros((2, width), jnp.float32).at[0].set(grad_ln).at[1, 0].set(loss_part)
    joined = jnp.concatenate(
        [grad_wout.reshape(blocks, -1, width), jnp.broadcast_to(extra[None], (blocks, 2, width))], axis=1
    )
    joined, unused = halving_scatter(joined.reshape(-1, width))
    grad_qkv, unused = halving_scatter(grad_wqkv)
    grad_out = joined[:-2]
    small = jnp.concatenate([joined[-2], joined[-1, :1]])
    count_all = shards * lax.axis_size("clip") * TOK_DEV
    return (small[-1] / count_all, grad_qkv.reshape(-1), grad_out.reshape(-1), small[:-1])


def solution(mesh):
    placed = (P("clip", "seq", None), P("clip", "seq", None), P("clip", "seq"), P(), P(), P())
    return jax.shard_map(
        per_device,
        mesh=mesh,
        in_specs=placed,
        out_specs=(P(), P(("seq", "clip")), P(("seq", "clip")), P()),
        check_vma=False,
    )
```

```python
import jax
import jax.numpy as jnp
from jax import lax
from jax.sharding import PartitionSpec as P

HEAD_DIM = 64
TOK_DEV = 128


def shifted(value, axis, steps):
    count = lax.axis_size(axis)
    pairs = [(source, (source + steps) % count) for source in range(count)]
    return lax.ppermute(value, axis, pairs)


def layer_norm(tokens, ln_gain):
    values = tokens.astype(jnp.float32)
    center = values - jnp.mean(values, axis=-1, keepdims=True)
    spread = jnp.mean(center * center, axis=-1, keepdims=True)
    normed = center * lax.rsqrt(spread + 1e-05)
    return (normed, (normed * ln_gain).astype(jnp.bfloat16))


def align_terms(student, target):
    target_f = target.astype(jnp.float32)
    inv_y = lax.rsqrt(jnp.sum(student * student, axis=-1, keepdims=True) + 1e-06)
    inv_t = lax.rsqrt(jnp.sum(target_f * target_f, axis=-1, keepdims=True) + 1e-06)
    differ = student * inv_y - target_f * inv_t
    token_loss = jnp.sum(differ * differ, axis=-1)
    slopes = 2.0 * differ
    grad_y = inv_y * slopes - student * (inv_y * inv_y * inv_y) * jnp.sum(
        slopes * student, axis=-1, keepdims=True
    )
    return (token_loss, grad_y)


def key_mask(key_count, rows, heads):
    slot_idx = jnp.arange(rows, dtype=jnp.int32)
    halves = slot_idx[None, :] < key_count[:, None]
    return jnp.repeat(halves, heads // 2, axis=0)


def head_scores(queries, pair_rows, key_count):
    rows = pair_rows.shape[0]
    heads = queries.shape[1]
    split_kv = pair_rows.reshape(rows, heads, 2, HEAD_DIM)
    scores = (
        jnp.einsum("qhd,khd->hqk", queries, split_kv[:, :, 0], preferred_element_type=jnp.float32)
        * 0.125
    )
    mask_rows = key_mask(key_count, rows, heads)
    return (jnp.where(mask_rows[:, None, :], scores, -1e30), split_kv)


def absorb(state, queries, pair_rows, key_count):
    row_max, row_sum, blended = state
    scores, split_kv = head_scores(queries, pair_rows, key_count)
    new_max = jnp.maximum(row_max, jnp.max(scores, axis=2))
    rescale = jnp.exp(row_max - new_max)
    weights = jnp.exp(scores - new_max[:, :, None])
    row_sum = row_sum * rescale + jnp.sum(weights, axis=2)
    blended = blended * rescale[:, :, None] + jnp.einsum(
        "hqk,khd->hqd",
        weights.astype(jnp.bfloat16),
        split_kv[:, :, 1],
        preferred_element_type=jnp.float32,
    )
    return (new_max, row_sum, blended)


def contribution(queries, grad_heads, log_total, row_dot, pair_rows, key_count):
    scores, split_kv = head_scores(queries, pair_rows, key_count)
    prob_full = jnp.exp(scores - log_total[:, :, None])
    d_value = jnp.einsum(
        "hqk,qhd->khd",
        prob_full.astype(jnp.bfloat16),
        grad_heads,
        preferred_element_type=jnp.float32,
    )
    d_prob = jnp.einsum(
        "qhd,khd->hqk", grad_heads, split_kv[:, :, 1], preferred_element_type=jnp.float32
    )
    d_score = (prob_full * (d_prob - row_dot[:, :, None])).astype(jnp.bfloat16)
    d_query = 0.125 * jnp.einsum(
        "hqk,khd->qhd", d_score, split_kv[:, :, 0], preferred_element_type=jnp.float32
    )
    d_key = 0.125 * jnp.einsum("hqk,qhd->khd", d_score, queries, preferred_element_type=jnp.float32)
    rows = pair_rows.shape[0]
    return (d_query, jnp.stack([d_key, d_value], axis=2).reshape(rows, -1))


def move_keys(pair_rows):
    moved = shifted(pair_rows, "seq", 1)
    return moved


def move_grads(accum):
    moved = shifted(accum.astype(jnp.bfloat16), "seq", 1).astype(accum.dtype)
    return moved


def exchange_bits():
    seq_bits = lax.axis_size("seq").bit_length() - 1
    clip_bits = lax.axis_size("clip").bit_length() - 1
    assert (1 << seq_bits) == lax.axis_size("seq")
    assert (1 << clip_bits) == lax.axis_size("clip")
    return seq_bits, clip_bits


def exchange_order(values):
    seq_bits, clip_bits = exchange_bits()
    total = seq_bits + clip_bits
    lead = values.shape[0]
    split = values.reshape([lead] + [2] * total + [-1])
    seq_dims = [1 + seq_bits - 1 - bit for bit in range(seq_bits)]
    clip_dims = [1 + seq_bits + clip_bits - 1 - bit for bit in range(clip_bits)]
    perm = [0] + seq_dims + clip_dims + [total + 1]
    return split.transpose(perm).reshape(values.shape)


def halving_scatter(grad, small=None):
    seq_bits, clip_bits = exchange_bits()
    total = seq_bits + clip_bits
    seq_n = lax.axis_size("seq")
    clip_n = lax.axis_size("clip")
    data = grad.reshape([2] * total + [-1, grad.shape[1]])
    seq_keys = [("seq", bit) for bit in range(seq_bits)]
    clip_keys = [("clip", bit) for bit in range(clip_bits)]
    order_a = seq_keys + clip_keys
    order_b = [seq_keys[0]] + seq_keys[1:][::-1][:1] + clip_keys[:1] + seq_keys[1:][::-1][1:] + clip_keys[1:]
    me_seq = lax.axis_index("seq")
    me_clip = lax.axis_index("clip")
    core_bit = me_seq & 1
    left_a = list(order_a)
    left_b = list(order_a)

    def own_bit(key):
        axis, bit = key
        return ((me_seq if axis == "seq" else me_clip) >> bit) & 1

    def flip(seq_i, clip_i, key):
        axis, bit = key
        if axis == "seq":
            return (seq_i ^ (1 << bit)) * clip_n + clip_i
        return seq_i * clip_n + (clip_i ^ (1 << bit))

    for step in range(total):
        key_a, key_b = order_a[step], order_b[step]
        dim_a, dim_b = left_a.index(key_a), left_b.index(key_b)
        mine_a, mine_b = own_bit(key_a), own_bit(key_b)
        pairs = []
        for seq_i in range(seq_n):
            for clip_i in range(clip_n):
                key = key_a if (seq_i & 1) == 0 else key_b
                pairs.append((seq_i * clip_n + clip_i, flip(seq_i, clip_i, key)))
        keep = jnp.where(
            core_bit == 0,
            lax.dynamic_index_in_dim(data, mine_a, axis=dim_a, keepdims=False),
            lax.dynamic_index_in_dim(data, mine_b, axis=dim_b, keepdims=False),
        )
        give = jnp.where(
            core_bit == 0,
            lax.dynamic_index_in_dim(data, 1 - mine_a, axis=dim_a, keepdims=False),
            lax.dynamic_index_in_dim(data, 1 - mine_b, axis=dim_b, keepdims=False),
        )
        left_a.pop(dim_a)
        left_b.pop(dim_b)
        if small is None:
            got = lax.ppermute(give.astype(jnp.bfloat16), ("seq", "clip"), pairs)
        else:
            got, got_small = lax.ppermute((give.astype(jnp.bfloat16), small), ("seq", "clip"), pairs)
            small = small + got_small
        data = keep + got.astype(jnp.float32)
    return data, small


def xor_pairs(mask):
    count = lax.axis_size("seq")
    return [(src, src ^ mask) for src in range(count)]


def gather_blocks(block):
    half = lax.axis_size("seq") // 2
    same_core = [block] + [lax.ppermute(block, "seq", xor_pairs(2 * k)) for k in range(1, half)]
    group = jnp.stack(same_core)
    other = lax.ppermute(group, "seq", xor_pairs(1))
    return jnp.concatenate([group, other], axis=0)


def return_blocks(own_parts, other_parts):
    half = lax.axis_size("seq") // 2
    got = lax.ppermute(other_parts, "seq", xor_pairs(1))
    summed = own_parts + got.astype(jnp.float32)
    accum = summed[0]
    for k in range(1, half):
        sent = lax.ppermute(summed[k].astype(jnp.bfloat16), "seq", xor_pairs(2 * k))
        accum = accum + sent.astype(jnp.float32)
    return accum


def per_device(raw_tokens, teacher, keep_rows, w_qkv, w_out, ln_gain):
    shards = lax.axis_size("seq")
    my_index = lax.axis_index("seq")
    row_ids = keep_rows[0]
    list_slots = row_ids.shape[0]
    is_kept = row_ids >= 0
    kept_count = jnp.sum(is_kept.astype(jnp.int32))
    safe_ids = jnp.maximum(row_ids, 0)
    kept_tokens = jnp.where(is_kept[:, None], raw_tokens[0][safe_ids], jnp.zeros((), jnp.bfloat16))
    kept_target = jnp.where(is_kept[:, None], teacher[0][safe_ids], jnp.zeros((), jnp.bfloat16))
    count_table = lax.all_to_all(
        jnp.broadcast_to(kept_count.reshape(1, 1), (shards, 1)), "seq", 0, 0, tiled=True
    ).reshape(shards)
    shard_ids = jnp.arange(shards, dtype=jnp.int32)
    per_peer = -(-list_slots // shards)
    starts = jnp.cumsum(count_table) - count_table
    before = jnp.sum(jnp.where(shard_ids < my_index, count_table, 0))
    slot_ids = jnp.arange(per_peer, dtype=jnp.int32)
    pick = (shard_ids[:, None] - before) % shards + slot_ids[None, :] * shards
    pick_ok = pick < kept_count
    pick_safe = jnp.minimum(pick, list_slots - 1)
    send_tokens = jnp.where(
        pick_ok[:, :, None], kept_tokens[pick_safe], jnp.zeros((), jnp.bfloat16)
    )
    send_target = jnp.where(
        pick_ok[:, :, None], kept_target[pick_safe], jnp.zeros((), jnp.bfloat16)
    )
    got_both = lax.all_to_all(
        jnp.concatenate([send_tokens, send_target], axis=2), "seq", split_axis=0, concat_axis=0, tiled=True
    )
    from_pick = (my_index - starts[:, None]) % shards + slot_ids[None, :] * shards
    from_ok = from_pick < count_table[:, None]
    place = jnp.where(from_ok, (starts[:, None] + from_pick) // shards, TOK_DEV).reshape(-1)
    width = send_tokens.shape[2]
    both = (
        jnp.zeros((TOK_DEV, 2 * width), jnp.bfloat16)
        .at[place]
        .set(got_both.reshape(-1, 2 * width), mode="drop")
    )
    tokens = both[:, :width]
    target = both[:, width:]
    rows = tokens.shape[0]
    inner = w_out.shape[0]
    heads = inner // HEAD_DIM
    normed, hidden = layer_norm(tokens, ln_gain)
    queries = (
        jnp.dot(hidden, w_qkv[:, :inner], preferred_element_type=jnp.float32)
        .astype(jnp.bfloat16)
        .reshape(rows, heads, HEAD_DIM)
        .transpose(1, 0, 2)
    )
    pair_cols = jnp.dot(w_qkv[:, inner:].T, hidden.T, preferred_element_type=jnp.float32).astype(
        jnp.bfloat16
    )
    gathered = gather_blocks(pair_cols)
    split_kv = gathered.reshape(shards, heads, 2, HEAD_DIM, rows)
    keys_b = split_kv[:, :, 0]
    values_b = split_kv[:, :, 1]
    queries_b = jnp.broadcast_to(queries[None], (shards,) + queries.shape)
    scores = (
        jnp.einsum("ihqd,ihdt->ihqt", queries_b, keys_b, preferred_element_type=jnp.float32) * 0.125
    )
    row_max = jnp.max(scores, axis=(0, 3))
    weights = jnp.exp(scores - row_max[None, :, :, None])
    row_sum = jnp.sum(weights, axis=(0, 3))
    blended = jnp.sum(
        jnp.einsum(
            "ihqt,ihdt->ihqd", weights.astype(jnp.bfloat16), values_b, preferred_element_type=jnp.float32
        ),
        axis=0,
    )
    log_total = row_max + jnp.log(row_sum)
    attended = (
        (blended / row_sum[:, :, None]).transpose(1, 0, 2).reshape(rows, inner).astype(jnp.bfloat16)
    )
    student = tokens.astype(jnp.float32) + jnp.dot(
        attended, w_out, preferred_element_type=jnp.float32
    )
    token_loss, grad_y = align_terms(student, target)
    grad_b = grad_y.astype(jnp.bfloat16)
    grad_wout = jnp.dot(exchange_order(attended).T, grad_b, preferred_element_type=jnp.float32)
    grad_heads = (
        jnp.dot(grad_b, w_out.T, preferred_element_type=jnp.float32)
        .astype(jnp.bfloat16)
        .reshape(rows, heads, HEAD_DIM)
        .transpose(1, 0, 2)
    )
    row_dot = jnp.sum(
        grad_heads.astype(jnp.float32)
        * attended.reshape(rows, heads, HEAD_DIM).transpose(1, 0, 2).astype(jnp.float32),
        axis=2,
    )
    prob_full = jnp.exp(scores - log_total[None, :, :, None])
    grad_heads_b = jnp.broadcast_to(grad_heads[None], (shards,) + grad_heads.shape)
    d_value_b = jnp.einsum(
        "ihqd,ihqt->ihdt", grad_heads_b, prob_full.astype(jnp.bfloat16), preferred_element_type=jnp.float32
    )
    d_prob = jnp.einsum("ihqd,ihdt->ihqt", grad_heads_b, values_b, preferred_element_type=jnp.float32)
    d_score = (prob_full * (d_prob - row_dot[None, :, :, None])).astype(jnp.bfloat16)
    d_query_t = 0.125 * jnp.sum(
        jnp.einsum("ihqt,ihdt->ihdq", d_score, keys_b, preferred_element_type=jnp.float32), axis=0
    )
    d_key_b = 0.125 * jnp.einsum(
        "ihqd,ihqt->ihdt", queries_b, d_score, preferred_element_type=jnp.float32
    )
    half = shards // 2
    own_pairs = jnp.stack([d_key_b[:half], d_value_b[:half]], axis=2).reshape(half, 2 * inner, rows)
    other_pairs = jnp.stack([d_key_b[half:], d_value_b[half:]], axis=2).reshape(half, 2 * inner, rows)
    accum = return_blocks(own_pairs, other_pairs.astype(jnp.bfloat16))
    d_proj_t = jnp.concatenate([d_query_t.reshape(inner, rows), accum], axis=0).astype(jnp.bfloat16)
    grad_wqkv = jnp.einsum(
        "tf,ct->fc", exchange_order(hidden), d_proj_t, preferred_element_type=jnp.float32
    )
    d_hidden = jnp.einsum("ct,fc->tf", d_proj_t, w_qkv, preferred_element_type=jnp.float32)
    grad_ln = jnp.sum(d_hidden * normed, axis=0)
    loss_part = jnp.sum(token_loss)
    small = jnp.concatenate([grad_ln, loss_part.reshape(1)])
    grad_out, unused = halving_scatter(grad_wout)
    grad_qkv, small = halving_scatter(grad_wqkv, small)
    count_all = shards * lax.axis_size("clip") * TOK_DEV
    return (small[-1] / count_all, grad_qkv.reshape(-1), grad_out.reshape(-1), small[:-1])


def solution(mesh):
    placed = (P("clip", "seq", None), P("clip", "seq", None), P("clip", "seq"), P(), P(), P())
    return jax.shard_map(
        per_device,
        mesh=mesh,
        in_specs=placed,
        out_specs=(P(), P(("seq", "clip")), P(("seq", "clip")), P()),
        check_vma=False,
    )
```

```python
import jax
import jax.numpy as jnp
from jax import lax
from jax.sharding import PartitionSpec as P

HEAD_DIM = 64
TOK_DEV = 128


def shifted(value, axis, steps):
    count = lax.axis_size(axis)
    pairs = [(source, (source + steps) % count) for source in range(count)]
    return lax.ppermute(value, axis, pairs)


def layer_norm(tokens, ln_gain):
    values = tokens.astype(jnp.float32)
    center = values - jnp.mean(values, axis=-1, keepdims=True)
    spread = jnp.mean(center * center, axis=-1, keepdims=True)
    normed = center * lax.rsqrt(spread + 1e-05)
    return (normed, (normed * ln_gain).astype(jnp.bfloat16))


def align_terms(student, target):
    target_f = target.astype(jnp.float32)
    inv_y = lax.rsqrt(jnp.sum(student * student, axis=-1, keepdims=True) + 1e-06)
    inv_t = lax.rsqrt(jnp.sum(target_f * target_f, axis=-1, keepdims=True) + 1e-06)
    differ = student * inv_y - target_f * inv_t
    token_loss = jnp.sum(differ * differ, axis=-1)
    slopes = 2.0 * differ
    grad_y = inv_y * slopes - student * (inv_y * inv_y * inv_y) * jnp.sum(
        slopes * student, axis=-1, keepdims=True
    )
    return (token_loss, grad_y)


def key_mask(key_count, rows, heads):
    slot_idx = jnp.arange(rows, dtype=jnp.int32)
    halves = slot_idx[None, :] < key_count[:, None]
    return jnp.repeat(halves, heads // 2, axis=0)


def head_scores(queries, pair_rows, key_count):
    rows = pair_rows.shape[0]
    heads = queries.shape[1]
    split_kv = pair_rows.reshape(rows, heads, 2, HEAD_DIM)
    scores = (
        jnp.einsum("qhd,khd->hqk", queries, split_kv[:, :, 0], preferred_element_type=jnp.float32)
        * 0.125
    )
    mask_rows = key_mask(key_count, rows, heads)
    return (jnp.where(mask_rows[:, None, :], scores, -1e30), split_kv)


def absorb(state, queries, pair_rows, key_count):
    row_max, row_sum, blended = state
    scores, split_kv = head_scores(queries, pair_rows, key_count)
    new_max = jnp.maximum(row_max, jnp.max(scores, axis=2))
    rescale = jnp.exp(row_max - new_max)
    weights = jnp.exp(scores - new_max[:, :, None])
    row_sum = row_sum * rescale + jnp.sum(weights, axis=2)
    blended = blended * rescale[:, :, None] + jnp.einsum(
        "hqk,khd->hqd",
        weights.astype(jnp.bfloat16),
        split_kv[:, :, 1],
        preferred_element_type=jnp.float32,
    )
    return (new_max, row_sum, blended)


def contribution(queries, grad_heads, log_total, row_dot, pair_rows, key_count):
    scores, split_kv = head_scores(queries, pair_rows, key_count)
    prob_full = jnp.exp(scores - log_total[:, :, None])
    d_value = jnp.einsum(
        "hqk,qhd->khd",
        prob_full.astype(jnp.bfloat16),
        grad_heads,
        preferred_element_type=jnp.float32,
    )
    d_prob = jnp.einsum(
        "qhd,khd->hqk", grad_heads, split_kv[:, :, 1], preferred_element_type=jnp.float32
    )
    d_score = (prob_full * (d_prob - row_dot[:, :, None])).astype(jnp.bfloat16)
    d_query = 0.125 * jnp.einsum(
        "hqk,khd->qhd", d_score, split_kv[:, :, 0], preferred_element_type=jnp.float32
    )
    d_key = 0.125 * jnp.einsum("hqk,qhd->khd", d_score, queries, preferred_element_type=jnp.float32)
    rows = pair_rows.shape[0]
    return (d_query, jnp.stack([d_key, d_value], axis=2).reshape(rows, -1))


def move_keys(pair_rows):
    moved = shifted(pair_rows, "seq", 1)
    return moved


def move_grads(accum):
    moved = shifted(accum.astype(jnp.bfloat16), "seq", 1).astype(accum.dtype)
    return moved


def exchange_bits():
    seq_bits = lax.axis_size("seq").bit_length() - 1
    clip_bits = lax.axis_size("clip").bit_length() - 1
    assert (1 << seq_bits) == lax.axis_size("seq")
    assert (1 << clip_bits) == lax.axis_size("clip")
    return seq_bits, clip_bits


def exchange_order(values):
    seq_bits, clip_bits = exchange_bits()
    total = seq_bits + clip_bits
    lead = values.shape[0]
    split = values.reshape([lead] + [2] * total + [-1])
    seq_dims = [1 + seq_bits - 1 - bit for bit in range(seq_bits)]
    clip_dims = [1 + seq_bits + clip_bits - 1 - bit for bit in range(clip_bits)]
    perm = [0] + seq_dims + clip_dims + [total + 1]
    return split.transpose(perm).reshape(values.shape)


def halving_scatter(grad, small=None, split=True):
    seq_bits, clip_bits = exchange_bits()
    total = seq_bits + clip_bits
    seq_n = lax.axis_size("seq")
    clip_n = lax.axis_size("clip")
    data = grad.reshape([2] * total + [-1, grad.shape[1]])
    seq_keys = [("seq", bit) for bit in range(seq_bits)]
    clip_keys = [("clip", bit) for bit in range(clip_bits)]
    order_a = seq_keys + clip_keys
    order_b = [seq_keys[0]] + seq_keys[1:][::-1][:1] + clip_keys[:1] + seq_keys[1:][::-1][1:] + clip_keys[1:]
    if not split:
        order_b = list(order_a)
    me_seq = lax.axis_index("seq")
    me_clip = lax.axis_index("clip")
    core_bit = me_seq & 1
    left_a = list(order_a)
    left_b = list(order_a)

    def own_bit(key):
        axis, bit = key
        return ((me_seq if axis == "seq" else me_clip) >> bit) & 1

    def flip(seq_i, clip_i, key):
        axis, bit = key
        if axis == "seq":
            return (seq_i ^ (1 << bit)) * clip_n + clip_i
        return seq_i * clip_n + (clip_i ^ (1 << bit))

    for step in range(total):
        key_a, key_b = order_a[step], order_b[step]
        dim_a, dim_b = left_a.index(key_a), left_b.index(key_b)
        mine_a, mine_b = own_bit(key_a), own_bit(key_b)
        pairs = []
        for seq_i in range(seq_n):
            for clip_i in range(clip_n):
                key = key_a if (seq_i & 1) == 0 else key_b
                pairs.append((seq_i * clip_n + clip_i, flip(seq_i, clip_i, key)))
        keep = jnp.where(
            core_bit == 0,
            lax.dynamic_index_in_dim(data, mine_a, axis=dim_a, keepdims=False),
            lax.dynamic_index_in_dim(data, mine_b, axis=dim_b, keepdims=False),
        )
        give = jnp.where(
            core_bit == 0,
            lax.dynamic_index_in_dim(data, 1 - mine_a, axis=dim_a, keepdims=False),
            lax.dynamic_index_in_dim(data, 1 - mine_b, axis=dim_b, keepdims=False),
        )
        left_a.pop(dim_a)
        left_b.pop(dim_b)
        if small is None:
            got = lax.ppermute(give.astype(jnp.bfloat16), ("seq", "clip"), pairs)
        else:
            got, got_small = lax.ppermute((give.astype(jnp.bfloat16), small), ("seq", "clip"), pairs)
            small = small + got_small
        data = keep + got.astype(jnp.float32)
    return data, small


def xor_pairs(mask):
    count = lax.axis_size("seq")
    return [(src, src ^ mask) for src in range(count)]


def gather_blocks(block):
    half = lax.axis_size("seq") // 2
    same_core = [block] + [lax.ppermute(block, "seq", xor_pairs(2 * k)) for k in range(1, half)]
    group = jnp.stack(same_core)
    other = lax.ppermute(group, "seq", xor_pairs(1))
    return jnp.concatenate([group, other], axis=0)


def return_blocks(own_parts, other_parts):
    half = lax.axis_size("seq") // 2
    got = lax.ppermute(other_parts, "seq", xor_pairs(1))
    summed = own_parts + got.astype(jnp.float32)
    accum = summed[0]
    for k in range(1, half):
        sent = lax.ppermute(summed[k].astype(jnp.bfloat16), "seq", xor_pairs(2 * k))
        accum = accum + sent.astype(jnp.float32)
    return accum


def per_device(raw_tokens, teacher, keep_rows, w_qkv, w_out, ln_gain):
    shards = lax.axis_size("seq")
    my_index = lax.axis_index("seq")
    row_ids = keep_rows[0]
    list_slots = row_ids.shape[0]
    is_kept = row_ids >= 0
    kept_count = jnp.sum(is_kept.astype(jnp.int32))
    safe_ids = jnp.maximum(row_ids, 0)
    kept_tokens = jnp.where(is_kept[:, None], raw_tokens[0][safe_ids], jnp.zeros((), jnp.bfloat16))
    kept_target = jnp.where(is_kept[:, None], teacher[0][safe_ids], jnp.zeros((), jnp.bfloat16))
    count_table = lax.all_to_all(
        jnp.broadcast_to(kept_count.reshape(1, 1), (shards, 1)), "seq", 0, 0, tiled=True
    ).reshape(shards)
    shard_ids = jnp.arange(shards, dtype=jnp.int32)
    per_peer = -(-list_slots // shards)
    starts = jnp.cumsum(count_table) - count_table
    before = jnp.sum(jnp.where(shard_ids < my_index, count_table, 0))
    slot_ids = jnp.arange(per_peer, dtype=jnp.int32)
    pick = (shard_ids[:, None] - before) % shards + slot_ids[None, :] * shards
    pick_ok = pick < kept_count
    pick_safe = jnp.minimum(pick, list_slots - 1)
    send_tokens = jnp.where(
        pick_ok[:, :, None], kept_tokens[pick_safe], jnp.zeros((), jnp.bfloat16)
    )
    send_target = jnp.where(
        pick_ok[:, :, None], kept_target[pick_safe], jnp.zeros((), jnp.bfloat16)
    )
    got_both = lax.all_to_all(
        jnp.concatenate([send_tokens, send_target], axis=2), "seq", split_axis=0, concat_axis=0, tiled=True
    )
    from_pick = (my_index - starts[:, None]) % shards + slot_ids[None, :] * shards
    from_ok = from_pick < count_table[:, None]
    place = jnp.where(from_ok, (starts[:, None] + from_pick) // shards, TOK_DEV).reshape(-1)
    width = send_tokens.shape[2]
    both = (
        jnp.zeros((TOK_DEV, 2 * width), jnp.bfloat16)
        .at[place]
        .set(got_both.reshape(-1, 2 * width), mode="drop")
    )
    tokens = both[:, :width]
    target = both[:, width:]
    rows = tokens.shape[0]
    inner = w_out.shape[0]
    heads = inner // HEAD_DIM
    normed, hidden = layer_norm(tokens, ln_gain)
    queries = (
        jnp.dot(hidden, w_qkv[:, :inner], preferred_element_type=jnp.float32)
        .astype(jnp.bfloat16)
        .reshape(rows, heads, HEAD_DIM)
        .transpose(1, 0, 2)
    )
    pair_cols = jnp.dot(w_qkv[:, inner:].T, hidden.T, preferred_element_type=jnp.float32).astype(
        jnp.bfloat16
    )
    gathered = gather_blocks(pair_cols)
    split_kv = gathered.reshape(shards, heads, 2, HEAD_DIM, rows)
    keys_b = split_kv[:, :, 0]
    values_b = split_kv[:, :, 1]
    queries_b = jnp.broadcast_to(queries[None], (shards,) + queries.shape)
    scores = (
        jnp.einsum("ihqd,ihdt->ihqt", queries_b, keys_b, preferred_element_type=jnp.float32) * 0.125
    )
    row_max = jnp.max(scores, axis=(0, 3))
    weights = jnp.exp(scores - row_max[None, :, :, None])
    row_sum = jnp.sum(weights, axis=(0, 3))
    blended = jnp.sum(
        jnp.einsum(
            "ihqt,ihdt->ihqd", weights.astype(jnp.bfloat16), values_b, preferred_element_type=jnp.float32
        ),
        axis=0,
    )
    log_total = row_max + jnp.log(row_sum)
    attended = (
        (blended / row_sum[:, :, None]).transpose(1, 0, 2).reshape(rows, inner).astype(jnp.bfloat16)
    )
    student = tokens.astype(jnp.float32) + jnp.dot(
        attended, w_out, preferred_element_type=jnp.float32
    )
    token_loss, grad_y = align_terms(student, target)
    grad_b = grad_y.astype(jnp.bfloat16)
    grad_wout = jnp.dot(exchange_order(attended).T, grad_b, preferred_element_type=jnp.float32)
    grad_heads = (
        jnp.dot(grad_b, w_out.T, preferred_element_type=jnp.float32)
        .astype(jnp.bfloat16)
        .reshape(rows, heads, HEAD_DIM)
        .transpose(1, 0, 2)
    )
    row_dot = jnp.sum(
        grad_heads.astype(jnp.float32)
        * attended.reshape(rows, heads, HEAD_DIM).transpose(1, 0, 2).astype(jnp.float32),
        axis=2,
    )
    prob_full = jnp.exp(scores - log_total[None, :, :, None])
    grad_heads_b = jnp.broadcast_to(grad_heads[None], (shards,) + grad_heads.shape)
    d_value_b = jnp.einsum(
        "ihqd,ihqt->ihdt", grad_heads_b, prob_full.astype(jnp.bfloat16), preferred_element_type=jnp.float32
    )
    d_prob = jnp.einsum("ihqd,ihdt->ihqt", grad_heads_b, values_b, preferred_element_type=jnp.float32)
    d_score = (prob_full * (d_prob - row_dot[None, :, :, None])).astype(jnp.bfloat16)
    d_query_t = 0.125 * jnp.sum(
        jnp.einsum("ihqt,ihdt->ihdq", d_score, keys_b, preferred_element_type=jnp.float32), axis=0
    )
    d_key_b = 0.125 * jnp.einsum(
        "ihqd,ihqt->ihdt", queries_b, d_score, preferred_element_type=jnp.float32
    )
    half = shards // 2
    own_pairs = jnp.stack([d_key_b[:half], d_value_b[:half]], axis=2).reshape(half, 2 * inner, rows)
    other_pairs = jnp.stack([d_key_b[half:], d_value_b[half:]], axis=2).reshape(half, 2 * inner, rows)
    accum = return_blocks(own_pairs, other_pairs.astype(jnp.bfloat16))
    d_proj_t = jnp.concatenate([d_query_t.reshape(inner, rows), accum], axis=0).astype(jnp.bfloat16)
    grad_wqkv = jnp.einsum(
        "tf,ct->fc", exchange_order(hidden), d_proj_t, preferred_element_type=jnp.float32
    )
    d_hidden = jnp.einsum("ct,fc->tf", d_proj_t, w_qkv, preferred_element_type=jnp.float32)
    grad_ln = jnp.sum(d_hidden * normed, axis=0)
    loss_part = jnp.sum(token_loss)
    small = jnp.concatenate([grad_ln, loss_part.reshape(1)])
    grad_out, unused = halving_scatter(grad_wout, split=False)
    grad_qkv, small = halving_scatter(grad_wqkv, small)
    count_all = shards * lax.axis_size("clip") * TOK_DEV
    return (small[-1] / count_all, grad_qkv.reshape(-1), grad_out.reshape(-1), small[:-1])


def solution(mesh):
    placed = (P("clip", "seq", None), P("clip", "seq", None), P("clip", "seq"), P(), P(), P())
    return jax.shard_map(
        per_device,
        mesh=mesh,
        in_specs=placed,
        out_specs=(P(), P(("seq", "clip")), P(("seq", "clip")), P()),
        check_vma=False,
    )
```
